32 devices in a mesh: grp: 2 (over y), dp: 4 (over x, core), sp: 4 (over z).
Axes of the slice: x: 2, y: 2, z: 4, core: 2. Of those that a mesh axis runs over, the one named last changes fastest.
Arguments:
- rollout_rows: bfloat16 [4096, 5120], P(('grp', 'dp', 'sp')), parts along dimension 0, may hold values from -28 to 28
- routing: int32 [4096], P('grp'), parts along dimension 0, may hold values from 0 to 3, as said below
- segment_labels: int32 [8, 512], P(('grp', 'dp'), 'sp'), parts along dimension 0, may hold values from 0 to 3, never falling along the last dimension, each value on 1 to 256 neighbouring positions
- upstream: bfloat16 [8, 512, 4096], P(('grp', 'dp'), 'sp'), parts along dimension 0, may hold values from -24 to 24
- passes: int32 [32], P('grp'), parts along dimension 0, may hold values from 0 to 10
- group_ids: int32 [32], P('grp'), parts along dimension 0, may hold values from 0 to 1, as said below
Outputs:
- query_gradient: bfloat16 [8, 512, 4096], P(('grp', 'dp'), 'sp'), parts along dimension 0
- kv_grads: bfloat16 [8, 512, 1024], P(('grp', 'dp'), 'sp'), parts along dimension 0
The draws below stay inside these ranges and needn't reach their ends.
There are 2 independent parts, one for each index of `grp`. The reference program is written for one: setup_inputs(seed, part) draws one part's arguments, and reference() takes and returns one part's arrays. A program takes and returns all parts, laid end to end along the dimension named above; each array names one. Nothing has to cross between parts.
Inputs may be any that keep to these rules, and one draw needn't show every extreme that they name: `routing`: among the rows of one column j (rows i with (i // 128) % (4) == j) every owner receives exactly 128 rows; the rows of one device go to each owner in numbers 0, 32 or 64, and every device sends exactly 64 rows to one owner. `group_ids`: every group holds exactly 8 completions.
All inputs are finite; a program needn't handle non-finite values.
Results may differ from the reference program's by a relative error of at most 0.012.
Values may be sent and summed in bfloat16 or wider, within the bound.
No kernel may reach another device: no remote copies, remote signals or barrier semaphores. Data moves between devices by JAX's collectives and lax.ppermute only.
A program may use at most 128 MiB of HBM per device.

```python
import math
import jax
import jax.numpy as jnp
import numpy as np
from jax import lax

QUERY_HEADS = 32
KEY_VALUE_HEADS = 4
HEAD_SIZE = 128
TOK_DEV = 128
SEGS = 4
GROUP = 8
TESTS = 10
BIN_POSITIONS = 512
SAMPLES = 16
N_DP = 4
N_SP = 4


def draw_rollout_rows(key, part):
    row_count = N_DP * N_SP * TOK_DEV
    total_width = (QUERY_HEADS + 2 * KEY_VALUE_HEADS) * HEAD_SIZE
    key_one = jax.random.fold_in(key, 0)
    return jnp.clip(jax.random.normal(key_one, (row_count, total_width), jnp.float32), -6.0, 6.0).astype(jnp.bfloat16)


def draw_routing(key, part):
    share = TOK_DEV // N_DP

    def one_column(column_key):
        key_perm, key_shift, key_order = jax.random.split(column_key, 3)
        first_perm = jax.random.permutation(key_perm, N_DP)
        shift_by = jax.random.randint(key_shift, (), 1, N_DP)
        second_perm = first_perm[(jnp.arange(N_DP) + shift_by) % N_DP]
        owners = jnp.arange(N_DP)
        counts = share + share * (first_perm[:, None] == owners[None, :]).astype(jnp.int32) - share * (second_perm[:, None] == owners[None, :]).astype(jnp.int32)
        end_marks = jnp.cumsum(counts, axis=1)
        positions = jnp.arange(TOK_DEV)
        owner_rows = jnp.sum((positions[None, :, None] >= end_marks[:, None, :]).astype(jnp.int32), axis=2)
        row_keys = jax.random.split(key_order, N_DP)
        return jax.vmap(jax.random.permutation)(row_keys, owner_rows)
    column_draws = jax.vmap(one_column)(jax.random.split(key, N_SP))
    return jnp.transpose(column_draws, (1, 0, 2)).reshape(N_DP * N_SP * TOK_DEV).astype(jnp.int32)


def draw_group_ids(key, part):
    return (jax.random.permutation(key, N_DP * SEGS) // GROUP).astype(jnp.int32)


def with_ends(entries, rng, smallest, largest):
    longest = entries.shape.index(max(entries.shape))
    spots = []
    for shift in (0, 1):
        where = [jax.random.randint(jax.random.fold_in(rng, axis), (), 0, length) for axis, length in enumerate(entries.shape)]
        where[longest] = (where[longest] + shift) % entries.shape[longest]
        spots.append(tuple(where))
    return entries.at[spots[0]].set(smallest).at[spots[1]].set(largest)


def level_of(stream_key, shape, cuts, least, high):
    def one(position, shards_of):
        draws = jax.random.uniform(jax.random.fold_in(jax.random.fold_in(stream_key, 6), position), (shards_of,), jnp.float32, least / len(cuts), high / len(cuts))
        return jnp.repeat(jnp.exp(draws), shape[position] // shards_of).reshape((-1,) + (1,) * (len(shape) - position - 1))

    level = one(*cuts[0])
    for cut in cuts[1:]:
        level = level * one(*cut)
    return level


def length_profile(number_of, total, most, skew):
    loads = [(1 << 20) // math.isqrt(rank ** skew) + 1 for rank in range(2, number_of + 1)]
    surplus, holding = total - most - (number_of - 1), [1] * (number_of - 1)
    while surplus > 0:
        candidates = [i for i in range(number_of - 1) if holding[i] < most]
        pool, left = sum([loads[i] for i in candidates]), surplus
        for i in candidates:
            extra = min(most - holding[i], max(1, left * loads[i] // pool), surplus)
            holding[i] = holding[i] + extra
            surplus = surplus - extra
    return np.array([most] + holding)


def uneven_parts(own_key, count, total, bound, slope):
    if count == 2:
        one = jax.random.randint(own_key, (), max(1, total - bound), min(bound, total - 1) + 1)
        return jnp.stack([one, total - one])
    lengths = jnp.asarray(length_profile(count, total, bound, slope), jnp.int32)
    couples = (count - 1) // 2
    giver, receiver = lengths[1:1 + 2 * couples:2], lengths[2:2 + 2 * couples:2]
    margin = jnp.minimum(giver - 1, bound - receiver)
    shifted = jax.random.randint(jax.random.fold_in(own_key, 1), (couples,), 0, 1 << 20) % (margin + 1)
    lengths = lengths.at[1:1 + 2 * couples:2].set(giver - shifted).at[2:2 + 2 * couples:2].set(receiver + shifted)
    return lengths[jax.random.permutation(jax.random.fold_in(own_key, 2), count)]


def gaussian(key, dims, scale, most, pieces=(), kind=jnp.bfloat16):
    values = jax.random.normal(key, dims, jnp.float32) * scale
    if len(pieces) > 0:
        values = level_of(key, dims, pieces, -0.22, 0.18) * values
    return jnp.clip(values, min=-most, max=most).astype(kind)


def setup_inputs(seed: int = 0, part: int = 0) -> dict:
    streams_of = jax.random.split(jax.random.key(seed), 7)
    own_keys = jax.random.split(jax.random.fold_in(streams_of[6], part), 7)
    rollout_rows = draw_rollout_rows(jax.random.fold_in(jax.random.fold_in(streams_of[6], part), 71), part)
    routing = draw_routing(jax.random.fold_in(jax.random.fold_in(streams_of[6], part), 71), part)
    segment_labels = jax.vmap(lambda own: jnp.searchsorted(jnp.cumsum(uneven_parts(own, SEGS, BIN_POSITIONS, BIN_POSITIONS // 2, 1)), jnp.arange(BIN_POSITIONS), side="right"))(jax.random.split(own_keys[2], N_DP)).reshape((N_DP, BIN_POSITIONS)).astype(jnp.int32)
    upstream = gaussian(own_keys[3], (N_DP, BIN_POSITIONS, QUERY_HEADS * HEAD_SIZE), 4.0, 24.0, ((0, 4), (1, 4)))
    passes = with_ends(jax.random.randint(own_keys[4], (SAMPLES,), 0, TESTS + 1), jax.random.fold_in(own_keys[4], 1), 0, TESTS).astype(jnp.int32)
    group_ids = draw_group_ids(jax.random.fold_in(jax.random.fold_in(streams_of[6], part), 71), part)
    return dict(rollout_rows=rollout_rows, routing=routing, segment_labels=segment_labels, upstream=upstream, passes=passes, group_ids=group_ids)


def pack_bins(rollout_rows, routing):
    total_width = rollout_rows.shape[1]
    blocks = rollout_rows.reshape(N_DP, N_SP, TOK_DEV, total_width)
    owners = routing.reshape(N_DP, N_SP, TOK_DEV)

    def one_column(column_rows, column_owners):
        flat_rows = column_rows.reshape(N_DP * TOK_DEV, total_width)
        ordering = jnp.argsort(column_owners.reshape(N_DP * TOK_DEV), stable=True)
        return flat_rows[ordering].reshape(N_DP, TOK_DEV, total_width)
    packed_tensor = jax.vmap(one_column, in_axes=(1, 1), out_axes=1)(blocks, owners)
    return packed_tensor.reshape(N_DP, BIN_POSITIONS, total_width)

def group_advantage(passes, group_ids):
    reward = passes.astype(jnp.float32) / TESTS
    labels = jnp.arange(group_ids.shape[0] // GROUP, dtype=jnp.int32)
    member = (group_ids[:, None] == labels[None, :]).astype(jnp.float32)
    group_mean = lax.optimization_barrier(jnp.sum(member * reward[:, None], axis=0)) / lax.optimization_barrier(jnp.sum(member, axis=0))
    return reward - lax.optimization_barrier(jnp.sum(member * group_mean[None, :], axis=1))

def group_backward(inputs):
    query_rows, key_matrix, value_matrix, grads_out, segment_list = inputs
    inv_root = 1.0 / math.sqrt(HEAD_SIZE)
    places = jnp.arange(BIN_POSITIONS, dtype=jnp.int32)
    allowed = (segment_list[:, None] == segment_list[None, :]) & (places[None, :] <= places[:, None])

    def one_head(totals, head_pair):
        key_sum, value_sum = totals
        query_head, grad_head = head_pair
        scores = jnp.dot(query_head, key_matrix.T, preferred_element_type=jnp.float32) * inv_root
        scores = jnp.where(allowed, scores, -1e+30)
        row_top = lax.optimization_barrier(jnp.max(scores, axis=1, keepdims=True))
        scaled_exp = jnp.exp(scores - row_top)
        weights = scaled_exp / lax.optimization_barrier(jnp.sum(scaled_exp, axis=1, keepdims=True))
        weight_grads = jnp.dot(grad_head, value_matrix.T, preferred_element_type=jnp.float32)
        row_dot = lax.optimization_barrier(jnp.sum(weights * weight_grads, axis=1, keepdims=True))
        score_grads = (weights * (weight_grads - row_dot) * inv_root).astype(jnp.bfloat16)
        query_grad = jnp.dot(score_grads, key_matrix, preferred_element_type=jnp.float32).astype(jnp.bfloat16)
        key_sum = key_sum + jnp.dot(score_grads.T, query_head, preferred_element_type=jnp.float32)
        value_sum = value_sum + jnp.dot(weights.astype(jnp.bfloat16).T, grad_head, preferred_element_type=jnp.float32)
        return ((key_sum, value_sum), query_grad)
    initial = (jnp.zeros((BIN_POSITIONS, HEAD_SIZE), jnp.float32), jnp.zeros((BIN_POSITIONS, HEAD_SIZE), jnp.float32))
    (key_sum, value_sum), query_gradient = lax.scan(one_head, initial, (query_rows, grads_out))
    return (query_gradient, key_sum.astype(jnp.bfloat16), value_sum.astype(jnp.bfloat16))

def reference(rollout_rows, routing, segment_labels, upstream, passes, group_ids):
    packed_tensor = pack_bins(rollout_rows, routing)
    query_group = QUERY_HEADS // KEY_VALUE_HEADS
    query_rows = packed_tensor[:, :, :QUERY_HEADS * HEAD_SIZE].reshape(N_DP, BIN_POSITIONS, KEY_VALUE_HEADS, query_group, HEAD_SIZE)
    query_rows = jnp.transpose(query_rows, (0, 2, 3, 1, 4)).reshape(N_DP * KEY_VALUE_HEADS, query_group, BIN_POSITIONS, HEAD_SIZE)
    key_matrix = packed_tensor[:, :, QUERY_HEADS * HEAD_SIZE:(QUERY_HEADS + KEY_VALUE_HEADS) * HEAD_SIZE].reshape(N_DP, BIN_POSITIONS, KEY_VALUE_HEADS, HEAD_SIZE)
    key_matrix = jnp.transpose(key_matrix, (0, 2, 1, 3)).reshape(N_DP * KEY_VALUE_HEADS, BIN_POSITIONS, HEAD_SIZE)
    value_matrix = packed_tensor[:, :, (QUERY_HEADS + KEY_VALUE_HEADS) * HEAD_SIZE:].reshape(N_DP, BIN_POSITIONS, KEY_VALUE_HEADS, HEAD_SIZE)
    value_matrix = jnp.transpose(value_matrix, (0, 2, 1, 3)).reshape(N_DP * KEY_VALUE_HEADS, BIN_POSITIONS, HEAD_SIZE)
    advantage = group_advantage(passes, group_ids)
    bin_adv = advantage.reshape(N_DP, SEGS)
    member = segment_labels[:, :, None] == jnp.arange(SEGS, dtype=jnp.int32)[None, None, :]
    token_adv = lax.optimization_barrier(jnp.sum(jnp.where(member, bin_adv[:, None, :], 0.0), axis=2))
    weighted_result = (upstream.astype(jnp.float32) * token_adv[:, :, None]).astype(jnp.bfloat16)
    gradient_list = weighted_result.reshape(N_DP, BIN_POSITIONS, KEY_VALUE_HEADS, query_group, HEAD_SIZE)
    gradient_list = jnp.transpose(gradient_list, (0, 2, 3, 1, 4)).reshape(N_DP * KEY_VALUE_HEADS, query_group, BIN_POSITIONS, HEAD_SIZE)
    segment_list = jnp.repeat(segment_labels, KEY_VALUE_HEADS, axis=0)
    query_gradient, key_gradient, value_gradient = lax.map(group_backward, (query_rows, key_matrix, value_matrix, gradient_list, segment_list))
    query_gradient = query_gradient.reshape(N_DP, KEY_VALUE_HEADS, query_group, BIN_POSITIONS, HEAD_SIZE)
    query_gradient = jnp.transpose(query_gradient, (0, 3, 1, 2, 4)).reshape(N_DP, BIN_POSITIONS, QUERY_HEADS * HEAD_SIZE)
    key_gradient = jnp.transpose(key_gradient.reshape(N_DP, KEY_VALUE_HEADS, BIN_POSITIONS, HEAD_SIZE), (0, 2, 1, 3)).reshape(N_DP, BIN_POSITIONS, KEY_VALUE_HEADS * HEAD_SIZE)
    value_gradient = jnp.transpose(value_gradient.reshape(N_DP, KEY_VALUE_HEADS, BIN_POSITIONS, HEAD_SIZE), (0, 2, 1, 3)).reshape(N_DP, BIN_POSITIONS, KEY_VALUE_HEADS * HEAD_SIZE)
    kv_grads = jnp.concatenate([key_gradient, value_gradient], axis=2)
    return (query_gradient, kv_grads)
```

```python
import math

import jax
import jax.numpy as jnp
from jax import lax
from jax.sharding import PartitionSpec as P

QUERY_HEADS = 32
KEY_VALUE_HEADS = 4
HEAD_SIZE = 128
SEGS = 4
GROUP = 8
TESTS = 10


def group_advantage(passes, group_ids):
    reward = passes.astype(jnp.float32) / TESTS
    labels = jnp.arange(group_ids.shape[0] // GROUP, dtype=jnp.int32)
    member = (group_ids[:, None] == labels[None, :]).astype(jnp.float32)
    group_mean = jnp.sum(member * reward[:, None], axis=0) / jnp.sum(member, axis=0)
    return reward - jnp.sum(member * group_mean[None, :], axis=1)


def exchange_rows(rollout_rows, routing, dp_size, sp_size, dp_index, sp_index):
    token_rows = rollout_rows.shape[0]
    capacity = 2 * token_rows // dp_size
    layout_plan = routing.reshape(dp_size, sp_size, token_rows)
    column_plan = lax.dynamic_index_in_dim(layout_plan, sp_index, axis=1, keepdims=False)
    own_plan = lax.dynamic_index_in_dim(column_plan, dp_index, axis=0, keepdims=False)
    targets = jnp.arange(dp_size, dtype=jnp.int32)
    hit_table = (own_plan[:, None] == targets[None, :]).astype(jnp.int32)
    rank_rows = jnp.sum((jnp.cumsum(hit_table, axis=0) - 1) * hit_table, axis=1)
    slot_ids = own_plan * capacity + rank_rows
    slots = jnp.arange(dp_size * capacity, dtype=jnp.int32)
    send_pick = (slots[:, None] == slot_ids[None, :]).astype(rollout_rows.dtype)
    outgoing = jnp.dot(send_pick, rollout_rows, preferred_element_type=jnp.float32).astype(
        rollout_rows.dtype
    )
    arrived = lax.all_to_all(
        outgoing.reshape(dp_size, capacity, -1), "dp", split_axis=0, concat_axis=0, tiled=True
    ).reshape(dp_size * capacity, -1)
    load_table = jnp.sum((column_plan == dp_index).astype(jnp.int32), axis=1)
    end_marks = jnp.cumsum(load_table)
    start_marks = end_marks - load_table
    positions = jnp.arange(token_rows, dtype=jnp.int32)
    source = jnp.sum((positions[:, None] >= end_marks[None, :]).astype(jnp.int32), axis=1)
    chosen_start = jnp.sum(
        jnp.where(source[:, None] == targets[None, :], start_marks[None, :], 0), axis=1
    )
    pick_ids = source * capacity + positions - chosen_start
    recv_pick = (pick_ids[:, None] == slots[None, :]).astype(arrived.dtype)
    return jnp.dot(recv_pick, arrived, preferred_element_type=jnp.float32).astype(arrived.dtype)


def attend(query, grads, key_mat, value_mat, allowed):
    inv_root = 1.0 / math.sqrt(HEAD_SIZE)
    scores = (
        jnp.einsum("tghd,sgd->tghs", query, key_mat, preferred_element_type=jnp.float32) * inv_root
    )
    scores = jnp.where(allowed[:, None, None, :], scores, -1e30)
    row_top = jnp.max(scores, axis=3, keepdims=True)
    scaled_exp = jnp.exp(scores - row_top)
    weights = scaled_exp / jnp.sum(scaled_exp, axis=3, keepdims=True)
    weight_grads = jnp.einsum(
        "tghd,sgd->tghs", grads, value_mat, preferred_element_type=jnp.float32
    )
    row_dot = jnp.sum(weights * weight_grads, axis=3, keepdims=True)
    score_grads = (weights * (weight_grads - row_dot) * inv_root).astype(jnp.bfloat16)
    query_grad = jnp.einsum(
        "tghs,sgd->tghd", score_grads, key_mat, preferred_element_type=jnp.float32
    ).astype(jnp.bfloat16)
    key_part = jnp.einsum("tghs,tghd->sgd", score_grads, query, preferred_element_type=jnp.float32)
    value_part = jnp.einsum(
        "tghs,tghd->sgd", weights.astype(jnp.bfloat16), grads, preferred_element_type=jnp.float32
    )
    return query_grad, key_part, value_part


def body(rollout_rows, routing, segment_labels, upstream, passes, group_ids):
    dp_size = lax.axis_size("dp")
    sp_size = lax.axis_size("sp")
    dp_index = lax.axis_index("dp")
    sp_index = lax.axis_index("sp")
    token_rows = rollout_rows.shape[0]
    query_group = QUERY_HEADS // KEY_VALUE_HEADS
    kv_width = 2 * KEY_VALUE_HEADS * HEAD_SIZE
    seq_len = sp_size * token_rows

    packed = exchange_rows(rollout_rows, routing, dp_size, sp_size, dp_index, sp_index)
    own_seg = segment_labels[0]
    label_cols = jnp.broadcast_to(own_seg.astype(jnp.bfloat16)[:, None], (token_rows, HEAD_SIZE))
    kv_local = jnp.concatenate([packed[:, QUERY_HEADS * HEAD_SIZE :], label_cols], axis=1)
    kv_all = lax.all_gather(kv_local, "sp", axis=0, tiled=True)
    key_mat = kv_all[:, : KEY_VALUE_HEADS * HEAD_SIZE].reshape(seq_len, KEY_VALUE_HEADS, HEAD_SIZE)
    value_mat = kv_all[:, KEY_VALUE_HEADS * HEAD_SIZE : kv_width].reshape(
        seq_len, KEY_VALUE_HEADS, HEAD_SIZE
    )
    key_seg = kv_all[:, kv_width].astype(jnp.int32)

    advantage = group_advantage(passes, group_ids)
    bin_adv = lax.dynamic_slice_in_dim(advantage, dp_index * SEGS, SEGS)
    tok_adv = jnp.sum(
        jnp.where(
            own_seg[:, None] == jnp.arange(SEGS, dtype=jnp.int32)[None, :], bin_adv[None, :], 0.0
        ),
        axis=1,
    )
    weighted = (upstream[0].astype(jnp.float32) * tok_adv[:, None]).astype(jnp.bfloat16)

    query = packed[:, : QUERY_HEADS * HEAD_SIZE].reshape(
        token_rows, KEY_VALUE_HEADS, query_group, HEAD_SIZE
    )
    grads = weighted.reshape(token_rows, KEY_VALUE_HEADS, query_group, HEAD_SIZE)
    query_pos = sp_index * token_rows + jnp.arange(token_rows, dtype=jnp.int32)
    key_pos = jnp.arange(seq_len, dtype=jnp.int32)
    allowed = (own_seg[:, None] == key_seg[None, :]) & (key_pos[None, :] <= query_pos[:, None])

    chunks = max(1, min(KEY_VALUE_HEADS, seq_len // 512))
    if chunks == 1:
        query_grad, key_part, value_part = attend(query, grads, key_mat, value_mat, allowed)
    else:
        per = KEY_VALUE_HEADS // chunks

        def one_chunk(c):
            start = c * per
            return attend(
                lax.dynamic_slice_in_dim(query, start, per, axis=1),
                lax.dynamic_slice_in_dim(grads, start, per, axis=1),
                lax.dynamic_slice_in_dim(key_mat, start, per, axis=1),
                lax.dynamic_slice_in_dim(value_mat, start, per, axis=1),
                allowed,
            )

        qg, kp, vp = lax.map(one_chunk, jnp.arange(chunks, dtype=jnp.int32))
        query_grad = jnp.moveaxis(qg, 0, 1).reshape(token_rows, KEY_VALUE_HEADS, query_group, HEAD_SIZE)
        key_part = jnp.moveaxis(kp, 0, 1).reshape(seq_len, KEY_VALUE_HEADS, HEAD_SIZE)
        value_part = jnp.moveaxis(vp, 0, 1).reshape(seq_len, KEY_VALUE_HEADS, HEAD_SIZE)

    query_gradient = query_grad.reshape(1, token_rows, QUERY_HEADS * HEAD_SIZE)
    partial = jnp.concatenate(
        [
            key_part.reshape(seq_len, KEY_VALUE_HEADS * HEAD_SIZE),
            value_part.reshape(seq_len, KEY_VALUE_HEADS * HEAD_SIZE),
        ],
        axis=1,
    ).astype(jnp.bfloat16)
    kv_grads = lax.psum_scatter(partial, "sp", scatter_dimension=0, tiled=True)
    return (query_gradient, kv_grads.reshape(1, token_rows, kv_width))


def solution(mesh):
    return jax.shard_map(
        body,
        mesh=mesh,
        in_specs=(
            P(("grp", "dp", "sp"), None),
            P("grp"),
            P(("grp", "dp"), "sp"),
            P(("grp", "dp"), "sp", None),
            P("grp"),
            P("grp"),
        ),
        out_specs=(P(("grp", "dp"), "sp", None), P(("grp", "dp"), "sp", None)),
        check_vma=False,
    )
```

```python
import math

import jax
import jax.numpy as jnp
from jax import lax
from jax.sharding import PartitionSpec as P

QUERY_HEADS = 32
KEY_VALUE_HEADS = 4
HEAD_SIZE = 128
SEGS = 4
GROUP = 8
TESTS = 10


def group_advantage(passes, group_ids):
    reward = passes.astype(jnp.float32) / TESTS
    labels = jnp.arange(group_ids.shape[0] // GROUP, dtype=jnp.int32)
    member = (group_ids[:, None] == labels[None, :]).astype(jnp.float32)
    group_mean = jnp.sum(member * reward[:, None], axis=0) / jnp.sum(member, axis=0)
    return reward - jnp.sum(member * group_mean[None, :], axis=1)


def exchange_rows(rollout_rows, routing, dp_size, sp_size, dp_index, sp_index):
    token_rows = rollout_rows.shape[0]
    capacity = 2 * token_rows // dp_size
    layout_plan = routing.reshape(dp_size, sp_size, token_rows)
    column_plan = lax.dynamic_index_in_dim(layout_plan, sp_index, axis=1, keepdims=False)
    own_plan = lax.dynamic_index_in_dim(column_plan, dp_index, axis=0, keepdims=False)
    targets = jnp.arange(dp_size, dtype=jnp.int32)
    hit_table = (own_plan[:, None] == targets[None, :]).astype(jnp.int32)
    rank_rows = jnp.sum((jnp.cumsum(hit_table, axis=0) - 1) * hit_table, axis=1)
    slot_ids = own_plan * capacity + rank_rows
    slots = jnp.arange(dp_size * capacity, dtype=jnp.int32)
    send_pick = (slots[:, None] == slot_ids[None, :]).astype(rollout_rows.dtype)
    outgoing = jnp.dot(send_pick, rollout_rows, preferred_element_type=jnp.float32).astype(
        rollout_rows.dtype
    )
    arrived = lax.all_to_all(
        outgoing.reshape(dp_size, capacity, -1), "dp", split_axis=0, concat_axis=0, tiled=True
    ).reshape(dp_size * capacity, -1)
    load_table = jnp.sum((column_plan == dp_index).astype(jnp.int32), axis=1)
    end_marks = jnp.cumsum(load_table)
    start_marks = end_marks - load_table
    positions = jnp.arange(token_rows, dtype=jnp.int32)
    source = jnp.sum((positions[:, None] >= end_marks[None, :]).astype(jnp.int32), axis=1)
    chosen_start = jnp.sum(
        jnp.where(source[:, None] == targets[None, :], start_marks[None, :], 0), axis=1
    )
    pick_ids = source * capacity + positions - chosen_start
    recv_pick = (pick_ids[:, None] == slots[None, :]).astype(arrived.dtype)
    return jnp.dot(recv_pick, arrived, preferred_element_type=jnp.float32).astype(arrived.dtype)


def attend(query, grads, key_mat, value_mat, allowed):
    inv_root = 1.0 / math.sqrt(HEAD_SIZE)
    scores = (
        jnp.einsum("tghd,sgd->tghs", query, key_mat, preferred_element_type=jnp.float32) * inv_root
    )
    scores = jnp.where(allowed[:, None, None, :], scores, -1e30)
    row_top = jnp.max(scores, axis=3, keepdims=True)
    scaled_exp = jnp.exp(scores - row_top)
    weights = scaled_exp / jnp.sum(scaled_exp, axis=3, keepdims=True)
    weight_grads = jnp.einsum(
        "tghd,sgd->tghs", grads, value_mat, preferred_element_type=jnp.float32
    )
    row_dot = jnp.sum(weights * weight_grads, axis=3, keepdims=True)
    score_grads = (weights * (weight_grads - row_dot) * inv_root).astype(jnp.bfloat16)
    query_grad = jnp.einsum(
        "tghs,sgd->tghd", score_grads, key_mat, preferred_element_type=jnp.float32
    ).astype(jnp.bfloat16)
    key_part = jnp.einsum("tghs,tghd->sgd", score_grads, query, preferred_element_type=jnp.float32)
    value_part = jnp.einsum(
        "tghs,tghd->sgd", weights.astype(jnp.bfloat16), grads, preferred_element_type=jnp.float32
    )
    return query_grad, key_part, value_part


def body(rollout_rows, routing, segment_labels, upstream, passes, group_ids):
    dp_size = lax.axis_size("dp")
    sp_size = lax.axis_size("sp")
    dp_index = lax.axis_index("dp")
    sp_index = lax.axis_index("sp")
    token_rows = rollout_rows.shape[0]
    query_group = QUERY_HEADS // KEY_VALUE_HEADS
    kv_width = 2 * KEY_VALUE_HEADS * HEAD_SIZE
    seq_len = sp_size * token_rows

    packed = exchange_rows(rollout_rows, routing, dp_size, sp_size, dp_index, sp_index)
    own_seg = segment_labels[0]
    label_cols = jnp.broadcast_to(own_seg.astype(jnp.bfloat16)[:, None], (token_rows, HEAD_SIZE))
    kv_local = jnp.concatenate([packed[:, QUERY_HEADS * HEAD_SIZE :], label_cols], axis=1)
    kv_rel = [kv_local] + [
        lax.ppermute(kv_local, "sp", [(k, k + shift) for k in range(sp_size - shift)])
        for shift in range(1, sp_size)
    ]
    kv_all = jnp.concatenate(kv_rel, axis=0)
    key_mat = kv_all[:, : KEY_VALUE_HEADS * HEAD_SIZE].reshape(seq_len, KEY_VALUE_HEADS, HEAD_SIZE)
    value_mat = kv_all[:, KEY_VALUE_HEADS * HEAD_SIZE : kv_width].reshape(
        seq_len, KEY_VALUE_HEADS, HEAD_SIZE
    )
    key_seg = kv_all[:, kv_width].astype(jnp.int32)

    advantage = group_advantage(passes, group_ids)
    bin_adv = lax.dynamic_slice_in_dim(advantage, dp_index * SEGS, SEGS)
    tok_adv = jnp.sum(
        jnp.where(
            own_seg[:, None] == jnp.arange(SEGS, dtype=jnp.int32)[None, :], bin_adv[None, :], 0.0
        ),
        axis=1,
    )
    weighted = (upstream[0].astype(jnp.float32) * tok_adv[:, None]).astype(jnp.bfloat16)

    query = packed[:, : QUERY_HEADS * HEAD_SIZE].reshape(
        token_rows, KEY_VALUE_HEADS, query_group, HEAD_SIZE
    )
    grads = weighted.reshape(token_rows, KEY_VALUE_HEADS, query_group, HEAD_SIZE)
    query_pos = sp_index * token_rows + jnp.arange(token_rows, dtype=jnp.int32)
    rel_block = jnp.arange(seq_len, dtype=jnp.int32) // token_rows
    key_pos = (sp_index - rel_block) * token_rows + jnp.arange(seq_len, dtype=jnp.int32) % token_rows
    allowed = (
        (own_seg[:, None] == key_seg[None, :])
        & (key_pos[None, :] <= query_pos[:, None])
        & (key_pos[None, :] >= 0)
    )

    chunks = max(1, min(KEY_VALUE_HEADS, seq_len // 512))
    if chunks == 1:
        query_grad, key_part, value_part = attend(query, grads, key_mat, value_mat, allowed)
    else:
        per = KEY_VALUE_HEADS // chunks

        def one_chunk(c):
            start = c * per
            return attend(
                lax.dynamic_slice_in_dim(query, start, per, axis=1),
                lax.dynamic_slice_in_dim(grads, start, per, axis=1),
                lax.dynamic_slice_in_dim(key_mat, start, per, axis=1),
                lax.dynamic_slice_in_dim(value_mat, start, per, axis=1),
                allowed,
            )

        qg, kp, vp = lax.map(one_chunk, jnp.arange(chunks, dtype=jnp.int32))
        query_grad = jnp.moveaxis(qg, 0, 1).reshape(token_rows, KEY_VALUE_HEADS, query_group, HEAD_SIZE)
        key_part = jnp.moveaxis(kp, 0, 1).reshape(seq_len, KEY_VALUE_HEADS, HEAD_SIZE)
        value_part = jnp.moveaxis(vp, 0, 1).reshape(seq_len, KEY_VALUE_HEADS, HEAD_SIZE)

    query_gradient = query_grad.reshape(1, token_rows, QUERY_HEADS * HEAD_SIZE)
    partial = jnp.concatenate(
        [
            key_part.reshape(sp_size, token_rows, KEY_VALUE_HEADS * HEAD_SIZE),
            value_part.reshape(sp_size, token_rows, KEY_VALUE_HEADS * HEAD_SIZE),
        ],
        axis=2,
    )
    kv_total = partial[0]
    for shift in range(1, sp_size):
        kv_total = kv_total + lax.ppermute(
            partial[shift].astype(jnp.bfloat16),
            "sp",
            [(k, k - shift) for k in range(shift, sp_size)],
        ).astype(jnp.float32)
    kv_grads = kv_total.astype(jnp.bfloat16)
    return (query_gradient, kv_grads.reshape(1, token_rows, kv_width))


def solution(mesh):
    return jax.shard_map(
        body,
        mesh=mesh,
        in_specs=(
            P(("grp", "dp", "sp"), None),
            P("grp"),
            P(("grp", "dp"), "sp"),
            P(("grp", "dp"), "sp", None),
            P("grp"),
            P("grp"),
        ),
        out_specs=(P(("grp", "dp"), "sp", None), P(("grp", "dp"), "sp", None)),
        check_vma=False,
    )
```

```python
import math

import jax
import jax.numpy as jnp
from jax import lax
from jax.sharding import PartitionSpec as P

QUERY_HEADS = 32
KEY_VALUE_HEADS = 4
HEAD_SIZE = 128
SEGS = 4
GROUP = 8
TESTS = 10


def group_advantage(passes, group_ids):
    reward = passes.astype(jnp.float32) / TESTS
    labels = jnp.arange(group_ids.shape[0] // GROUP, dtype=jnp.int32)
    member = (group_ids[:, None] == labels[None, :]).astype(jnp.float32)
    group_mean = jnp.sum(member * reward[:, None], axis=0) / jnp.sum(member, axis=0)
    return reward - jnp.sum(member * group_mean[None, :], axis=1)


def exchange_rows(rollout_rows, routing, dp_size, sp_size, dp_index, sp_index):
    token_rows = rollout_rows.shape[0]
    capacity = 2 * token_rows // dp_size
    layout_plan = routing.reshape(dp_size, sp_size, token_rows)
    column_plan = lax.dynamic_index_in_dim(layout_plan, sp_index, axis=1, keepdims=False)
    own_plan = lax.dynamic_index_in_dim(column_plan, dp_index, axis=0, keepdims=False)
    targets = jnp.arange(dp_size, dtype=jnp.int32)
    hit_table = (own_plan[:, None] == targets[None, :]).astype(jnp.int32)
    rank_rows = jnp.sum((jnp.cumsum(hit_table, axis=0) - 1) * hit_table, axis=1)
    slot_ids = own_plan * capacity + rank_rows
    slots = jnp.arange(dp_size * capacity, dtype=jnp.int32)
    send_pick = (slots[:, None] == slot_ids[None, :]).astype(rollout_rows.dtype)
    outgoing = jnp.dot(send_pick, rollout_rows, preferred_element_type=jnp.float32).astype(
        rollout_rows.dtype
    )
    arrived = lax.all_to_all(
        outgoing.reshape(dp_size, capacity, -1), "dp", split_axis=0, concat_axis=0, tiled=True
    ).reshape(dp_size * capacity, -1)
    load_table = jnp.sum((column_plan == dp_index).astype(jnp.int32), axis=1)
    end_marks = jnp.cumsum(load_table)
    start_marks = end_marks - load_table
    positions = jnp.arange(token_rows, dtype=jnp.int32)
    source = jnp.sum((positions[:, None] >= end_marks[None, :]).astype(jnp.int32), axis=1)
    chosen_start = jnp.sum(
        jnp.where(source[:, None] == targets[None, :], start_marks[None, :], 0), axis=1
    )
    pick_ids = source * capacity + positions - chosen_start
    recv_pick = (pick_ids[:, None] == slots[None, :]).astype(arrived.dtype)
    return jnp.dot(recv_pick, arrived, preferred_element_type=jnp.float32).astype(arrived.dtype)


def attend(query, grads, key_mat, value_mat, allowed):
    inv_root = 1.0 / math.sqrt(HEAD_SIZE)
    scores = (
        jnp.einsum("tghd,sgd->tghs", query, key_mat, preferred_element_type=jnp.float32) * inv_root
    )
    scores = jnp.where(allowed[:, None, None, :], scores, -1e30)
    row_top = jnp.max(scores, axis=3, keepdims=True)
    scaled_exp = jnp.exp(scores - row_top)
    weights = scaled_exp / jnp.sum(scaled_exp, axis=3, keepdims=True)
    weight_grads = jnp.einsum(
        "tghd,sgd->tghs", grads, value_mat, preferred_element_type=jnp.float32
    )
    row_dot = jnp.sum(weights * weight_grads, axis=3, keepdims=True)
    score_grads = (weights * (weight_grads - row_dot) * inv_root).astype(jnp.bfloat16)
    query_grad = jnp.einsum(
        "tghs,sgd->tghd", score_grads, key_mat, preferred_element_type=jnp.float32
    ).astype(jnp.bfloat16)
    key_part = jnp.einsum("tghs,tghd->sgd", score_grads, query, preferred_element_type=jnp.float32)
    value_part = jnp.einsum(
        "tghs,tghd->sgd", weights.astype(jnp.bfloat16), grads, preferred_element_type=jnp.float32
    )
    return query_grad, key_part, value_part


def body(rollout_rows, routing, segment_labels, upstream, passes, group_ids):
    dp_size = lax.axis_size("dp")
    sp_size = lax.axis_size("sp")
    dp_index = lax.axis_index("dp")
    sp_index = lax.axis_index("sp")
    token_rows = rollout_rows.shape[0]
    query_group = QUERY_HEADS // KEY_VALUE_HEADS
    kv_width = 2 * KEY_VALUE_HEADS * HEAD_SIZE
    longest_segment = sp_size * token_rows // 2
    reach = min(sp_size - 1, (longest_segment + token_rows - 2) // token_rows)
    seq_len = (reach + 1) * token_rows

    packed = exchange_rows(rollout_rows, routing, dp_size, sp_size, dp_index, sp_index)
    own_seg = segment_labels[0]
    label_cols = jnp.broadcast_to(own_seg.astype(jnp.bfloat16)[:, None], (token_rows, HEAD_SIZE))
    kv_local = jnp.concatenate([packed[:, QUERY_HEADS * HEAD_SIZE :], label_cols], axis=1)
    kv_rel = [kv_local] + [
        lax.ppermute(kv_local, "sp", [(k, k + shift) for k in range(sp_size - shift)])
        for shift in range(1, reach + 1)
    ]
    kv_all = jnp.concatenate(kv_rel, axis=0)
    key_mat = kv_all[:, : KEY_VALUE_HEADS * HEAD_SIZE].reshape(seq_len, KEY_VALUE_HEADS, HEAD_SIZE)
    value_mat = kv_all[:, KEY_VALUE_HEADS * HEAD_SIZE : kv_width].reshape(
        seq_len, KEY_VALUE_HEADS, HEAD_SIZE
    )
    key_seg = kv_all[:, kv_width].astype(jnp.int32)

    advantage = group_advantage(passes, group_ids)
    bin_adv = lax.dynamic_slice_in_dim(advantage, dp_index * SEGS, SEGS)
    tok_adv = jnp.sum(
        jnp.where(
            own_seg[:, None] == jnp.arange(SEGS, dtype=jnp.int32)[None, :], bin_adv[None, :], 0.0
        ),
        axis=1,
    )
    weighted = (upstream[0].astype(jnp.float32) * tok_adv[:, None]).astype(jnp.bfloat16)

    query = packed[:, : QUERY_HEADS * HEAD_SIZE].reshape(
        token_rows, KEY_VALUE_HEADS, query_group, HEAD_SIZE
    )
    grads = weighted.reshape(token_rows, KEY_VALUE_HEADS, query_group, HEAD_SIZE)
    query_pos = sp_index * token_rows + jnp.arange(token_rows, dtype=jnp.int32)
    rel_block = jnp.arange(seq_len, dtype=jnp.int32) // token_rows
    key_pos = (sp_index - rel_block) * token_rows + jnp.arange(seq_len, dtype=jnp.int32) % token_rows
    allowed = (
        (own_seg[:, None] == key_seg[None, :])
        & (key_pos[None, :] <= query_pos[:, None])
        & (key_pos[None, :] >= 0)
    )

    chunks = max(1, min(KEY_VALUE_HEADS, seq_len // 512))
    if chunks == 1:
        query_grad, key_part, value_part = attend(query, grads, key_mat, value_mat, allowed)
    else:
        per = KEY_VALUE_HEADS // chunks

        def one_chunk(c):
            start = c * per
            return attend(
                lax.dynamic_slice_in_dim(query, start, per, axis=1),
                lax.dynamic_slice_in_dim(grads, start, per, axis=1),
                lax.dynamic_slice_in_dim(key_mat, start, per, axis=1),
                lax.dynamic_slice_in_dim(value_mat, start, per, axis=1),
                allowed,
            )

        qg, kp, vp = lax.map(one_chunk, jnp.arange(chunks, dtype=jnp.int32))
        query_grad = jnp.moveaxis(qg, 0, 1).reshape(token_rows, KEY_VALUE_HEADS, query_group, HEAD_SIZE)
        key_part = jnp.moveaxis(kp, 0, 1).reshape(seq_len, KEY_VALUE_HEADS, HEAD_SIZE)
        value_part = jnp.moveaxis(vp, 0, 1).reshape(seq_len, KEY_VALUE_HEADS, HEAD_SIZE)

    query_gradient = query_grad.reshape(1, token_rows, QUERY_HEADS * HEAD_SIZE)
    partial = jnp.concatenate(
        [
            key_part.reshape(reach + 1, token_rows, KEY_VALUE_HEADS * HEAD_SIZE),
            value_part.reshape(reach + 1, token_rows, KEY_VALUE_HEADS * HEAD_SIZE),
        ],
        axis=2,
    )
    kv_total = partial[0]
    for shift in range(1, reach + 1):
        kv_total = kv_total + lax.ppermute(
            partial[shift].astype(jnp.bfloat16),
            "sp",
            [(k, k - shift) for k in range(shift, sp_size)],
        ).astype(jnp.float32)
    kv_grads = kv_total.astype(jnp.bfloat16)
    return (query_gradient, kv_grads.reshape(1, token_rows, kv_width))


def solution(mesh):
    return jax.shard_map(
        body,
        mesh=mesh,
        in_specs=(
            P(("grp", "dp", "sp"), None),
            P("grp"),
            P(("grp", "dp"), "sp"),
            P(("grp", "dp"), "sp", None),
            P("grp"),
            P("grp"),
        ),
        out_specs=(P(("grp", "dp"), "sp", None), P(("grp", "dp"), "sp", None)),
        check_vma=False,
    )
```

```python
import math

import jax
import jax.numpy as jnp
from jax import lax
from jax.experimental import pallas as pl
from jax.sharding import PartitionSpec as P

QUERY_HEADS = 32
KEY_VALUE_HEADS = 4
HEAD_SIZE = 128
SEGS = 4
GROUP = 8
TESTS = 10


def group_advantage(passes, group_ids):
    reward = passes.astype(jnp.float32) / TESTS
    labels = jnp.arange(group_ids.shape[0] // GROUP, dtype=jnp.int32)
    member = (group_ids[:, None] == labels[None, :]).astype(jnp.float32)
    group_mean = jnp.sum(member * reward[:, None], axis=0) / jnp.sum(member, axis=0)
    return reward - jnp.sum(member * group_mean[None, :], axis=1)


def exchange_rows(rollout_rows, routing, dp_size, sp_size, dp_index, sp_index):
    token_rows = rollout_rows.shape[0]
    capacity = 2 * token_rows // dp_size
    layout_plan = routing.reshape(dp_size, sp_size, token_rows)
    column_plan = lax.dynamic_index_in_dim(layout_plan, sp_index, axis=1, keepdims=False)
    own_plan = lax.dynamic_index_in_dim(column_plan, dp_index, axis=0, keepdims=False)
    targets = jnp.arange(dp_size, dtype=jnp.int32)
    hit_table = (own_plan[:, None] == targets[None, :]).astype(jnp.int32)
    rank_rows = jnp.sum((jnp.cumsum(hit_table, axis=0) - 1) * hit_table, axis=1)
    slot_ids = own_plan * capacity + rank_rows
    slots = jnp.arange(dp_size * capacity, dtype=jnp.int32)
    send_pick = (slots[:, None] == slot_ids[None, :]).astype(rollout_rows.dtype)
    outgoing = jnp.dot(send_pick, rollout_rows, preferred_element_type=jnp.float32).astype(
        rollout_rows.dtype
    )
    arrived = lax.all_to_all(
        outgoing.reshape(dp_size, capacity, -1), "dp", split_axis=0, concat_axis=0, tiled=True
    ).reshape(dp_size * capacity, -1)
    load_table = jnp.sum((column_plan == dp_index).astype(jnp.int32), axis=1)
    end_marks = jnp.cumsum(load_table)
    start_marks = end_marks - load_table
    positions = jnp.arange(token_rows, dtype=jnp.int32)
    source = jnp.sum((positions[:, None] >= end_marks[None, :]).astype(jnp.int32), axis=1)
    chosen_start = jnp.sum(
        jnp.where(source[:, None] == targets[None, :], start_marks[None, :], 0), axis=1
    )
    pick_ids = source * capacity + positions - chosen_start
    recv_pick = (pick_ids[:, None] == slots[None, :]).astype(arrived.dtype)
    return jnp.dot(recv_pick, arrived, preferred_element_type=jnp.float32).astype(arrived.dtype)


def attend(query, grads, key_mat, value_mat, allowed):
    inv_root = 1.0 / math.sqrt(HEAD_SIZE)
    scores = (
        jnp.einsum("tghd,sgd->tghs", query, key_mat, preferred_element_type=jnp.float32) * inv_root
    )
    scores = jnp.where(allowed[:, None, None, :], scores, -1e30)
    row_top = jnp.max(scores, axis=3, keepdims=True)
    scaled_exp = jnp.exp(scores - row_top)
    weights = scaled_exp / jnp.sum(scaled_exp, axis=3, keepdims=True)
    weight_grads = jnp.einsum(
        "tghd,sgd->tghs", grads, value_mat, preferred_element_type=jnp.float32
    )
    row_dot = jnp.sum(weights * weight_grads, axis=3, keepdims=True)
    score_grads = (weights * (weight_grads - row_dot) * inv_root).astype(jnp.bfloat16)
    query_grad = jnp.einsum(
        "tghs,sgd->tghd", score_grads, key_mat, preferred_element_type=jnp.float32
    ).astype(jnp.bfloat16)
    key_part = jnp.einsum("tghs,tghd->sgd", score_grads, query, preferred_element_type=jnp.float32)
    value_part = jnp.einsum(
        "tghs,tghd->sgd", weights.astype(jnp.bfloat16), grads, preferred_element_type=jnp.float32
    )
    return query_grad, key_part, value_part


def attend_kernel(q_ref, g_ref, k_ref, v_ref, m_ref, dq_ref, kp_ref, vp_ref):
    inv_root = 1.0 / math.sqrt(HEAD_SIZE)
    key_mat = k_ref[...]
    value_mat = v_ref[...]
    allowed = m_ref[...] > 0.5
    key_sum = jnp.zeros(kp_ref.shape, jnp.float32)
    value_sum = jnp.zeros(vp_ref.shape, jnp.float32)
    for head in range(q_ref.shape[1] // HEAD_SIZE):
        cols = slice(head * HEAD_SIZE, (head + 1) * HEAD_SIZE)
        query_head = q_ref[:, cols]
        grad_head = g_ref[:, cols]
        scores = (
            lax.dot_general(
                query_head, key_mat, (((1,), (1,)), ((), ())), preferred_element_type=jnp.float32
            )
            * inv_root
        )
        scores = jnp.where(allowed, scores, -1e30)
        row_top = jnp.max(scores, axis=1, keepdims=True)
        scaled_exp = jnp.exp(scores - row_top)
        weights = scaled_exp / jnp.sum(scaled_exp, axis=1, keepdims=True)
        weight_grads = lax.dot_general(
            grad_head, value_mat, (((1,), (1,)), ((), ())), preferred_element_type=jnp.float32
        )
        row_dot = jnp.sum(weights * weight_grads, axis=1, keepdims=True)
        score_grads = (weights * (weight_grads - row_dot) * inv_root).astype(jnp.bfloat16)
        dq_ref[:, cols] = jnp.dot(
            score_grads, key_mat, preferred_element_type=jnp.float32
        ).astype(dq_ref.dtype)
        key_sum = key_sum + lax.dot_general(
            score_grads, query_head, (((0,), (0,)), ((), ())), preferred_element_type=jnp.float32
        )
        value_sum = value_sum + lax.dot_general(
            weights.astype(jnp.bfloat16),
            grad_head,
            (((0,), (0,)), ((), ())),
            preferred_element_type=jnp.float32,
        )
    kp_ref[...] = key_sum
    vp_ref[...] = value_sum


def attend_pallas(packed, weighted, kv_all, mask):
    token_rows = packed.shape[0]
    key_rows = kv_all.shape[0]
    group_width = QUERY_HEADS // KEY_VALUE_HEADS * HEAD_SIZE
    flops = 10 * token_rows * key_rows * HEAD_SIZE * QUERY_HEADS
    bytes_accessed = 2 * (3 * token_rows * QUERY_HEADS * HEAD_SIZE) + 2 * key_rows * 1024 * 3 + 4 * token_rows * key_rows
    return pl.pallas_call(
        attend_kernel,
        grid=(KEY_VALUE_HEADS,),
        in_specs=[
            pl.BlockSpec((token_rows, group_width), lambda g: (0, g)),
            pl.BlockSpec((token_rows, group_width), lambda g: (0, g)),
            pl.BlockSpec((key_rows, HEAD_SIZE), lambda g: (0, g)),
            pl.BlockSpec((key_rows, HEAD_SIZE), lambda g: (0, KEY_VALUE_HEADS + g)),
            pl.BlockSpec((token_rows, key_rows), lambda g: (0, 0)),
        ],
        out_specs=[
            pl.BlockSpec((token_rows, group_width), lambda g: (0, g)),
            pl.BlockSpec((key_rows, HEAD_SIZE), lambda g: (0, g)),
            pl.BlockSpec((key_rows, HEAD_SIZE), lambda g: (0, g)),
        ],
        out_shape=[
            jax.ShapeDtypeStruct((token_rows, QUERY_HEADS * HEAD_SIZE), jnp.bfloat16),
            jax.ShapeDtypeStruct((key_rows, KEY_VALUE_HEADS * HEAD_SIZE), jnp.float32),
            jax.ShapeDtypeStruct((key_rows, KEY_VALUE_HEADS * HEAD_SIZE), jnp.float32),
        ],
        cost_estimate=pl.CostEstimate(
            flops=flops, transcendentals=token_rows * key_rows * QUERY_HEADS, bytes_accessed=bytes_accessed
        ),
    )(packed, weighted, kv_all, kv_all, mask)


def body(rollout_rows, routing, segment_labels, upstream, passes, group_ids):
    dp_size = lax.axis_size("dp")
    sp_size = lax.axis_size("sp")
    dp_index = lax.axis_index("dp")
    sp_index = lax.axis_index("sp")
    token_rows = rollout_rows.shape[0]
    query_group = QUERY_HEADS // KEY_VALUE_HEADS
    kv_width = 2 * KEY_VALUE_HEADS * HEAD_SIZE
    longest_segment = sp_size * token_rows // 2
    reach = min(sp_size - 1, (longest_segment + token_rows - 2) // token_rows)
    seq_len = (reach + 1) * token_rows

    packed = exchange_rows(rollout_rows, routing, dp_size, sp_size, dp_index, sp_index)
    own_seg = segment_labels[0]
    label_cols = jnp.broadcast_to(own_seg.astype(jnp.bfloat16)[:, None], (token_rows, HEAD_SIZE))
    kv_local = jnp.concatenate([packed[:, QUERY_HEADS * HEAD_SIZE :], label_cols], axis=1)
    kv_rel = [kv_local] + [
        lax.ppermute(kv_local, "sp", [(k, k + shift) for k in range(sp_size - shift)])
        for shift in range(1, reach + 1)
    ]
    kv_all = jnp.concatenate(kv_rel, axis=0)
    key_seg = kv_all[:, kv_width].astype(jnp.int32)

    advantage = group_advantage(passes, group_ids)
    bin_adv = lax.dynamic_slice_in_dim(advantage, dp_index * SEGS, SEGS)
    tok_adv = jnp.sum(
        jnp.where(
            own_seg[:, None] == jnp.arange(SEGS, dtype=jnp.int32)[None, :], bin_adv[None, :], 0.0
        ),
        axis=1,
    )
    weighted = (upstream[0].astype(jnp.float32) * tok_adv[:, None]).astype(jnp.bfloat16)

    query_pos = sp_index * token_rows + jnp.arange(token_rows, dtype=jnp.int32)
    rel_block = jnp.arange(seq_len, dtype=jnp.int32) // token_rows
    key_pos = (sp_index - rel_block) * token_rows + jnp.arange(seq_len, dtype=jnp.int32) % token_rows
    allowed = (
        (own_seg[:, None] == key_seg[None, :])
        & (key_pos[None, :] <= query_pos[:, None])
        & (key_pos[None, :] >= 0)
    )
    query_grad, key_part, value_part = attend_pallas(
        packed, weighted, kv_all, allowed.astype(jnp.float32)
    )
    query_gradient = query_grad.reshape(1, token_rows, QUERY_HEADS * HEAD_SIZE)
    partial = jnp.concatenate(
        [
            key_part.reshape(reach + 1, token_rows, KEY_VALUE_HEADS * HEAD_SIZE),
            value_part.reshape(reach + 1, token_rows, KEY_VALUE_HEADS * HEAD_SIZE),
        ],
        axis=2,
    )
    kv_total = partial[0]
    for shift in range(1, reach + 1):
        kv_total = kv_total + lax.ppermute(
            partial[shift].astype(jnp.bfloat16),
            "sp",
            [(k, k - shift) for k in range(shift, sp_size)],
        ).astype(jnp.float32)
    kv_grads = kv_total.astype(jnp.bfloat16)
    return (query_gradient, kv_grads.reshape(1, token_rows, kv_width))


def solution(mesh):
    return jax.shard_map(
        body,
        mesh=mesh,
        in_specs=(
            P(("grp", "dp", "sp"), None),
            P("grp"),
            P(("grp", "dp"), "sp"),
            P(("grp", "dp"), "sp", None),
            P("grp"),
            P("grp"),
        ),
        out_specs=(P(("grp", "dp"), "sp", None), P(("grp", "dp"), "sp", None)),
        check_vma=False,
    )
```

```python
import math

import jax
import jax.numpy as jnp
from jax import lax
from jax.experimental import pallas as pl
from jax.sharding import PartitionSpec as P

QUERY_HEADS = 32
KEY_VALUE_HEADS = 4
HEAD_SIZE = 128
SEGS = 4
GROUP = 8
TESTS = 10


def group_advantage(passes, group_ids):
    reward = passes.astype(jnp.float32) / TESTS
    labels = jnp.arange(group_ids.shape[0] // GROUP, dtype=jnp.int32)
    member = (group_ids[:, None] == labels[None, :]).astype(jnp.float32)
    group_mean = jnp.sum(member * reward[:, None], axis=0) / jnp.sum(member, axis=0)
    return reward - jnp.sum(member * group_mean[None, :], axis=1)


def exchange_rows(rollout_rows, routing, dp_size, sp_size, dp_index, sp_index):
    token_rows = rollout_rows.shape[0]
    capacity = 2 * token_rows // dp_size
    layout_plan = routing.reshape(dp_size, sp_size, token_rows)
    column_plan = lax.dynamic_index_in_dim(layout_plan, sp_index, axis=1, keepdims=False)
    own_plan = lax.dynamic_index_in_dim(column_plan, dp_index, axis=0, keepdims=False)
    targets = jnp.arange(dp_size, dtype=jnp.int32)
    hit_table = (own_plan[:, None] == targets[None, :]).astype(jnp.int32)
    rank_rows = jnp.sum((jnp.cumsum(hit_table, axis=0) - 1) * hit_table, axis=1)
    slot_ids = own_plan * capacity + rank_rows
    slots = jnp.arange(dp_size * capacity, dtype=jnp.int32)
    send_pick = (slots[:, None] == slot_ids[None, :]).astype(rollout_rows.dtype)

    def send(columns):
        outgoing = jnp.dot(send_pick, columns, preferred_element_type=jnp.float32).astype(
            columns.dtype
        )
        return lax.all_to_all(
            outgoing.reshape(dp_size, capacity, -1), "dp", split_axis=0, concat_axis=0, tiled=True
        ).reshape(dp_size * capacity, -1)

    arrived_kv = send(rollout_rows[:, QUERY_HEADS * HEAD_SIZE :])
    arrived_q = send(rollout_rows[:, : QUERY_HEADS * HEAD_SIZE])
    load_table = jnp.sum((column_plan == dp_index).astype(jnp.int32), axis=1)
    end_marks = jnp.cumsum(load_table)
    start_marks = end_marks - load_table
    positions = jnp.arange(token_rows, dtype=jnp.int32)
    source = jnp.sum((positions[:, None] >= end_marks[None, :]).astype(jnp.int32), axis=1)
    chosen_start = jnp.sum(
        jnp.where(source[:, None] == targets[None, :], start_marks[None, :], 0), axis=1
    )
    pick_ids = source * capacity + positions - chosen_start
    recv_pick = (pick_ids[:, None] == slots[None, :]).astype(arrived_kv.dtype)

    def receive(arrived):
        return jnp.dot(recv_pick, arrived, preferred_element_type=jnp.float32).astype(arrived.dtype)

    return receive(arrived_q), receive(arrived_kv)


def attend(query, grads, key_mat, value_mat, allowed):
    inv_root = 1.0 / math.sqrt(HEAD_SIZE)
    scores = (
        jnp.einsum("tghd,sgd->tghs", query, key_mat, preferred_element_type=jnp.float32) * inv_root
    )
    scores = jnp.where(allowed[:, None, None, :], scores, -1e30)
    row_top = jnp.max(scores, axis=3, keepdims=True)
    scaled_exp = jnp.exp(scores - row_top)
    weights = scaled_exp / jnp.sum(scaled_exp, axis=3, keepdims=True)
    weight_grads = jnp.einsum(
        "tghd,sgd->tghs", grads, value_mat, preferred_element_type=jnp.float32
    )
    row_dot = jnp.sum(weights * weight_grads, axis=3, keepdims=True)
    score_grads = (weights * (weight_grads - row_dot) * inv_root).astype(jnp.bfloat16)
    query_grad = jnp.einsum(
        "tghs,sgd->tghd", score_grads, key_mat, preferred_element_type=jnp.float32
    ).astype(jnp.bfloat16)
    key_part = jnp.einsum("tghs,tghd->sgd", score_grads, query, preferred_element_type=jnp.float32)
    value_part = jnp.einsum(
        "tghs,tghd->sgd", weights.astype(jnp.bfloat16), grads, preferred_element_type=jnp.float32
    )
    return query_grad, key_part, value_part


def attend_kernel(q_ref, g_ref, k_ref, v_ref, m_ref, dq_ref, kp_ref, vp_ref):
    inv_root = 1.0 / math.sqrt(HEAD_SIZE)
    key_mat = k_ref[...]
    value_mat = v_ref[...]
    allowed = m_ref[...] > 0.5
    key_sum = jnp.zeros(kp_ref.shape, jnp.float32)
    value_sum = jnp.zeros(vp_ref.shape, jnp.float32)
    for head in range(q_ref.shape[1] // HEAD_SIZE):
        cols = slice(head * HEAD_SIZE, (head + 1) * HEAD_SIZE)
        query_head = q_ref[:, cols]
        grad_head = g_ref[:, cols]
        scores = (
            lax.dot_general(
                query_head, key_mat, (((1,), (1,)), ((), ())), preferred_element_type=jnp.float32
            )
            * inv_root
        )
        scores = jnp.where(allowed, scores, -1e30)
        row_top = jnp.max(scores, axis=1, keepdims=True)
        scaled_exp = jnp.exp(scores - row_top)
        weights = scaled_exp / jnp.sum(scaled_exp, axis=1, keepdims=True)
        weight_grads = lax.dot_general(
            grad_head, value_mat, (((1,), (1,)), ((), ())), preferred_element_type=jnp.float32
        )
        row_dot = jnp.sum(weights * weight_grads, axis=1, keepdims=True)
        score_grads = (weights * (weight_grads - row_dot) * inv_root).astype(jnp.bfloat16)
        dq_ref[:, cols] = jnp.dot(
            score_grads, key_mat, preferred_element_type=jnp.float32
        ).astype(dq_ref.dtype)
        key_sum = key_sum + lax.dot_general(
            score_grads, query_head, (((0,), (0,)), ((), ())), preferred_element_type=jnp.float32
        )
        value_sum = value_sum + lax.dot_general(
            weights.astype(jnp.bfloat16),
            grad_head,
            (((0,), (0,)), ((), ())),
            preferred_element_type=jnp.float32,
        )
    kp_ref[...] = key_sum
    vp_ref[...] = value_sum


def attend_pallas(packed, weighted, kv_all, mask):
    token_rows = packed.shape[0]
    key_rows = kv_all.shape[0]
    group_width = QUERY_HEADS // KEY_VALUE_HEADS * HEAD_SIZE
    flops = 10 * token_rows * key_rows * HEAD_SIZE * QUERY_HEADS
    bytes_accessed = 2 * (3 * token_rows * QUERY_HEADS * HEAD_SIZE) + 2 * key_rows * 1024 * 3 + 4 * token_rows * key_rows
    return pl.pallas_call(
        attend_kernel,
        grid=(KEY_VALUE_HEADS,),
        in_specs=[
            pl.BlockSpec((token_rows, group_width), lambda g: (0, g)),
            pl.BlockSpec((token_rows, group_width), lambda g: (0, g)),
            pl.BlockSpec((key_rows, HEAD_SIZE), lambda g: (0, g)),
            pl.BlockSpec((key_rows, HEAD_SIZE), lambda g: (0, KEY_VALUE_HEADS + g)),
            pl.BlockSpec((token_rows, key_rows), lambda g: (0, 0)),
        ],
        out_specs=[
            pl.BlockSpec((token_rows, group_width), lambda g: (0, g)),
            pl.BlockSpec((key_rows, HEAD_SIZE), lambda g: (0, g)),
            pl.BlockSpec((key_rows, HEAD_SIZE), lambda g: (0, g)),
        ],
        out_shape=[
            jax.ShapeDtypeStruct((token_rows, QUERY_HEADS * HEAD_SIZE), jnp.bfloat16),
            jax.ShapeDtypeStruct((key_rows, KEY_VALUE_HEADS * HEAD_SIZE), jnp.float32),
            jax.ShapeDtypeStruct((key_rows, KEY_VALUE_HEADS * HEAD_SIZE), jnp.float32),
        ],
        cost_estimate=pl.CostEstimate(
            flops=flops, transcendentals=token_rows * key_rows * QUERY_HEADS, bytes_accessed=bytes_accessed
        ),
    )(packed, weighted, kv_all, kv_all, mask)


def body(rollout_rows, routing, segment_labels, upstream, passes, group_ids):
    dp_size = lax.axis_size("dp")
    sp_size = lax.axis_size("sp")
    dp_index = lax.axis_index("dp")
    sp_index = lax.axis_index("sp")
    token_rows = rollout_rows.shape[0]
    query_group = QUERY_HEADS // KEY_VALUE_HEADS
    kv_width = 2 * KEY_VALUE_HEADS * HEAD_SIZE
    longest_segment = sp_size * token_rows // 2
    reach = min(sp_size - 1, (longest_segment + token_rows - 2) // token_rows)
    seq_len = (reach + 1) * token_rows

    packed_q, packed_kv = exchange_rows(rollout_rows, routing, dp_size, sp_size, dp_index, sp_index)
    own_seg = segment_labels[0]
    label_cols = jnp.broadcast_to(own_seg.astype(jnp.bfloat16)[:, None], (token_rows, HEAD_SIZE))
    kv_local = jnp.concatenate([packed_kv, label_cols], axis=1)
    kv_rel = [kv_local] + [
        lax.ppermute(kv_local, "sp", [(k, k + shift) for k in range(sp_size - shift)])
        for shift in range(1, reach + 1)
    ]
    kv_all = jnp.concatenate(kv_rel, axis=0)
    key_seg = kv_all[:, kv_width].astype(jnp.int32)

    advantage = group_advantage(passes, group_ids)
    bin_adv = lax.dynamic_slice_in_dim(advantage, dp_index * SEGS, SEGS)
    tok_adv = jnp.sum(
        jnp.where(
            own_seg[:, None] == jnp.arange(SEGS, dtype=jnp.int32)[None, :], bin_adv[None, :], 0.0
        ),
        axis=1,
    )
    weighted = (upstream[0].astype(jnp.float32) * tok_adv[:, None]).astype(jnp.bfloat16)

    query_pos = sp_index * token_rows + jnp.arange(token_rows, dtype=jnp.int32)
    rel_block = jnp.arange(seq_len, dtype=jnp.int32) // token_rows
    key_pos = (sp_index - rel_block) * token_rows + jnp.arange(seq_len, dtype=jnp.int32) % token_rows
    allowed = (
        (own_seg[:, None] == key_seg[None, :])
        & (key_pos[None, :] <= query_pos[:, None])
        & (key_pos[None, :] >= 0)
    )
    query_grad, key_part, value_part = attend_pallas(
        packed_q, weighted, kv_all, allowed.astype(jnp.float32)
    )
    query_gradient = query_grad.reshape(1, token_rows, QUERY_HEADS * HEAD_SIZE)
    partial = jnp.concatenate(
        [
            key_part.reshape(reach + 1, token_rows, KEY_VALUE_HEADS * HEAD_SIZE),
            value_part.reshape(reach + 1, token_rows, KEY_VALUE_HEADS * HEAD_SIZE),
        ],
        axis=2,
    )
    kv_total = partial[0]
    for shift in range(1, reach + 1):
        kv_total = kv_total + lax.ppermute(
            partial[shift].astype(jnp.bfloat16),
            "sp",
            [(k, k - shift) for k in range(shift, sp_size)],
        ).astype(jnp.float32)
    kv_grads = kv_total.astype(jnp.bfloat16)
    return (query_gradient, kv_grads.reshape(1, token_rows, kv_width))


def solution(mesh):
    return jax.shard_map(
        body,
        mesh=mesh,
        in_specs=(
            P(("grp", "dp", "sp"), None),
            P("grp"),
            P(("grp", "dp"), "sp"),
            P(("grp", "dp"), "sp", None),
            P("grp"),
            P("grp"),
        ),
        out_specs=(P(("grp", "dp"), "sp", None), P(("grp", "dp"), "sp", None)),
        check_vma=False,
    )
```

```python
import math

import jax
import jax.numpy as jnp
from jax import lax
from jax.experimental import pallas as pl
from jax.sharding import PartitionSpec as P

QUERY_HEADS = 32
KEY_VALUE_HEADS = 4
HEAD_SIZE = 128
SEGS = 4
GROUP = 8
TESTS = 10


def group_advantage(passes, group_ids):
    reward = passes.astype(jnp.float32) / TESTS
    labels = jnp.arange(group_ids.shape[0] // GROUP, dtype=jnp.int32)
    member = (group_ids[:, None] == labels[None, :]).astype(jnp.float32)
    group_mean = jnp.sum(member * reward[:, None], axis=0) / jnp.sum(member, axis=0)
    return reward - jnp.sum(member * group_mean[None, :], axis=1)


def exchange_rows(rollout_rows, routing, dp_size, sp_size, dp_index, sp_index):
    token_rows = rollout_rows.shape[0]
    capacity = 2 * token_rows // dp_size
    layout_plan = routing.reshape(dp_size, sp_size, token_rows)
    column_plan = lax.dynamic_index_in_dim(layout_plan, sp_index, axis=1, keepdims=False)
    own_plan = lax.dynamic_index_in_dim(column_plan, dp_index, axis=0, keepdims=False)
    targets = jnp.arange(dp_size, dtype=jnp.int32)
    hit_table = (own_plan[:, None] == targets[None, :]).astype(jnp.int32)
    rank_rows = jnp.sum((jnp.cumsum(hit_table, axis=0) - 1) * hit_table, axis=1)
    slot_ids = own_plan * capacity + rank_rows
    slots = jnp.arange(dp_size * capacity, dtype=jnp.int32)
    send_pick = (slots[:, None] == slot_ids[None, :]).astype(rollout_rows.dtype)

    def send(columns):
        outgoing = jnp.dot(send_pick, columns, preferred_element_type=jnp.float32).astype(
            columns.dtype
        )
        return lax.all_to_all(
            outgoing.reshape(dp_size, capacity, -1), "dp", split_axis=0, concat_axis=0, tiled=True
        ).reshape(dp_size * capacity, -1)

    arrived_kv = send(rollout_rows[:, QUERY_HEADS * HEAD_SIZE :])
    half = QUERY_HEADS * HEAD_SIZE // 2
    arrived_q = [send(rollout_rows[:, part * half : (part + 1) * half]) for part in range(2)]
    load_table = jnp.sum((column_plan == dp_index).astype(jnp.int32), axis=1)
    end_marks = jnp.cumsum(load_table)
    start_marks = end_marks - load_table
    positions = jnp.arange(token_rows, dtype=jnp.int32)
    source = jnp.sum((positions[:, None] >= end_marks[None, :]).astype(jnp.int32), axis=1)
    chosen_start = jnp.sum(
        jnp.where(source[:, None] == targets[None, :], start_marks[None, :], 0), axis=1
    )
    pick_ids = source * capacity + positions - chosen_start
    recv_pick = (pick_ids[:, None] == slots[None, :]).astype(arrived_kv.dtype)

    def receive(arrived):
        return jnp.dot(recv_pick, arrived, preferred_element_type=jnp.float32).astype(arrived.dtype)

    return [receive(part) for part in arrived_q], receive(arrived_kv)


def attend(query, grads, key_mat, value_mat, allowed):
    inv_root = 1.0 / math.sqrt(HEAD_SIZE)
    scores = (
        jnp.einsum("tghd,sgd->tghs", query, key_mat, preferred_element_type=jnp.float32) * inv_root
    )
    scores = jnp.where(allowed[:, None, None, :], scores, -1e30)
    row_top = jnp.max(scores, axis=3, keepdims=True)
    scaled_exp = jnp.exp(scores - row_top)
    weights = scaled_exp / jnp.sum(scaled_exp, axis=3, keepdims=True)
    weight_grads = jnp.einsum(
        "tghd,sgd->tghs", grads, value_mat, preferred_element_type=jnp.float32
    )
    row_dot = jnp.sum(weights * weight_grads, axis=3, keepdims=True)
    score_grads = (weights * (weight_grads - row_dot) * inv_root).astype(jnp.bfloat16)
    query_grad = jnp.einsum(
        "tghs,sgd->tghd", score_grads, key_mat, preferred_element_type=jnp.float32
    ).astype(jnp.bfloat16)
    key_part = jnp.einsum("tghs,tghd->sgd", score_grads, query, preferred_element_type=jnp.float32)
    value_part = jnp.einsum(
        "tghs,tghd->sgd", weights.astype(jnp.bfloat16), grads, preferred_element_type=jnp.float32
    )
    return query_grad, key_part, value_part


def attend_kernel(q_ref, g_ref, k_ref, v_ref, m_ref, dq_ref, kp_ref, vp_ref):
    inv_root = 1.0 / math.sqrt(HEAD_SIZE)
    key_mat = k_ref[...]
    value_mat = v_ref[...]
    allowed = m_ref[...] > 0.5
    key_sum = jnp.zeros(kp_ref.shape, jnp.float32)
    value_sum = jnp.zeros(vp_ref.shape, jnp.float32)
    for head in range(q_ref.shape[1] // HEAD_SIZE):
        cols = slice(head * HEAD_SIZE, (head + 1) * HEAD_SIZE)
        query_head = q_ref[:, cols]
        grad_head = g_ref[:, cols]
        scores = (
            lax.dot_general(
                query_head, key_mat, (((1,), (1,)), ((), ())), preferred_element_type=jnp.float32
            )
            * inv_root
        )
        scores = jnp.where(allowed, scores, -1e30)
        row_top = jnp.max(scores, axis=1, keepdims=True)
        scaled_exp = jnp.exp(scores - row_top)
        weights = scaled_exp / jnp.sum(scaled_exp, axis=1, keepdims=True)
        weight_grads = lax.dot_general(
            grad_head, value_mat, (((1,), (1,)), ((), ())), preferred_element_type=jnp.float32
        )
        row_dot = jnp.sum(weights * weight_grads, axis=1, keepdims=True)
        score_grads = (weights * (weight_grads - row_dot) * inv_root).astype(jnp.bfloat16)
        dq_ref[:, cols] = jnp.dot(
            score_grads, key_mat, preferred_element_type=jnp.float32
        ).astype(dq_ref.dtype)
        key_sum = key_sum + lax.dot_general(
            score_grads, query_head, (((0,), (0,)), ((), ())), preferred_element_type=jnp.float32
        )
        value_sum = value_sum + lax.dot_general(
            weights.astype(jnp.bfloat16),
            grad_head,
            (((0,), (0,)), ((), ())),
            preferred_element_type=jnp.float32,
        )
    kp_ref[...] = key_sum
    vp_ref[...] = value_sum


def attend_pallas(packed, weighted, kv_all, mask, first_group, groups):
    token_rows = packed.shape[0]
    key_rows = kv_all.shape[0]
    group_width = QUERY_HEADS // KEY_VALUE_HEADS * HEAD_SIZE
    heads = groups * (QUERY_HEADS // KEY_VALUE_HEADS)
    flops = 10 * token_rows * key_rows * HEAD_SIZE * heads
    bytes_accessed = 6 * token_rows * heads * HEAD_SIZE + 12 * key_rows * groups * HEAD_SIZE + 4 * token_rows * key_rows
    return pl.pallas_call(
        attend_kernel,
        grid=(groups,),
        in_specs=[
            pl.BlockSpec((token_rows, group_width), lambda g: (0, g)),
            pl.BlockSpec((token_rows, group_width), lambda g: (0, g)),
            pl.BlockSpec((key_rows, HEAD_SIZE), lambda g: (0, first_group + g)),
            pl.BlockSpec((key_rows, HEAD_SIZE), lambda g: (0, KEY_VALUE_HEADS + first_group + g)),
            pl.BlockSpec((token_rows, key_rows), lambda g: (0, 0)),
        ],
        out_specs=[
            pl.BlockSpec((token_rows, group_width), lambda g: (0, g)),
            pl.BlockSpec((key_rows, HEAD_SIZE), lambda g: (0, g)),
            pl.BlockSpec((key_rows, HEAD_SIZE), lambda g: (0, g)),
        ],
        out_shape=[
            jax.ShapeDtypeStruct((token_rows, groups * group_width), jnp.bfloat16),
            jax.ShapeDtypeStruct((key_rows, groups * HEAD_SIZE), jnp.float32),
            jax.ShapeDtypeStruct((key_rows, groups * HEAD_SIZE), jnp.float32),
        ],
        cost_estimate=pl.CostEstimate(
            flops=flops, transcendentals=token_rows * key_rows * QUERY_HEADS, bytes_accessed=bytes_accessed
        ),
    )(packed, weighted, kv_all, kv_all, mask)


def body(rollout_rows, routing, segment_labels, upstream, passes, group_ids):
    dp_size = lax.axis_size("dp")
    sp_size = lax.axis_size("sp")
    dp_index = lax.axis_index("dp")
    sp_index = lax.axis_index("sp")
    token_rows = rollout_rows.shape[0]
    query_group = QUERY_HEADS // KEY_VALUE_HEADS
    kv_width = 2 * KEY_VALUE_HEADS * HEAD_SIZE
    longest_segment = sp_size * token_rows // 2
    reach = min(sp_size - 1, (longest_segment + token_rows - 2) // token_rows)
    seq_len = (reach + 1) * token_rows

    packed_q, packed_kv = exchange_rows(rollout_rows, routing, dp_size, sp_size, dp_index, sp_index)
    own_seg = segment_labels[0]
    label_cols = jnp.broadcast_to(own_seg.astype(jnp.bfloat16)[:, None], (token_rows, HEAD_SIZE))
    kv_local = jnp.concatenate([packed_kv, label_cols], axis=1)
    kv_rel = [kv_local] + [
        lax.ppermute(kv_local, "sp", [(k, k + shift) for k in range(sp_size - shift)])
        for shift in range(1, reach + 1)
    ]
    kv_all = jnp.concatenate(kv_rel, axis=0)
    key_seg = kv_all[:, kv_width].astype(jnp.int32)

    advantage = group_advantage(passes, group_ids)
    bin_adv = lax.dynamic_slice_in_dim(advantage, dp_index * SEGS, SEGS)
    tok_adv = jnp.sum(
        jnp.where(
            own_seg[:, None] == jnp.arange(SEGS, dtype=jnp.int32)[None, :], bin_adv[None, :], 0.0
        ),
        axis=1,
    )
    weighted = (upstream[0].astype(jnp.float32) * tok_adv[:, None]).astype(jnp.bfloat16)

    query_pos = sp_index * token_rows + jnp.arange(token_rows, dtype=jnp.int32)
    rel_block = jnp.arange(seq_len, dtype=jnp.int32) // token_rows
    key_pos = (sp_index - rel_block) * token_rows + jnp.arange(seq_len, dtype=jnp.int32) % token_rows
    allowed = (
        (own_seg[:, None] == key_seg[None, :])
        & (key_pos[None, :] <= query_pos[:, None])
        & (key_pos[None, :] >= 0)
    )
    mask = allowed.astype(jnp.float32)
    groups = KEY_VALUE_HEADS // 2
    half = QUERY_HEADS * HEAD_SIZE // 2
    query_parts, key_parts, value_parts = [], [], []
    for part in range(2):
        query_grad, key_part, value_part = attend_pallas(
            packed_q[part],
            weighted[:, part * half : (part + 1) * half],
            kv_all,
            mask,
            part * groups,
            groups,
        )
        partial = jnp.concatenate([key_part, value_part], axis=1).reshape(
            reach + 1, token_rows, 2 * groups * HEAD_SIZE
        )
        total = partial[0]
        for shift in range(1, reach + 1):
            total = total + lax.ppermute(
                partial[shift].astype(jnp.bfloat16),
                "sp",
                [(k, k - shift) for k in range(shift, sp_size)],
            ).astype(jnp.float32)
        query_parts.append(query_grad)
        key_parts.append(total[:, : groups * HEAD_SIZE])
        value_parts.append(total[:, groups * HEAD_SIZE :])
    query_gradient = jnp.concatenate(query_parts, axis=1).reshape(
        1, token_rows, QUERY_HEADS * HEAD_SIZE
    )
    kv_grads = jnp.concatenate(key_parts + value_parts, axis=1).astype(jnp.bfloat16)
    return (query_gradient, kv_grads.reshape(1, token_rows, kv_width))


def solution(mesh):
    return jax.shard_map(
        body,
        mesh=mesh,
        in_specs=(
            P(("grp", "dp", "sp"), None),
            P("grp"),
            P(("grp", "dp"), "sp"),
            P(("grp", "dp"), "sp", None),
            P("grp"),
            P("grp"),
        ),
        out_specs=(P(("grp", "dp"), "sp", None), P(("grp", "dp"), "sp", None)),
        check_vma=False,
    )
```

```python
import math

import jax
import jax.numpy as jnp
from jax import lax
from jax.experimental import pallas as pl
from jax.sharding import PartitionSpec as P

QUERY_HEADS = 32
KEY_VALUE_HEADS = 4
HEAD_SIZE = 128
SEGS = 4
GROUP = 8
TESTS = 10


def group_advantage(passes, group_ids):
    reward = passes.astype(jnp.float32) / TESTS
    labels = jnp.arange(group_ids.shape[0] // GROUP, dtype=jnp.int32)
    member = (group_ids[:, None] == labels[None, :]).astype(jnp.float32)
    group_mean = jnp.sum(member * reward[:, None], axis=0) / jnp.sum(member, axis=0)
    return reward - jnp.sum(member * group_mean[None, :], axis=1)


def exchange_rows(rollout_rows, routing, dp_size, sp_size, dp_index, sp_index):
    token_rows = rollout_rows.shape[0]
    capacity = 2 * token_rows // dp_size
    layout_plan = routing.reshape(dp_size, sp_size, token_rows)
    column_plan = lax.dynamic_index_in_dim(layout_plan, sp_index, axis=1, keepdims=False)
    own_plan = lax.dynamic_index_in_dim(column_plan, dp_index, axis=0, keepdims=False)
    targets = jnp.arange(dp_size, dtype=jnp.int32)
    hit_table = (own_plan[:, None] == targets[None, :]).astype(jnp.int32)
    rank_rows = jnp.sum((jnp.cumsum(hit_table, axis=0) - 1) * hit_table, axis=1)
    slot_ids = own_plan * capacity + rank_rows
    slots = jnp.arange(dp_size * capacity, dtype=jnp.int32)
    send_pick = (slots[:, None] == slot_ids[None, :]).astype(rollout_rows.dtype)

    def send(columns):
        outgoing = jnp.dot(send_pick, columns, preferred_element_type=jnp.float32).astype(
            columns.dtype
        )
        return lax.all_to_all(
            outgoing.reshape(dp_size, capacity, -1), "dp", split_axis=0, concat_axis=0, tiled=True
        ).reshape(dp_size * capacity, -1)

    arrived_kv = send(rollout_rows[:, QUERY_HEADS * HEAD_SIZE :])
    arrived_q = send(rollout_rows[:, : QUERY_HEADS * HEAD_SIZE])
    load_table = jnp.sum((column_plan == dp_index).astype(jnp.int32), axis=1)
    end_marks = jnp.cumsum(load_table)
    start_marks = end_marks - load_table
    positions = jnp.arange(token_rows, dtype=jnp.int32)
    source = jnp.sum((positions[:, None] >= end_marks[None, :]).astype(jnp.int32), axis=1)
    chosen_start = jnp.sum(
        jnp.where(source[:, None] == targets[None, :], start_marks[None, :], 0), axis=1
    )
    pick_ids = source * capacity + positions - chosen_start
    recv_pick = (pick_ids[:, None] == slots[None, :]).astype(arrived_kv.dtype)

    def receive(arrived):
        return jnp.dot(recv_pick, arrived, preferred_element_type=jnp.float32).astype(arrived.dtype)

    return receive(arrived_q), receive(arrived_kv)


def attend(query, grads, key_mat, value_mat, allowed):
    inv_root = 1.0 / math.sqrt(HEAD_SIZE)
    scores = (
        jnp.einsum("tghd,sgd->tghs", query, key_mat, preferred_element_type=jnp.float32) * inv_root
    )
    scores = jnp.where(allowed[:, None, None, :], scores, -1e30)
    row_top = jnp.max(scores, axis=3, keepdims=True)
    scaled_exp = jnp.exp(scores - row_top)
    weights = scaled_exp / jnp.sum(scaled_exp, axis=3, keepdims=True)
    weight_grads = jnp.einsum(
        "tghd,sgd->tghs", grads, value_mat, preferred_element_type=jnp.float32
    )
    row_dot = jnp.sum(weights * weight_grads, axis=3, keepdims=True)
    score_grads = (weights * (weight_grads - row_dot) * inv_root).astype(jnp.bfloat16)
    query_grad = jnp.einsum(
        "tghs,sgd->tghd", score_grads, key_mat, preferred_element_type=jnp.float32
    ).astype(jnp.bfloat16)
    key_part = jnp.einsum("tghs,tghd->sgd", score_grads, query, preferred_element_type=jnp.float32)
    value_part = jnp.einsum(
        "tghs,tghd->sgd", weights.astype(jnp.bfloat16), grads, preferred_element_type=jnp.float32
    )
    return query_grad, key_part, value_part


def attend_kernel(q_ref, g_ref, k_ref, v_ref, m_ref, dq_ref, kp_ref, vp_ref):
    inv_root = 1.0 / math.sqrt(HEAD_SIZE)
    key_mat = k_ref[...]
    value_mat = v_ref[...]
    allowed = m_ref[...] > 0.5
    key_sum = jnp.zeros(kp_ref.shape, jnp.float32)
    value_sum = jnp.zeros(vp_ref.shape, jnp.float32)
    for head in range(q_ref.shape[1] // HEAD_SIZE):
        cols = slice(head * HEAD_SIZE, (head + 1) * HEAD_SIZE)
        query_head = q_ref[:, cols]
        grad_head = g_ref[:, cols]
        scores = (
            lax.dot_general(
                key_mat, query_head, (((1,), (1,)), ((), ())), preferred_element_type=jnp.float32
            )
            * inv_root
        )
        scores = jnp.where(allowed, scores, -1e30)
        row_top = jnp.max(scores, axis=0, keepdims=True)
        scaled_exp = jnp.exp(scores - row_top)
        weights = scaled_exp / jnp.sum(scaled_exp, axis=0, keepdims=True)
        weight_grads = lax.dot_general(
            value_mat, grad_head, (((1,), (1,)), ((), ())), preferred_element_type=jnp.float32
        )
        row_dot = jnp.sum(weights * weight_grads, axis=0, keepdims=True)
        score_grads = (weights * (weight_grads - row_dot) * inv_root).astype(jnp.bfloat16)
        dq_ref[:, cols] = lax.dot_general(
            score_grads, key_mat, (((0,), (0,)), ((), ())), preferred_element_type=jnp.float32
        ).astype(dq_ref.dtype)
        key_sum = key_sum + jnp.dot(score_grads, query_head, preferred_element_type=jnp.float32)
        value_sum = value_sum + jnp.dot(
            weights.astype(jnp.bfloat16), grad_head, preferred_element_type=jnp.float32
        )
    kp_ref[...] = key_sum
    vp_ref[...] = value_sum


def attend_pallas(packed, weighted, kv_all, mask, first_group, groups):
    token_rows = packed.shape[0]
    key_rows = kv_all.shape[0]
    group_width = QUERY_HEADS // KEY_VALUE_HEADS * HEAD_SIZE
    heads = groups * (QUERY_HEADS // KEY_VALUE_HEADS)
    flops = 10 * token_rows * key_rows * HEAD_SIZE * heads
    bytes_accessed = 6 * token_rows * heads * HEAD_SIZE + 12 * key_rows * groups * HEAD_SIZE + 4 * token_rows * key_rows
    return pl.pallas_call(
        attend_kernel,
        grid=(groups,),
        in_specs=[
            pl.BlockSpec((token_rows, group_width), lambda g: (0, first_group + g)),
            pl.BlockSpec((token_rows, group_width), lambda g: (0, first_group + g)),
            pl.BlockSpec((key_rows, HEAD_SIZE), lambda g: (0, first_group + g)),
            pl.BlockSpec((key_rows, HEAD_SIZE), lambda g: (0, KEY_VALUE_HEADS + first_group + g)),
            pl.BlockSpec((key_rows, token_rows), lambda g: (0, 0)),
        ],
        out_specs=[
            pl.BlockSpec((token_rows, group_width), lambda g: (0, g)),
            pl.BlockSpec((key_rows, HEAD_SIZE), lambda g: (0, g)),
            pl.BlockSpec((key_rows, HEAD_SIZE), lambda g: (0, g)),
        ],
        out_shape=[
            jax.ShapeDtypeStruct((token_rows, groups * group_width), jnp.bfloat16),
            jax.ShapeDtypeStruct((key_rows, groups * HEAD_SIZE), jnp.float32),
            jax.ShapeDtypeStruct((key_rows, groups * HEAD_SIZE), jnp.float32),
        ],
        cost_estimate=pl.CostEstimate(
            flops=flops, transcendentals=token_rows * key_rows * QUERY_HEADS, bytes_accessed=bytes_accessed
        ),
    )(packed, weighted, kv_all, kv_all, mask)


def body(rollout_rows, routing, segment_labels, upstream, passes, group_ids):
    dp_size = lax.axis_size("dp")
    sp_size = lax.axis_size("sp")
    dp_index = lax.axis_index("dp")
    sp_index = lax.axis_index("sp")
    token_rows = rollout_rows.shape[0]
    query_group = QUERY_HEADS // KEY_VALUE_HEADS
    kv_width = 2 * KEY_VALUE_HEADS * HEAD_SIZE
    longest_segment = sp_size * token_rows // 2
    reach = min(sp_size - 1, (longest_segment + token_rows - 2) // token_rows)
    seq_len = (reach + 1) * token_rows

    packed_q, packed_kv = exchange_rows(rollout_rows, routing, dp_size, sp_size, dp_index, sp_index)
    own_seg = segment_labels[0]
    label_cols = jnp.broadcast_to(own_seg.astype(jnp.bfloat16)[:, None], (token_rows, HEAD_SIZE))
    kv_local = jnp.concatenate([packed_kv, label_cols], axis=1)
    kv_rel = [kv_local] + [
        lax.ppermute(kv_local, "sp", [(k, k + shift) for k in range(sp_size - shift)])
        for shift in range(1, reach + 1)
    ]
    kv_all = jnp.concatenate(kv_rel, axis=0)
    key_seg = kv_all[:, kv_width].astype(jnp.int32)

    advantage = group_advantage(passes, group_ids)
    bin_adv = lax.dynamic_slice_in_dim(advantage, dp_index * SEGS, SEGS)
    tok_adv = jnp.sum(
        jnp.where(
            own_seg[:, None] == jnp.arange(SEGS, dtype=jnp.int32)[None, :], bin_adv[None, :], 0.0
        ),
        axis=1,
    )
    weighted = (upstream[0].astype(jnp.float32) * tok_adv[:, None]).astype(jnp.bfloat16)

    query_pos = sp_index * token_rows + jnp.arange(token_rows, dtype=jnp.int32)
    rel_block = jnp.arange(seq_len, dtype=jnp.int32) // token_rows
    key_pos = (sp_index - rel_block) * token_rows + jnp.arange(seq_len, dtype=jnp.int32) % token_rows
    allowed = (
        (own_seg[:, None] == key_seg[None, :])
        & (key_pos[None, :] <= query_pos[:, None])
        & (key_pos[None, :] >= 0)
    )
    mask = allowed.T.astype(jnp.float32)
    groups = KEY_VALUE_HEADS // 2
    query_parts, key_parts, value_parts = [], [], []
    for part in range(2):
        query_grad, key_part, value_part = attend_pallas(
            packed_q,
            weighted,
            kv_all,
            mask,
            part * groups,
            groups,
        )
        partial = jnp.concatenate([key_part, value_part], axis=1).reshape(
            reach + 1, token_rows, 2 * groups * HEAD_SIZE
        )
        total = partial[0]
        for shift in range(1, reach + 1):
            total = total + lax.ppermute(
                partial[shift].astype(jnp.bfloat16),
                "sp",
                [(k, k - shift) for k in range(shift, sp_size)],
            ).astype(jnp.float32)
        query_parts.append(query_grad)
        key_parts.append(total[:, : groups * HEAD_SIZE])
        value_parts.append(total[:, groups * HEAD_SIZE :])
    query_gradient = jnp.concatenate(query_parts, axis=1).reshape(
        1, token_rows, QUERY_HEADS * HEAD_SIZE
    )
    kv_grads = jnp.concatenate(key_parts + value_parts, axis=1).astype(jnp.bfloat16)
    return (query_gradient, kv_grads.reshape(1, token_rows, kv_width))


def solution(mesh):
    return jax.shard_map(
        body,
        mesh=mesh,
        in_specs=(
            P(("grp", "dp", "sp"), None),
            P("grp"),
            P(("grp", "dp"), "sp"),
            P(("grp", "dp"), "sp", None),
            P("grp"),
            P("grp"),
        ),
        out_specs=(P(("grp", "dp"), "sp", None), P(("grp", "dp"), "sp", None)),
        check_vma=False,
    )
```

```python
import math

import jax
import jax.numpy as jnp
from jax import lax
from jax.experimental import pallas as pl
from jax.sharding import PartitionSpec as P


QUERY_HEADS = 32
KEY_VALUE_HEADS = 4
HEAD_SIZE = 128
SEGS = 4
GROUP = 8
TESTS = 10


def group_advantage(passes, group_ids):
    reward = passes.astype(jnp.float32) / TESTS
    labels = jnp.arange(group_ids.shape[0] // GROUP, dtype=jnp.int32)
    member = (group_ids[:, None] == labels[None, :]).astype(jnp.float32)
    group_mean = jnp.sum(member * reward[:, None], axis=0) / jnp.sum(member, axis=0)
    return reward - jnp.sum(member * group_mean[None, :], axis=1)


def exchange_rows(rollout_rows, routing, dp_size, sp_size, dp_index, sp_index):
    token_rows = rollout_rows.shape[0]
    capacity = 2 * token_rows // dp_size
    layout_plan = routing.reshape(dp_size, sp_size, token_rows)
    column_plan = lax.dynamic_index_in_dim(layout_plan, sp_index, axis=1, keepdims=False)
    own_plan = lax.dynamic_index_in_dim(column_plan, dp_index, axis=0, keepdims=False)
    targets = jnp.arange(dp_size, dtype=jnp.int32)
    hit_table = (own_plan[:, None] == targets[None, :]).astype(jnp.int32)
    rank_rows = jnp.sum((jnp.cumsum(hit_table, axis=0) - 1) * hit_table, axis=1)
    slot_ids = own_plan * capacity + rank_rows
    slots = jnp.arange(dp_size * capacity, dtype=jnp.int32)
    send_pick = (slots[:, None] == slot_ids[None, :]).astype(rollout_rows.dtype)

    def send(columns):
        outgoing = jnp.dot(send_pick, columns, preferred_element_type=jnp.float32).astype(
            columns.dtype
        )
        return lax.all_to_all(
            outgoing.reshape(dp_size, capacity, -1), "dp", split_axis=0, concat_axis=0, tiled=True
        ).reshape(dp_size * capacity, -1)

    arrived_kv = send(rollout_rows[:, QUERY_HEADS * HEAD_SIZE :])
    arrived_q = send(rollout_rows[:, : QUERY_HEADS * HEAD_SIZE])
    load_table = jnp.sum((column_plan == dp_index).astype(jnp.int32), axis=1)
    end_marks = jnp.cumsum(load_table)
    start_marks = end_marks - load_table
    positions = jnp.arange(token_rows, dtype=jnp.int32)
    source = jnp.sum((positions[:, None] >= end_marks[None, :]).astype(jnp.int32), axis=1)
    chosen_start = jnp.sum(
        jnp.where(source[:, None] == targets[None, :], start_marks[None, :], 0), axis=1
    )
    pick_ids = source * capacity + positions - chosen_start
    recv_pick = (pick_ids[:, None] == slots[None, :]).astype(arrived_kv.dtype)

    def receive(arrived):
        return jnp.dot(recv_pick, arrived, preferred_element_type=jnp.float32).astype(arrived.dtype)

    return receive(arrived_q), receive(arrived_kv)


def attend_kernel(q_ref, g_ref, k_ref, v_ref, m_ref, dq_ref, kp_ref, vp_ref):
    inv_root = 1.0 / math.sqrt(HEAD_SIZE)
    key_mat = k_ref[...]
    value_mat = v_ref[...]
    allowed = m_ref[...] > 0.5
    key_sum = jnp.zeros(kp_ref.shape, jnp.float32)
    value_sum = jnp.zeros(vp_ref.shape, jnp.float32)
    for head in range(q_ref.shape[1] // HEAD_SIZE):
        cols = slice(head * HEAD_SIZE, (head + 1) * HEAD_SIZE)
        query_head = q_ref[:, cols]
        grad_head = g_ref[:, cols]
        scores = (
            lax.dot_general(
                key_mat, query_head, (((1,), (1,)), ((), ())), preferred_element_type=jnp.float32
            )
            * inv_root
        )
        scores = jnp.where(allowed, scores, -1e30)
        row_top = jnp.max(scores, axis=0, keepdims=True)
        scaled_exp = jnp.exp(scores - row_top)
        weights = scaled_exp / jnp.sum(scaled_exp, axis=0, keepdims=True)
        weight_grads = lax.dot_general(
            value_mat, grad_head, (((1,), (1,)), ((), ())), preferred_element_type=jnp.float32
        )
        row_dot = jnp.sum(weights * weight_grads, axis=0, keepdims=True)
        score_grads = (weights * (weight_grads - row_dot) * inv_root).astype(jnp.bfloat16)
        dq_ref[:, cols] = lax.dot_general(
            score_grads, key_mat, (((0,), (0,)), ((), ())), preferred_element_type=jnp.float32
        ).astype(dq_ref.dtype)
        key_sum = key_sum + jnp.dot(score_grads, query_head, preferred_element_type=jnp.float32)
        value_sum = value_sum + jnp.dot(
            weights.astype(jnp.bfloat16), grad_head, preferred_element_type=jnp.float32
        )
    kp_ref[...] = key_sum
    vp_ref[...] = value_sum


def attend_pallas(packed, weighted, kv_all, mask, first_group, groups):
    token_rows = packed.shape[0]
    key_rows = kv_all.shape[0]
    group_width = QUERY_HEADS // KEY_VALUE_HEADS * HEAD_SIZE
    heads = groups * (QUERY_HEADS // KEY_VALUE_HEADS)
    flops = 10 * token_rows * key_rows * HEAD_SIZE * heads
    bytes_accessed = 6 * token_rows * heads * HEAD_SIZE + 12 * key_rows * groups * HEAD_SIZE + 4 * token_rows * key_rows
    return pl.pallas_call(
        attend_kernel,
        grid=(groups,),
        in_specs=[
            pl.BlockSpec((token_rows, group_width), lambda g: (0, first_group + g)),
            pl.BlockSpec((token_rows, group_width), lambda g: (0, first_group + g)),
            pl.BlockSpec((key_rows, HEAD_SIZE), lambda g: (0, first_group + g)),
            pl.BlockSpec((key_rows, HEAD_SIZE), lambda g: (0, KEY_VALUE_HEADS + first_group + g)),
            pl.BlockSpec((key_rows, token_rows), lambda g: (0, 0)),
        ],
        out_specs=[
            pl.BlockSpec((token_rows, group_width), lambda g: (0, g)),
            pl.BlockSpec((key_rows, HEAD_SIZE), lambda g: (0, g)),
            pl.BlockSpec((key_rows, HEAD_SIZE), lambda g: (0, g)),
        ],
        out_shape=[
            jax.ShapeDtypeStruct((token_rows, groups * group_width), jnp.bfloat16),
            jax.ShapeDtypeStruct((key_rows, groups * HEAD_SIZE), jnp.float32),
            jax.ShapeDtypeStruct((key_rows, groups * HEAD_SIZE), jnp.float32),
        ],
        cost_estimate=pl.CostEstimate(
            flops=flops, transcendentals=token_rows * key_rows * QUERY_HEADS, bytes_accessed=bytes_accessed
        ),
    )(packed, weighted, kv_all, kv_all, mask)


def step(rollout_rows, routing, segment_labels, upstream, passes, group_ids):
    dp_size = lax.axis_size("dp")
    sp_size = lax.axis_size("sp")
    dp_index = lax.axis_index("dp")
    sp_index = lax.axis_index("sp")
    token_rows = rollout_rows.shape[0]
    kv_width = 2 * KEY_VALUE_HEADS * HEAD_SIZE
    longest_segment = sp_size * token_rows // 2
    reach = min(sp_size - 1, (longest_segment + token_rows - 2) // token_rows)
    seq_len = (reach + 1) * token_rows

    packed_q, packed_kv = exchange_rows(rollout_rows, routing, dp_size, sp_size, dp_index, sp_index)
    own_seg = segment_labels[0]
    label_cols = jnp.broadcast_to(own_seg.astype(jnp.bfloat16)[:, None], (token_rows, HEAD_SIZE))
    kv_local = jnp.concatenate([packed_kv, label_cols], axis=1)
    kv_rel = [kv_local] + [
        lax.ppermute(kv_local, "sp", [(k, k + shift) for k in range(sp_size - shift)])
        for shift in range(1, reach + 1)
    ]
    kv_all = jnp.concatenate(kv_rel, axis=0)
    key_seg = kv_all[:, kv_width].astype(jnp.int32)

    advantage = group_advantage(passes, group_ids)
    bin_adv = lax.dynamic_slice_in_dim(advantage, dp_index * SEGS, SEGS)
    tok_adv = jnp.sum(
        jnp.where(
            own_seg[:, None] == jnp.arange(SEGS, dtype=jnp.int32)[None, :], bin_adv[None, :], 0.0
        ),
        axis=1,
    )
    weighted = (upstream[0].astype(jnp.float32) * tok_adv[:, None]).astype(jnp.bfloat16)

    query_pos = sp_index * token_rows + jnp.arange(token_rows, dtype=jnp.int32)
    rel_block = jnp.arange(seq_len, dtype=jnp.int32) // token_rows
    key_pos = (sp_index - rel_block) * token_rows + jnp.arange(seq_len, dtype=jnp.int32) % token_rows
    allowed = (
        (own_seg[:, None] == key_seg[None, :])
        & (key_pos[None, :] <= query_pos[:, None])
        & (key_pos[None, :] >= 0)
    )
    mask = allowed.T.astype(jnp.float32)
    groups = KEY_VALUE_HEADS // 2
    query_parts, key_parts, value_parts = [], [], []
    for part in range(2):
        query_grad, key_part, value_part = attend_pallas(
            packed_q, weighted, kv_all, mask, part * groups, groups
        )
        partial = jnp.concatenate([key_part, value_part], axis=1).reshape(
            reach + 1, token_rows, 2 * groups * HEAD_SIZE
        )
        total = partial[0]
        for shift in range(1, reach + 1):
            arrived = lax.ppermute(
                partial[shift].astype(jnp.bfloat16),
                "sp",
                [(k, k - shift) for k in range(shift, sp_size)],
            )
            total = total + arrived.astype(jnp.float32)
        query_parts.append(query_grad)
        key_parts.append(total[:, : groups * HEAD_SIZE])
        value_parts.append(total[:, groups * HEAD_SIZE :])
    query_gradient = jnp.concatenate(query_parts, axis=1).reshape(
        1, token_rows, QUERY_HEADS * HEAD_SIZE
    )
    kv_grads = jnp.concatenate(key_parts + value_parts, axis=1).astype(jnp.bfloat16)
    return (query_gradient, kv_grads.reshape(1, token_rows, kv_width))


def solution(mesh):
    return jax.shard_map(
        step,
        mesh=mesh,
        in_specs=(
            P(("grp", "dp", "sp"), None),
            P("grp"),
            P(("grp", "dp"), "sp"),
            P(("grp", "dp"), "sp", None),
            P("grp"),
            P("grp"),
        ),
        out_specs=(P(("grp", "dp"), "sp", None), P(("grp", "dp"), "sp", None)),
        check_vma=False,
    )
```

```python
import math

import jax
import jax.numpy as jnp
from jax import lax
from jax.experimental import pallas as pl
from jax.sharding import PartitionSpec as P


QUERY_HEADS = 32
KEY_VALUE_HEADS = 4
HEAD_SIZE = 128
SEGS = 4
GROUP = 8
TESTS = 10


def group_advantage(passes, group_ids):
    reward = passes.astype(jnp.float32) / TESTS
    labels = jnp.arange(group_ids.shape[0] // GROUP, dtype=jnp.int32)
    member = (group_ids[:, None] == labels[None, :]).astype(jnp.float32)
    group_mean = jnp.sum(member * reward[:, None], axis=0) / jnp.sum(member, axis=0)
    return reward - jnp.sum(member * group_mean[None, :], axis=1)


def exchange_rows(rollout_rows, routing, dp_size, sp_size, dp_index, sp_index):
    token_rows = rollout_rows.shape[0]
    capacity = 2 * token_rows // dp_size
    layout_plan = routing.reshape(dp_size, sp_size, token_rows)
    column_plan = lax.dynamic_index_in_dim(layout_plan, sp_index, axis=1, keepdims=False)
    own_plan = lax.dynamic_index_in_dim(column_plan, dp_index, axis=0, keepdims=False)
    targets = jnp.arange(dp_size, dtype=jnp.int32)
    hit_table = (own_plan[:, None] == targets[None, :]).astype(jnp.int32)
    rank_rows = jnp.sum((jnp.cumsum(hit_table, axis=0) - 1) * hit_table, axis=1)
    slots = jnp.arange(dp_size * capacity, dtype=jnp.int32)
    load_table = jnp.sum((column_plan == dp_index).astype(jnp.int32), axis=1)
    end_marks = jnp.cumsum(load_table)
    start_marks = end_marks - load_table
    positions = jnp.arange(token_rows, dtype=jnp.int32)
    source = jnp.sum((positions[:, None] >= end_marks[None, :]).astype(jnp.int32), axis=1)
    chosen_start = jnp.sum(
        jnp.where(source[:, None] == targets[None, :], start_marks[None, :], 0), axis=1
    )

    def send(columns, by_permute):
        target_slot = (own_plan - dp_index) % dp_size if by_permute else own_plan
        send_pick = (slots[:, None] == (target_slot * capacity + rank_rows)[None, :]).astype(
            columns.dtype
        )
        outgoing = jnp.dot(send_pick, columns, preferred_element_type=jnp.float32).astype(
            columns.dtype
        ).reshape(dp_size, capacity, -1)
        if by_permute:
            arrived = jnp.stack(
                [outgoing[0]]
                + [
                    lax.ppermute(
                        outgoing[shift], "dp", [(k, (k + shift) % dp_size) for k in range(dp_size)]
                    )
                    for shift in range(1, dp_size)
                ]
            )
            source_slot = (dp_index - source) % dp_size
        else:
            arrived = lax.all_to_all(outgoing, "dp", split_axis=0, concat_axis=0, tiled=True)
            source_slot = source
        pick_ids = source_slot * capacity + positions - chosen_start
        recv_pick = (pick_ids[:, None] == slots[None, :]).astype(columns.dtype)
        return jnp.dot(
            recv_pick, arrived.reshape(dp_size * capacity, -1), preferred_element_type=jnp.float32
        ).astype(columns.dtype)

    packed_kv = send(rollout_rows[:, QUERY_HEADS * HEAD_SIZE :], True)
    packed_q = send(rollout_rows[:, : QUERY_HEADS * HEAD_SIZE], False)
    return packed_q, packed_kv


def attend_kernel(q_ref, g_ref, k_ref, v_ref, m_ref, dq_ref, kp_ref, vp_ref):
    inv_root = 1.0 / math.sqrt(HEAD_SIZE)
    key_mat = k_ref[...]
    value_mat = v_ref[...]
    allowed = m_ref[...] > 0.5
    key_sum = jnp.zeros(kp_ref.shape, jnp.float32)
    value_sum = jnp.zeros(vp_ref.shape, jnp.float32)
    for head in range(q_ref.shape[1] // HEAD_SIZE):
        cols = slice(head * HEAD_SIZE, (head + 1) * HEAD_SIZE)
        query_head = q_ref[:, cols]
        grad_head = g_ref[:, cols]
        scores = (
            lax.dot_general(
                key_mat, query_head, (((1,), (1,)), ((), ())), preferred_element_type=jnp.float32
            )
            * inv_root
        )
        scores = jnp.where(allowed, scores, -1e30)
        row_top = jnp.max(scores, axis=0, keepdims=True)
        scaled_exp = jnp.exp(scores - row_top)
        weights = scaled_exp / jnp.sum(scaled_exp, axis=0, keepdims=True)
        weight_grads = lax.dot_general(
            value_mat, grad_head, (((1,), (1,)), ((), ())), preferred_element_type=jnp.float32
        )
        row_dot = jnp.sum(weights * weight_grads, axis=0, keepdims=True)
        score_grads = (weights * (weight_grads - row_dot) * inv_root).astype(jnp.bfloat16)
        dq_ref[:, cols] = lax.dot_general(
            score_grads, key_mat, (((0,), (0,)), ((), ())), preferred_element_type=jnp.float32
        ).astype(dq_ref.dtype)
        key_sum = key_sum + jnp.dot(score_grads, query_head, preferred_element_type=jnp.float32)
        value_sum = value_sum + jnp.dot(
            weights.astype(jnp.bfloat16), grad_head, preferred_element_type=jnp.float32
        )
    kp_ref[...] = key_sum
    vp_ref[...] = value_sum


def attend_pallas(packed, weighted, kv_all, mask, first_group, groups):
    token_rows = packed.shape[0]
    key_rows = kv_all.shape[0]
    group_width = QUERY_HEADS // KEY_VALUE_HEADS * HEAD_SIZE
    heads = groups * (QUERY_HEADS // KEY_VALUE_HEADS)
    flops = 10 * token_rows * key_rows * HEAD_SIZE * heads
    bytes_accessed = 6 * token_rows * heads * HEAD_SIZE + 12 * key_rows * groups * HEAD_SIZE + 4 * token_rows * key_rows
    return pl.pallas_call(
        attend_kernel,
        grid=(groups,),
        in_specs=[
            pl.BlockSpec((token_rows, group_width), lambda g: (0, first_group + g)),
            pl.BlockSpec((token_rows, group_width), lambda g: (0, first_group + g)),
            pl.BlockSpec((key_rows, HEAD_SIZE), lambda g: (0, first_group + g)),
            pl.BlockSpec((key_rows, HEAD_SIZE), lambda g: (0, KEY_VALUE_HEADS + first_group + g)),
            pl.BlockSpec((key_rows, token_rows), lambda g: (0, 0)),
        ],
        out_specs=[
            pl.BlockSpec((token_rows, group_width), lambda g: (0, g)),
            pl.BlockSpec((key_rows, HEAD_SIZE), lambda g: (0, g)),
            pl.BlockSpec((key_rows, HEAD_SIZE), lambda g: (0, g)),
        ],
        out_shape=[
            jax.ShapeDtypeStruct((token_rows, groups * group_width), jnp.bfloat16),
            jax.ShapeDtypeStruct((key_rows, groups * HEAD_SIZE), jnp.float32),
            jax.ShapeDtypeStruct((key_rows, groups * HEAD_SIZE), jnp.float32),
        ],
        cost_estimate=pl.CostEstimate(
            flops=flops, transcendentals=token_rows * key_rows * QUERY_HEADS, bytes_accessed=bytes_accessed
        ),
    )(packed, weighted, kv_all, kv_all, mask)


def step(rollout_rows, routing, segment_labels, upstream, passes, group_ids):
    dp_size = lax.axis_size("dp")
    sp_size = lax.axis_size("sp")
    dp_index = lax.axis_index("dp")
    sp_index = lax.axis_index("sp")
    token_rows = rollout_rows.shape[0]
    kv_width = 2 * KEY_VALUE_HEADS * HEAD_SIZE
    longest_segment = sp_size * token_rows // 2
    reach = min(sp_size - 1, (longest_segment + token_rows - 2) // token_rows)
    seq_len = (reach + 1) * token_rows

    packed_q, packed_kv = exchange_rows(rollout_rows, routing, dp_size, sp_size, dp_index, sp_index)
    own_seg = segment_labels[0]
    label_cols = jnp.broadcast_to(own_seg.astype(jnp.bfloat16)[:, None], (token_rows, HEAD_SIZE))
    kv_local = jnp.concatenate([packed_kv, label_cols], axis=1)
    kv_rel = [kv_local] + [
        lax.ppermute(kv_local, "sp", [(k, k + shift) for k in range(sp_size - shift)])
        for shift in range(1, reach + 1)
    ]
    kv_all = jnp.concatenate(kv_rel, axis=0)
    key_seg = kv_all[:, kv_width].astype(jnp.int32)

    advantage = group_advantage(passes, group_ids)
    bin_adv = lax.dynamic_slice_in_dim(advantage, dp_index * SEGS, SEGS)
    tok_adv = jnp.sum(
        jnp.where(
            own_seg[:, None] == jnp.arange(SEGS, dtype=jnp.int32)[None, :], bin_adv[None, :], 0.0
        ),
        axis=1,
    )
    weighted = (upstream[0].astype(jnp.float32) * tok_adv[:, None]).astype(jnp.bfloat16)

    query_pos = sp_index * token_rows + jnp.arange(token_rows, dtype=jnp.int32)
    rel_block = jnp.arange(seq_len, dtype=jnp.int32) // token_rows
    key_pos = (sp_index - rel_block) * token_rows + jnp.arange(seq_len, dtype=jnp.int32) % token_rows
    allowed = (
        (own_seg[:, None] == key_seg[None, :])
        & (key_pos[None, :] <= query_pos[:, None])
        & (key_pos[None, :] >= 0)
    )
    mask = allowed.T.astype(jnp.float32)
    groups = KEY_VALUE_HEADS // 2
    query_parts, key_parts, value_parts = [], [], []
    for part in range(2):
        query_grad, key_part, value_part = attend_pallas(
            packed_q, weighted, kv_all, mask, part * groups, groups
        )
        partial = jnp.concatenate([key_part, value_part], axis=1).reshape(
            reach + 1, token_rows, 2 * groups * HEAD_SIZE
        )
        total = partial[0]
        for shift in range(1, reach + 1):
            arrived = lax.ppermute(
                partial[shift].astype(jnp.bfloat16),
                "sp",
                [(k, k - shift) for k in range(shift, sp_size)],
            )
            total = total + arrived.astype(jnp.float32)
        query_parts.append(query_grad)
        key_parts.append(total[:, : groups * HEAD_SIZE])
        value_parts.append(total[:, groups * HEAD_SIZE :])
    query_gradient = jnp.concatenate(query_parts, axis=1).reshape(
        1, token_rows, QUERY_HEADS * HEAD_SIZE
    )
    kv_grads = jnp.concatenate(key_parts + value_parts, axis=1).astype(jnp.bfloat16)
    return (query_gradient, kv_grads.reshape(1, token_rows, kv_width))


def solution(mesh):
    return jax.shard_map(
        step,
        mesh=mesh,
        in_specs=(
            P(("grp", "dp", "sp"), None),
            P("grp"),
            P(("grp", "dp"), "sp"),
            P(("grp", "dp"), "sp", None),
            P("grp"),
            P("grp"),
        ),
        out_specs=(P(("grp", "dp"), "sp", None), P(("grp", "dp"), "sp", None)),
        check_vma=False,
    )
```

```python
import functools
import math

import jax
import jax.numpy as jnp
from jax import lax
from jax.experimental import pallas as pl
from jax.sharding import PartitionSpec as P


QUERY_HEADS = 32
KEY_VALUE_HEADS = 4
HEAD_SIZE = 128
SEGS = 4
GROUP = 8
TESTS = 10


def group_advantage(passes, group_ids):
    reward = passes.astype(jnp.float32) / TESTS
    labels = jnp.arange(group_ids.shape[0] // GROUP, dtype=jnp.int32)
    member = (group_ids[:, None] == labels[None, :]).astype(jnp.float32)
    group_mean = jnp.sum(member * reward[:, None], axis=0) / jnp.sum(member, axis=0)
    return reward - jnp.sum(member * group_mean[None, :], axis=1)


def exchange_rows(rollout_rows, routing, dp_size, sp_size, dp_index, sp_index):
    token_rows = rollout_rows.shape[0]
    capacity = 2 * token_rows // dp_size
    layout_plan = routing.reshape(dp_size, sp_size, token_rows)
    column_plan = lax.dynamic_index_in_dim(layout_plan, sp_index, axis=1, keepdims=False)
    own_plan = lax.dynamic_index_in_dim(column_plan, dp_index, axis=0, keepdims=False)
    targets = jnp.arange(dp_size, dtype=jnp.int32)
    hit_table = (own_plan[:, None] == targets[None, :]).astype(jnp.int32)
    rank_rows = jnp.sum((jnp.cumsum(hit_table, axis=0) - 1) * hit_table, axis=1)
    slots = jnp.arange(dp_size * capacity, dtype=jnp.int32)
    load_table = jnp.sum((column_plan == dp_index).astype(jnp.int32), axis=1)
    end_marks = jnp.cumsum(load_table)
    start_marks = end_marks - load_table
    positions = jnp.arange(token_rows, dtype=jnp.int32)
    source = jnp.sum((positions[:, None] >= end_marks[None, :]).astype(jnp.int32), axis=1)
    chosen_start = jnp.sum(
        jnp.where(source[:, None] == targets[None, :], start_marks[None, :], 0), axis=1
    )

    def send(columns, by_permute):
        target_slot = (own_plan - dp_index) % dp_size if by_permute else own_plan
        send_pick = (slots[:, None] == (target_slot * capacity + rank_rows)[None, :]).astype(
            columns.dtype
        )
        outgoing = jnp.dot(send_pick, columns, preferred_element_type=jnp.float32).astype(
            columns.dtype
        ).reshape(dp_size, capacity, -1)
        if by_permute:
            arrived = jnp.stack(
                [outgoing[0]]
                + [
                    lax.ppermute(
                        outgoing[shift], "dp", [(k, (k + shift) % dp_size) for k in range(dp_size)]
                    )
                    for shift in range(1, dp_size)
                ]
            )
            source_slot = (dp_index - source) % dp_size
        else:
            arrived = lax.all_to_all(outgoing, "dp", split_axis=0, concat_axis=0, tiled=True)
            source_slot = source
        pick_ids = source_slot * capacity + positions - chosen_start
        recv_pick = (pick_ids[:, None] == slots[None, :]).astype(columns.dtype)
        return jnp.dot(
            recv_pick, arrived.reshape(dp_size * capacity, -1), preferred_element_type=jnp.float32
        ).astype(columns.dtype)

    packed_kv = send(rollout_rows[:, QUERY_HEADS * HEAD_SIZE :], True)
    packed_q = send(rollout_rows[:, : QUERY_HEADS * HEAD_SIZE], False)
    return packed_q, packed_kv


def attend_kernel(q_ref, g_ref, kv_ref, m_ref, dq_ref, local_ref, send_ref, *, first_group):
    inv_root = 1.0 / math.sqrt(HEAD_SIZE)
    token_rows = q_ref.shape[0]
    groups = local_ref.shape[1] // (2 * HEAD_SIZE)
    query_group = QUERY_HEADS // KEY_VALUE_HEADS
    bias = m_ref[...]
    for local_group in range(groups):
        group = first_group + local_group
        key_mat = kv_ref[:, group * HEAD_SIZE : (group + 1) * HEAD_SIZE]
        value_mat = kv_ref[
            :, (KEY_VALUE_HEADS + group) * HEAD_SIZE : (KEY_VALUE_HEADS + group + 1) * HEAD_SIZE
        ]
        key_sum = jnp.zeros(key_mat.shape, jnp.float32)
        value_sum = jnp.zeros(value_mat.shape, jnp.float32)
        for head in range(query_group):
            cols = slice(
                (local_group * query_group + head) * HEAD_SIZE,
                (local_group * query_group + head + 1) * HEAD_SIZE,
            )
            query_head = q_ref[:, cols]
            grad_head = g_ref[:, cols]
            scores = (
                lax.dot_general(
                    key_mat, query_head, (((1,), (1,)), ((), ())), preferred_element_type=jnp.float32
                )
                * inv_root
                + bias
            )
            row_top = jnp.max(scores, axis=0, keepdims=True)
            scaled_exp = jnp.exp(scores - row_top)
            weights = scaled_exp * (1.0 / jnp.sum(scaled_exp, axis=0, keepdims=True))
            weight_grads = lax.dot_general(
                value_mat, grad_head, (((1,), (1,)), ((), ())), preferred_element_type=jnp.float32
            )
            row_dot = jnp.sum(weights * weight_grads, axis=0, keepdims=True)
            score_grads = (weights * (weight_grads - row_dot) * inv_root).astype(jnp.bfloat16)
            dq_ref[:, cols] = lax.dot_general(
                score_grads, key_mat, (((0,), (0,)), ((), ())), preferred_element_type=jnp.float32
            ).astype(dq_ref.dtype)
            key_sum = key_sum + jnp.dot(score_grads, query_head, preferred_element_type=jnp.float32)
            value_sum = value_sum + jnp.dot(
                weights.astype(jnp.bfloat16), grad_head, preferred_element_type=jnp.float32
            )
        key_cols = slice(local_group * HEAD_SIZE, (local_group + 1) * HEAD_SIZE)
        value_cols = slice((groups + local_group) * HEAD_SIZE, (groups + local_group + 1) * HEAD_SIZE)
        local_ref[:, key_cols] = key_sum[:token_rows]
        local_ref[:, value_cols] = value_sum[:token_rows]
        for back in range(send_ref.shape[0]):
            rows = slice((back + 1) * token_rows, (back + 2) * token_rows)
            send_ref[back, :, key_cols] = key_sum[rows].astype(send_ref.dtype)
            send_ref[back, :, value_cols] = value_sum[rows].astype(send_ref.dtype)


def attend_pallas(packed, weighted, kv_all, bias, part, groups):
    token_rows = packed.shape[0]
    key_rows = kv_all.shape[0]
    reach = key_rows // token_rows - 1
    part_width = groups * (QUERY_HEADS // KEY_VALUE_HEADS) * HEAD_SIZE
    kv_width = 2 * groups * HEAD_SIZE
    heads = groups * (QUERY_HEADS // KEY_VALUE_HEADS)
    flops = 10 * token_rows * key_rows * HEAD_SIZE * heads
    bytes_accessed = 6 * token_rows * part_width + 2 * key_rows * kv_all.shape[1] + 4 * token_rows * key_rows
    whole = lambda i: (0, 0)
    return pl.pallas_call(
        functools.partial(attend_kernel, first_group=part * groups),
        grid=(1,),
        in_specs=[
            pl.BlockSpec((token_rows, part_width), lambda i: (0, part)),
            pl.BlockSpec((token_rows, part_width), lambda i: (0, part)),
            pl.BlockSpec(kv_all.shape, whole),
            pl.BlockSpec(bias.shape, whole),
        ],
        out_specs=[
            pl.BlockSpec((token_rows, part_width), whole),
            pl.BlockSpec((token_rows, kv_width), whole),
            pl.BlockSpec((reach, token_rows, kv_width), lambda i: (0, 0, 0)),
        ],
        out_shape=[
            jax.ShapeDtypeStruct((token_rows, part_width), jnp.bfloat16),
            jax.ShapeDtypeStruct((token_rows, kv_width), jnp.float32),
            jax.ShapeDtypeStruct((reach, token_rows, kv_width), jnp.bfloat16),
        ],
        cost_estimate=pl.CostEstimate(
            flops=flops, transcendentals=token_rows * key_rows * heads, bytes_accessed=bytes_accessed
        ),
    )(packed, weighted, kv_all, bias)


def step(rollout_rows, routing, segment_labels, upstream, passes, group_ids):
    dp_size = lax.axis_size("dp")
    sp_size = lax.axis_size("sp")
    dp_index = lax.axis_index("dp")
    sp_index = lax.axis_index("sp")
    token_rows = rollout_rows.shape[0]
    kv_width = 2 * KEY_VALUE_HEADS * HEAD_SIZE
    longest_segment = sp_size * token_rows // 2
    reach = min(sp_size - 1, (longest_segment + token_rows - 2) // token_rows)
    seq_len = (reach + 1) * token_rows

    packed_q, packed_kv = exchange_rows(rollout_rows, routing, dp_size, sp_size, dp_index, sp_index)
    own_seg = segment_labels[0]
    label_cols = jnp.broadcast_to(own_seg.astype(jnp.bfloat16)[:, None], (token_rows, HEAD_SIZE))
    kv_local = jnp.concatenate([packed_kv, label_cols], axis=1)
    kv_rel = [kv_local] + [
        lax.ppermute(kv_local, "sp", [(k, k + shift) for k in range(sp_size - shift)])
        for shift in range(1, reach + 1)
    ]
    kv_all = jnp.concatenate(kv_rel, axis=0)
    key_seg = kv_all[:, kv_width].astype(jnp.int32)

    advantage = group_advantage(passes, group_ids)
    bin_adv = lax.dynamic_slice_in_dim(advantage, dp_index * SEGS, SEGS)
    tok_adv = jnp.sum(
        jnp.where(
            own_seg[:, None] == jnp.arange(SEGS, dtype=jnp.int32)[None, :], bin_adv[None, :], 0.0
        ),
        axis=1,
    )
    weighted = (upstream[0].astype(jnp.float32) * tok_adv[:, None]).astype(jnp.bfloat16)

    query_pos = sp_index * token_rows + jnp.arange(token_rows, dtype=jnp.int32)
    rel_block = jnp.arange(seq_len, dtype=jnp.int32) // token_rows
    key_pos = (sp_index - rel_block) * token_rows + jnp.arange(seq_len, dtype=jnp.int32) % token_rows
    allowed = (
        (own_seg[:, None] == key_seg[None, :])
        & (key_pos[None, :] <= query_pos[:, None])
        & (key_pos[None, :] >= 0)
    )
    bias = jnp.where(allowed.T, 0.0, -1e30).astype(jnp.float32)
    groups = KEY_VALUE_HEADS // 2
    query_parts, key_parts, value_parts = [], [], []
    for part in range(2):
        query_grad, total, outgoing = attend_pallas(
            packed_q, weighted, kv_all, bias, part, groups
        )
        for shift in range(1, reach + 1):
            arrived = lax.ppermute(
                outgoing[shift - 1], "sp", [(k, k - shift) for k in range(shift, sp_size)]
            )
            total = total + arrived.astype(jnp.float32)
        query_parts.append(query_grad)
        key_parts.append(total[:, : groups * HEAD_SIZE])
        value_parts.append(total[:, groups * HEAD_SIZE :])
    query_gradient = jnp.concatenate(query_parts, axis=1).reshape(
        1, token_rows, QUERY_HEADS * HEAD_SIZE
    )
    kv_grads = jnp.concatenate(key_parts + value_parts, axis=1).astype(jnp.bfloat16)
    return (query_gradient, kv_grads.reshape(1, token_rows, kv_width))


def solution(mesh):
    return jax.shard_map(
        step,
        mesh=mesh,
        in_specs=(
            P(("grp", "dp", "sp"), None),
            P("grp"),
            P(("grp", "dp"), "sp"),
            P(("grp", "dp"), "sp", None),
            P("grp"),
            P("grp"),
        ),
        out_specs=(P(("grp", "dp"), "sp", None), P(("grp", "dp"), "sp", None)),
        check_vma=False,
    )
```

```python
import functools
import math

import jax
import jax.numpy as jnp
from jax import lax
from jax.experimental import pallas as pl
from jax.sharding import PartitionSpec as P


QUERY_HEADS = 32
KEY_VALUE_HEADS = 4
HEAD_SIZE = 128
SEGS = 4
GROUP = 8
TESTS = 10


def group_advantage(passes, group_ids):
    reward = passes.astype(jnp.float32) / TESTS
    labels = jnp.arange(group_ids.shape[0] // GROUP, dtype=jnp.int32)
    member = (group_ids[:, None] == labels[None, :]).astype(jnp.float32)
    group_mean = jnp.sum(member * reward[:, None], axis=0) / jnp.sum(member, axis=0)
    return reward - jnp.sum(member * group_mean[None, :], axis=1)


def exchange_rows(rollout_rows, routing, dp_size, sp_size, dp_index, sp_index):
    token_rows = rollout_rows.shape[0]
    capacity = 2 * token_rows // dp_size
    layout_plan = routing.reshape(dp_size, sp_size, token_rows)
    column_plan = lax.dynamic_index_in_dim(layout_plan, sp_index, axis=1, keepdims=False)
    own_plan = lax.dynamic_index_in_dim(column_plan, dp_index, axis=0, keepdims=False)
    targets = jnp.arange(dp_size, dtype=jnp.int32)
    hit_table = (own_plan[:, None] == targets[None, :]).astype(jnp.int32)
    rank_rows = jnp.sum((jnp.cumsum(hit_table, axis=0) - 1) * hit_table, axis=1)
    slots = jnp.arange(dp_size * capacity, dtype=jnp.int32)
    load_table = jnp.sum((column_plan == dp_index).astype(jnp.int32), axis=1)
    end_marks = jnp.cumsum(load_table)
    start_marks = end_marks - load_table
    positions = jnp.arange(token_rows, dtype=jnp.int32)
    source = jnp.sum((positions[:, None] >= end_marks[None, :]).astype(jnp.int32), axis=1)
    chosen_start = jnp.sum(
        jnp.where(source[:, None] == targets[None, :], start_marks[None, :], 0), axis=1
    )

    def send(columns, by_permute):
        target_slot = (own_plan - dp_index) % dp_size if by_permute else own_plan
        send_pick = (slots[:, None] == (target_slot * capacity + rank_rows)[None, :]).astype(
            columns.dtype
        )
        outgoing = jnp.dot(send_pick, columns, preferred_element_type=jnp.float32).astype(
            columns.dtype
        ).reshape(dp_size, capacity, -1)
        if by_permute:
            arrived = jnp.stack(
                [outgoing[0]]
                + [
                    lax.ppermute(
                        outgoing[shift], "dp", [(k, (k + shift) % dp_size) for k in range(dp_size)]
                    )
                    for shift in range(1, dp_size)
                ]
            )
            source_slot = (dp_index - source) % dp_size
        else:
            arrived = lax.all_to_all(outgoing, "dp", split_axis=0, concat_axis=0, tiled=True)
            source_slot = source
        pick_ids = source_slot * capacity + positions - chosen_start
        recv_pick = (pick_ids[:, None] == slots[None, :]).astype(columns.dtype)
        return jnp.dot(
            recv_pick, arrived.reshape(dp_size * capacity, -1), preferred_element_type=jnp.float32
        ).astype(columns.dtype)

    packed_kv = send(rollout_rows[:, QUERY_HEADS * HEAD_SIZE :], True)
    packed_q = send(rollout_rows[:, : QUERY_HEADS * HEAD_SIZE], True)
    return packed_q, packed_kv


def attend_kernel(q_ref, g_ref, kv_ref, m_ref, dq_ref, local_ref, *send_refs, first_group):
    inv_root = 1.0 / math.sqrt(HEAD_SIZE)
    token_rows = q_ref.shape[0]
    groups = local_ref.shape[1] // (2 * HEAD_SIZE)
    query_group = QUERY_HEADS // KEY_VALUE_HEADS
    bias = m_ref[...]
    for local_group in range(groups):
        group = first_group + local_group
        key_mat = kv_ref[:, group * HEAD_SIZE : (group + 1) * HEAD_SIZE]
        value_mat = kv_ref[
            :, (KEY_VALUE_HEADS + group) * HEAD_SIZE : (KEY_VALUE_HEADS + group + 1) * HEAD_SIZE
        ]
        key_sum = jnp.zeros(key_mat.shape, jnp.float32)
        value_sum = jnp.zeros(value_mat.shape, jnp.float32)
        for head in range(query_group):
            cols = slice(
                (local_group * query_group + head) * HEAD_SIZE,
                (local_group * query_group + head + 1) * HEAD_SIZE,
            )
            query_head = q_ref[:, cols]
            grad_head = g_ref[:, cols]
            scores = (
                lax.dot_general(
                    key_mat, query_head, (((1,), (1,)), ((), ())), preferred_element_type=jnp.float32
                )
                * inv_root
                + bias
            )
            row_top = jnp.max(scores, axis=0, keepdims=True)
            scaled_exp = jnp.exp(scores - row_top)
            weights = scaled_exp * (1.0 / jnp.sum(scaled_exp, axis=0, keepdims=True))
            weight_grads = lax.dot_general(
                value_mat, grad_head, (((1,), (1,)), ((), ())), preferred_element_type=jnp.float32
            )
            row_dot = jnp.sum(weights * weight_grads, axis=0, keepdims=True)
            score_grads = (weights * (weight_grads - row_dot) * inv_root).astype(jnp.bfloat16)
            dq_ref[:, cols] = lax.dot_general(
                score_grads, key_mat, (((0,), (0,)), ((), ())), preferred_element_type=jnp.float32
            ).astype(dq_ref.dtype)
            key_sum = key_sum + jnp.dot(score_grads, query_head, preferred_element_type=jnp.float32)
            value_sum = value_sum + jnp.dot(
                weights.astype(jnp.bfloat16), grad_head, preferred_element_type=jnp.float32
            )
        key_cols = slice(local_group * HEAD_SIZE, (local_group + 1) * HEAD_SIZE)
        value_cols = slice((groups + local_group) * HEAD_SIZE, (groups + local_group + 1) * HEAD_SIZE)
        local_ref[:, key_cols] = key_sum[:token_rows]
        local_ref[:, value_cols] = value_sum[:token_rows]
        for back, send_ref in enumerate(send_refs):
            rows = slice((back + 1) * token_rows, (back + 2) * token_rows)
            send_ref[:, key_cols] = key_sum[rows].astype(send_ref.dtype)
            send_ref[:, value_cols] = value_sum[rows].astype(send_ref.dtype)


def attend_pallas(packed, weighted, kv_all, bias, part, groups):
    token_rows = packed.shape[0]
    key_rows = kv_all.shape[0]
    reach = key_rows // token_rows - 1
    part_width = groups * (QUERY_HEADS // KEY_VALUE_HEADS) * HEAD_SIZE
    kv_width = 2 * groups * HEAD_SIZE
    heads = groups * (QUERY_HEADS // KEY_VALUE_HEADS)
    flops = 10 * token_rows * key_rows * HEAD_SIZE * heads
    bytes_accessed = 6 * token_rows * part_width + 2 * key_rows * kv_all.shape[1] + 4 * token_rows * key_rows
    whole = lambda i: (0, 0)
    return pl.pallas_call(
        functools.partial(attend_kernel, first_group=part * groups),
        grid=(1,),
        in_specs=[
            pl.BlockSpec((token_rows, part_width), lambda i: (0, part)),
            pl.BlockSpec((token_rows, part_width), lambda i: (0, part)),
            pl.BlockSpec(kv_all.shape, whole),
            pl.BlockSpec(bias.shape, whole),
        ],
        out_specs=[
            pl.BlockSpec((token_rows, part_width), whole)
        ]
        + [pl.BlockSpec((token_rows, kv_width), whole) for _ in range(reach + 1)],
        out_shape=[
            jax.ShapeDtypeStruct((token_rows, part_width), jnp.bfloat16),
            jax.ShapeDtypeStruct((token_rows, kv_width), jnp.float32),
        ]
        + [jax.ShapeDtypeStruct((token_rows, kv_width), jnp.bfloat16) for _ in range(reach)],
        cost_estimate=pl.CostEstimate(
            flops=flops, transcendentals=token_rows * key_rows * heads, bytes_accessed=bytes_accessed
        ),
    )(packed, weighted, kv_all, bias)


def step(rollout_rows, routing, segment_labels, upstream, passes, group_ids):
    dp_size = lax.axis_size("dp")
    sp_size = lax.axis_size("sp")
    dp_index = lax.axis_index("dp")
    sp_index = lax.axis_index("sp")
    token_rows = rollout_rows.shape[0]
    kv_width = 2 * KEY_VALUE_HEADS * HEAD_SIZE
    longest_segment = sp_size * token_rows // 2
    reach = min(sp_size - 1, (longest_segment + token_rows - 2) // token_rows)
    seq_len = (reach + 1) * token_rows

    packed_q, packed_kv = exchange_rows(rollout_rows, routing, dp_size, sp_size, dp_index, sp_index)
    own_seg = segment_labels[0]
    label_cols = jnp.broadcast_to(own_seg.astype(jnp.bfloat16)[:, None], (token_rows, HEAD_SIZE))
    kv_local = jnp.concatenate([packed_kv, label_cols], axis=1)
    kv_rel = [kv_local] + [
        lax.ppermute(kv_local, "sp", [(k, k + shift) for k in range(sp_size - shift)])
        for shift in range(1, reach + 1)
    ]
    kv_all = jnp.concatenate(kv_rel, axis=0)
    key_seg = kv_all[:, kv_width].astype(jnp.int32)

    advantage = group_advantage(passes, group_ids)
    bin_adv = lax.dynamic_slice_in_dim(advantage, dp_index * SEGS, SEGS)
    tok_adv = jnp.sum(
        jnp.where(
            own_seg[:, None] == jnp.arange(SEGS, dtype=jnp.int32)[None, :], bin_adv[None, :], 0.0
        ),
        axis=1,
    )
    weighted = (upstream[0].astype(jnp.float32) * tok_adv[:, None]).astype(jnp.bfloat16)

    query_pos = sp_index * token_rows + jnp.arange(token_rows, dtype=jnp.int32)
    rel_block = jnp.arange(seq_len, dtype=jnp.int32) // token_rows
    key_pos = (sp_index - rel_block) * token_rows + jnp.arange(seq_len, dtype=jnp.int32) % token_rows
    allowed = (
        (own_seg[:, None] == key_seg[None, :])
        & (key_pos[None, :] <= query_pos[:, None])
        & (key_pos[None, :] >= 0)
    )
    bias = jnp.where(allowed.T, 0.0, -1e30).astype(jnp.float32)
    groups = KEY_VALUE_HEADS // 2
    query_parts, key_parts, value_parts = [], [], []
    for part in range(2):
        query_grad, total, *outgoing = attend_pallas(
            packed_q, weighted, kv_all, bias, part, groups
        )
        for shift in range(1, reach + 1):
            arrived = lax.ppermute(
                outgoing[shift - 1], "sp", [(k, k - shift) for k in range(shift, sp_size)]
            )
            total = total + arrived.astype(jnp.float32)
        query_parts.append(query_grad)
        key_parts.append(total[:, : groups * HEAD_SIZE])
        value_parts.append(total[:, groups * HEAD_SIZE :])
    query_gradient = jnp.concatenate(query_parts, axis=1).reshape(
        1, token_rows, QUERY_HEADS * HEAD_SIZE
    )
    kv_grads = jnp.concatenate(key_parts + value_parts, axis=1).astype(jnp.bfloat16)
    return (query_gradient, kv_grads.reshape(1, token_rows, kv_width))


def solution(mesh):
    return jax.shard_map(
        step,
        mesh=mesh,
        in_specs=(
            P(("grp", "dp", "sp"), None),
            P("grp"),
            P(("grp", "dp"), "sp"),
            P(("grp", "dp"), "sp", None),
            P("grp"),
            P("grp"),
        ),
        out_specs=(P(("grp", "dp"), "sp", None), P(("grp", "dp"), "sp", None)),
        check_vma=False,
    )
```

```python
import functools
import math

import jax
import jax.numpy as jnp
from jax import lax
from jax.experimental import pallas as pl
from jax.sharding import PartitionSpec as P


QUERY_HEADS = 32
KEY_VALUE_HEADS = 4
HEAD_SIZE = 128
SEGS = 4
GROUP = 8
TESTS = 10


def group_advantage(passes, group_ids):
    reward = passes.astype(jnp.float32) / TESTS
    labels = jnp.arange(group_ids.shape[0] // GROUP, dtype=jnp.int32)
    member = (group_ids[:, None] == labels[None, :]).astype(jnp.float32)
    group_mean = jnp.sum(member * reward[:, None], axis=0) / jnp.sum(member, axis=0)
    return reward - jnp.sum(member * group_mean[None, :], axis=1)


def exchange_rows(rollout_rows, routing, dp_size, sp_size, dp_index, sp_index):
    token_rows = rollout_rows.shape[0]
    capacity = 2 * token_rows // dp_size
    layout_plan = routing.reshape(dp_size, sp_size, token_rows)
    column_plan = lax.dynamic_index_in_dim(layout_plan, sp_index, axis=1, keepdims=False)
    own_plan = lax.dynamic_index_in_dim(column_plan, dp_index, axis=0, keepdims=False)
    targets = jnp.arange(dp_size, dtype=jnp.int32)
    hit_table = (own_plan[:, None] == targets[None, :]).astype(jnp.int32)
    rank_rows = jnp.sum((jnp.cumsum(hit_table, axis=0) - 1) * hit_table, axis=1)
    slots = jnp.arange(dp_size * capacity, dtype=jnp.int32)
    load_table = jnp.sum((column_plan == dp_index).astype(jnp.int32), axis=1)
    end_marks = jnp.cumsum(load_table)
    start_marks = end_marks - load_table
    positions = jnp.arange(token_rows, dtype=jnp.int32)
    source = jnp.sum((positions[:, None] >= end_marks[None, :]).astype(jnp.int32), axis=1)
    chosen_start = jnp.sum(
        jnp.where(source[:, None] == targets[None, :], start_marks[None, :], 0), axis=1
    )

    def send(columns, by_permute):
        target_slot = (own_plan - dp_index) % dp_size if by_permute else own_plan
        send_pick = (slots[:, None] == (target_slot * capacity + rank_rows)[None, :]).astype(
            columns.dtype
        )
        outgoing = jnp.dot(send_pick, columns, preferred_element_type=jnp.float32).astype(
            columns.dtype
        ).reshape(dp_size, capacity, -1)
        if by_permute:
            chunks = [outgoing[0]] + [
                lax.ppermute(
                    outgoing[shift], "dp", [(k, (k + shift) % dp_size) for k in range(dp_size)]
                )
                for shift in range(1, dp_size)
            ]
            source_slot = (dp_index - source) % dp_size
        else:
            arrived = lax.all_to_all(outgoing, "dp", split_axis=0, concat_axis=0, tiled=True)
            chunks = [arrived[k] for k in range(dp_size)]
            source_slot = source
        pick_ids = source_slot * capacity + positions - chosen_start
        recv_pick = (pick_ids[:, None] == slots[None, :]).astype(columns.dtype)
        packed = sum(
            jnp.dot(
                recv_pick[:, k * capacity : (k + 1) * capacity],
                chunk,
                preferred_element_type=jnp.float32,
            )
            for k, chunk in enumerate(chunks)
        )
        return packed.astype(columns.dtype)

    packed_kv = send(rollout_rows[:, QUERY_HEADS * HEAD_SIZE :], True)
    packed_q = send(rollout_rows[:, : QUERY_HEADS * HEAD_SIZE], True)
    return packed_q, packed_kv


def attend_kernel(q_ref, g_ref, kv_ref, m_ref, dq_ref, local_ref, *send_refs, first_group):
    inv_root = 1.0 / math.sqrt(HEAD_SIZE)
    token_rows = q_ref.shape[0]
    groups = local_ref.shape[1] // (2 * HEAD_SIZE)
    query_group = QUERY_HEADS // KEY_VALUE_HEADS
    bias = m_ref[...]
    for local_group in range(groups):
        group = first_group + local_group
        key_mat = kv_ref[:, group * HEAD_SIZE : (group + 1) * HEAD_SIZE]
        value_mat = kv_ref[
            :, (KEY_VALUE_HEADS + group) * HEAD_SIZE : (KEY_VALUE_HEADS + group + 1) * HEAD_SIZE
        ]
        key_sum = jnp.zeros(key_mat.shape, jnp.float32)
        value_sum = jnp.zeros(value_mat.shape, jnp.float32)
        for head in range(query_group):
            cols = slice(
                (local_group * query_group + head) * HEAD_SIZE,
                (local_group * query_group + head + 1) * HEAD_SIZE,
            )
            query_head = q_ref[:, cols]
            grad_head = g_ref[:, cols]
            scores = (
                lax.dot_general(
                    key_mat, query_head, (((1,), (1,)), ((), ())), preferred_element_type=jnp.float32
                )
                * inv_root
                + bias
            )
            row_top = jnp.max(scores, axis=0, keepdims=True)
            scaled_exp = jnp.exp(scores - row_top)
            weights = scaled_exp * (1.0 / jnp.sum(scaled_exp, axis=0, keepdims=True))
            weight_grads = lax.dot_general(
                value_mat, grad_head, (((1,), (1,)), ((), ())), preferred_element_type=jnp.float32
            )
            row_dot = jnp.sum(weights * weight_grads, axis=0, keepdims=True)
            score_grads = (weights * (weight_grads - row_dot) * inv_root).astype(jnp.bfloat16)
            dq_ref[:, cols] = lax.dot_general(
                score_grads, key_mat, (((0,), (0,)), ((), ())), preferred_element_type=jnp.float32
            ).astype(dq_ref.dtype)
            key_sum = key_sum + jnp.dot(score_grads, query_head, preferred_element_type=jnp.float32)
            value_sum = value_sum + jnp.dot(
                weights.astype(jnp.bfloat16), grad_head, preferred_element_type=jnp.float32
            )
        key_cols = slice(local_group * HEAD_SIZE, (local_group + 1) * HEAD_SIZE)
        value_cols = slice((groups + local_group) * HEAD_SIZE, (groups + local_group + 1) * HEAD_SIZE)
        local_ref[:, key_cols] = key_sum[:token_rows]
        local_ref[:, value_cols] = value_sum[:token_rows]
        for back, send_ref in enumerate(send_refs):
            rows = slice((back + 1) * token_rows, (back + 2) * token_rows)
            send_ref[:, key_cols] = key_sum[rows].astype(send_ref.dtype)
            send_ref[:, value_cols] = value_sum[rows].astype(send_ref.dtype)


def attend_pallas(packed, weighted, kv_all, bias, part, groups):
    token_rows = packed.shape[0]
    key_rows = kv_all.shape[0]
    reach = key_rows // token_rows - 1
    part_width = groups * (QUERY_HEADS // KEY_VALUE_HEADS) * HEAD_SIZE
    kv_width = 2 * groups * HEAD_SIZE
    heads = groups * (QUERY_HEADS // KEY_VALUE_HEADS)
    flops = 10 * token_rows * key_rows * HEAD_SIZE * heads
    bytes_accessed = 6 * token_rows * part_width + 2 * key_rows * kv_all.shape[1] + 4 * token_rows * key_rows
    whole = lambda i: (0, 0)
    return pl.pallas_call(
        functools.partial(attend_kernel, first_group=part * groups),
        grid=(1,),
        in_specs=[
            pl.BlockSpec((token_rows, part_width), lambda i: (0, part)),
            pl.BlockSpec((token_rows, part_width), lambda i: (0, part)),
            pl.BlockSpec(kv_all.shape, whole),
            pl.BlockSpec(bias.shape, whole),
        ],
        out_specs=[
            pl.BlockSpec((token_rows, part_width), whole)
        ]
        + [pl.BlockSpec((token_rows, kv_width), whole) for _ in range(reach + 1)],
        out_shape=[
            jax.ShapeDtypeStruct((token_rows, part_width), jnp.bfloat16),
            jax.ShapeDtypeStruct((token_rows, kv_width), jnp.float32),
        ]
        + [jax.ShapeDtypeStruct((token_rows, kv_width), jnp.bfloat16) for _ in range(reach)],
        cost_estimate=pl.CostEstimate(
            flops=flops, transcendentals=token_rows * key_rows * heads, bytes_accessed=bytes_accessed
        ),
    )(packed, weighted, kv_all, bias)


def step(rollout_rows, routing, segment_labels, upstream, passes, group_ids):
    dp_size = lax.axis_size("dp")
    sp_size = lax.axis_size("sp")
    dp_index = lax.axis_index("dp")
    sp_index = lax.axis_index("sp")
    token_rows = rollout_rows.shape[0]
    kv_width = 2 * KEY_VALUE_HEADS * HEAD_SIZE
    longest_segment = sp_size * token_rows // 2
    reach = min(sp_size - 1, (longest_segment + token_rows - 2) // token_rows)
    seq_len = (reach + 1) * token_rows

    packed_q, packed_kv = exchange_rows(rollout_rows, routing, dp_size, sp_size, dp_index, sp_index)
    own_seg = segment_labels[0]
    label_cols = jnp.broadcast_to(own_seg.astype(jnp.bfloat16)[:, None], (token_rows, HEAD_SIZE))
    kv_local = jnp.concatenate([packed_kv, label_cols], axis=1)
    kv_rel = [kv_local] + [
        lax.ppermute(kv_local, "sp", [(k, k + shift) for k in range(sp_size - shift)])
        for shift in range(1, reach + 1)
    ]
    kv_all = jnp.concatenate(kv_rel, axis=0)
    key_seg = kv_all[:, kv_width].astype(jnp.int32)

    advantage = group_advantage(passes, group_ids)
    bin_adv = lax.dynamic_slice_in_dim(advantage, dp_index * SEGS, SEGS)
    tok_adv = jnp.sum(
        jnp.where(
            own_seg[:, None] == jnp.arange(SEGS, dtype=jnp.int32)[None, :], bin_adv[None, :], 0.0
        ),
        axis=1,
    )
    weighted = (upstream[0].astype(jnp.float32) * tok_adv[:, None]).astype(jnp.bfloat16)

    query_pos = sp_index * token_rows + jnp.arange(token_rows, dtype=jnp.int32)
    rel_block = jnp.arange(seq_len, dtype=jnp.int32) // token_rows
    key_pos = (sp_index - rel_block) * token_rows + jnp.arange(seq_len, dtype=jnp.int32) % token_rows
    allowed = (
        (own_seg[:, None] == key_seg[None, :])
        & (key_pos[None, :] <= query_pos[:, None])
        & (key_pos[None, :] >= 0)
    )
    bias = jnp.where(allowed.T, 0.0, -1e30).astype(jnp.float32)
    groups = KEY_VALUE_HEADS // 2
    query_parts, key_parts, value_parts = [], [], []
    for part in range(2):
        query_grad, total, *outgoing = attend_pallas(
            packed_q, weighted, kv_all, bias, part, groups
        )
        for shift in range(1, reach + 1):
            arrived = lax.ppermute(
                outgoing[shift - 1], "sp", [(k, k - shift) for k in range(shift, sp_size)]
            )
            total = total + arrived.astype(jnp.float32)
        query_parts.append(query_grad)
        key_parts.append(total[:, : groups * HEAD_SIZE])
        value_parts.append(total[:, groups * HEAD_SIZE :])
    query_gradient = jnp.concatenate(query_parts, axis=1).reshape(
        1, token_rows, QUERY_HEADS * HEAD_SIZE
    )
    kv_grads = jnp.concatenate(key_parts + value_parts, axis=1).astype(jnp.bfloat16)
    return (query_gradient, kv_grads.reshape(1, token_rows, kv_width))


def solution(mesh):
    return jax.shard_map(
        step,
        mesh=mesh,
        in_specs=(
            P(("grp", "dp", "sp"), None),
            P("grp"),
            P(("grp", "dp"), "sp"),
            P(("grp", "dp"), "sp", None),
            P("grp"),
            P("grp"),
        ),
        out_specs=(P(("grp", "dp"), "sp", None), P(("grp", "dp"), "sp", None)),
        check_vma=False,
    )
```

```python
import functools
import math

import jax
import jax.numpy as jnp
from jax import lax
from jax.experimental import pallas as pl
from jax.sharding import PartitionSpec as P


QUERY_HEADS = 32
KEY_VALUE_HEADS = 4
HEAD_SIZE = 128
SEGS = 4
GROUP = 8
TESTS = 10


def group_advantage(passes, group_ids):
    reward = passes.astype(jnp.float32) / TESTS
    labels = jnp.arange(group_ids.shape[0] // GROUP, dtype=jnp.int32)
    member = (group_ids[:, None] == labels[None, :]).astype(jnp.float32)
    group_mean = jnp.sum(member * reward[:, None], axis=0) / jnp.sum(member, axis=0)
    return reward - jnp.sum(member * group_mean[None, :], axis=1)


def exchange_rows(rollout_rows, routing, dp_size, sp_size, dp_index, sp_index):
    token_rows = rollout_rows.shape[0]
    capacity = 2 * token_rows // dp_size
    layout_plan = routing.reshape(dp_size, sp_size, token_rows)
    column_plan = lax.dynamic_index_in_dim(layout_plan, sp_index, axis=1, keepdims=False)
    own_plan = lax.dynamic_index_in_dim(column_plan, dp_index, axis=0, keepdims=False)
    targets = jnp.arange(dp_size, dtype=jnp.int32)
    hit_table = (own_plan[:, None] == targets[None, :]).astype(jnp.int32)
    rank_rows = jnp.sum((jnp.cumsum(hit_table, axis=0) - 1) * hit_table, axis=1)
    slots = jnp.arange(dp_size * capacity, dtype=jnp.int32)
    load_table = jnp.sum((column_plan == dp_index).astype(jnp.int32), axis=1)
    end_marks = jnp.cumsum(load_table)
    start_marks = end_marks - load_table
    positions = jnp.arange(token_rows, dtype=jnp.int32)
    source = jnp.sum((positions[:, None] >= end_marks[None, :]).astype(jnp.int32), axis=1)
    chosen_start = jnp.sum(
        jnp.where(source[:, None] == targets[None, :], start_marks[None, :], 0), axis=1
    )

    def send(columns, by_permute):
        target_slot = (own_plan - dp_index) % dp_size if by_permute else own_plan
        send_pick = (slots[:, None] == (target_slot * capacity + rank_rows)[None, :]).astype(
            columns.dtype
        )
        outgoing = jnp.dot(send_pick, columns, preferred_element_type=jnp.float32).astype(
            columns.dtype
        ).reshape(dp_size, capacity, -1)
        if by_permute:
            arrived = jnp.stack(
                [outgoing[0]]
                + [
                    lax.ppermute(
                        outgoing[shift], "dp", [(k, (k + shift) % dp_size) for k in range(dp_size)]
                    )
                    for shift in range(1, dp_size)
                ]
            )
            source_slot = (dp_index - source) % dp_size
        else:
            arrived = lax.all_to_all(outgoing, "dp", split_axis=0, concat_axis=0, tiled=True)
            source_slot = source
        pick_ids = source_slot * capacity + positions - chosen_start
        recv_pick = (pick_ids[:, None] == slots[None, :]).astype(columns.dtype)
        return jnp.dot(
            recv_pick, arrived.reshape(dp_size * capacity, -1), preferred_element_type=jnp.float32
        ).astype(columns.dtype)

    packed_kv = send(rollout_rows[:, QUERY_HEADS * HEAD_SIZE :], True)
    packed_q = send(rollout_rows[:, : QUERY_HEADS * HEAD_SIZE], True)
    return packed_q, packed_kv


def attend_kernel(q_ref, g_ref, kv_ref, m_ref, dq_ref, local_ref, *send_refs, first_group):
    inv_root = 1.0 / math.sqrt(HEAD_SIZE)
    token_rows = q_ref.shape[0]
    groups = local_ref.shape[1] // (2 * HEAD_SIZE)
    query_group = QUERY_HEADS // KEY_VALUE_HEADS
    bias = m_ref[...]
    for local_group in range(groups):
        group = first_group + local_group
        key_mat = kv_ref[:, group * HEAD_SIZE : (group + 1) * HEAD_SIZE]
        value_mat = kv_ref[
            :, (KEY_VALUE_HEADS + group) * HEAD_SIZE : (KEY_VALUE_HEADS + group + 1) * HEAD_SIZE
        ]
        key_sum = jnp.zeros(key_mat.shape, jnp.float32)
        value_sum = jnp.zeros(value_mat.shape, jnp.float32)
        for head in range(query_group):
            cols = slice(
                (local_group * query_group + head) * HEAD_SIZE,
                (local_group * query_group + head + 1) * HEAD_SIZE,
            )
            query_head = q_ref[:, cols]
            grad_head = g_ref[:, cols]
            scores = (
                lax.dot_general(
                    key_mat, query_head, (((1,), (1,)), ((), ())), preferred_element_type=jnp.float32
                )
                * inv_root
                + bias
            )
            row_top = jnp.max(scores, axis=0, keepdims=True)
            scaled_exp = jnp.exp(scores - row_top)
            weights = scaled_exp * (1.0 / jnp.sum(scaled_exp, axis=0, keepdims=True))
            weight_grads = lax.dot_general(
                value_mat, grad_head, (((1,), (1,)), ((), ())), preferred_element_type=jnp.float32
            )
            row_dot = jnp.sum(weights * weight_grads, axis=0, keepdims=True)
            score_grads = (weights * (weight_grads - row_dot) * inv_root).astype(jnp.bfloat16)
            dq_ref[:, cols] = lax.dot_general(
                score_grads, key_mat, (((0,), (0,)), ((), ())), preferred_element_type=jnp.float32
            ).astype(dq_ref.dtype)
            key_sum = key_sum + jnp.dot(score_grads, query_head, preferred_element_type=jnp.float32)
            value_sum = value_sum + jnp.dot(
                weights.astype(jnp.bfloat16), grad_head, preferred_element_type=jnp.float32
            )
        key_cols = slice(local_group * HEAD_SIZE, (local_group + 1) * HEAD_SIZE)
        value_cols = slice((groups + local_group) * HEAD_SIZE, (groups + local_group + 1) * HEAD_SIZE)
        local_ref[:, key_cols] = key_sum[:token_rows]
        local_ref[:, value_cols] = value_sum[:token_rows]
        for back, send_ref in enumerate(send_refs):
            rows = slice((back + 1) * token_rows, (back + 2) * token_rows)
            send_ref[:, key_cols] = key_sum[rows].astype(send_ref.dtype)
            send_ref[:, value_cols] = value_sum[rows].astype(send_ref.dtype)


def attend_pallas(packed, weighted, kv_all, bias, first_group, groups):
    token_rows = packed.shape[0]
    key_rows = kv_all.shape[0]
    reach = key_rows // token_rows - 1
    part_width = groups * (QUERY_HEADS // KEY_VALUE_HEADS) * HEAD_SIZE
    kv_width = 2 * groups * HEAD_SIZE
    heads = groups * (QUERY_HEADS // KEY_VALUE_HEADS)
    flops = 10 * token_rows * key_rows * HEAD_SIZE * heads
    bytes_accessed = 6 * token_rows * part_width + 2 * key_rows * kv_all.shape[1] + 4 * token_rows * key_rows
    whole = lambda i: (0, 0)
    return pl.pallas_call(
        functools.partial(attend_kernel, first_group=first_group),
        grid=(1,),
        in_specs=[
            pl.BlockSpec((token_rows, part_width), lambda i: (0, first_group // groups)),
            pl.BlockSpec((token_rows, part_width), lambda i: (0, first_group // groups)),
            pl.BlockSpec(kv_all.shape, whole),
            pl.BlockSpec(bias.shape, whole),
        ],
        out_specs=[
            pl.BlockSpec((token_rows, part_width), whole)
        ]
        + [pl.BlockSpec((token_rows, kv_width), whole) for _ in range(reach + 1)],
        out_shape=[
            jax.ShapeDtypeStruct((token_rows, part_width), jnp.bfloat16),
            jax.ShapeDtypeStruct((token_rows, kv_width), jnp.float32),
        ]
        + [jax.ShapeDtypeStruct((token_rows, kv_width), jnp.bfloat16) for _ in range(reach)],
        cost_estimate=pl.CostEstimate(
            flops=flops, transcendentals=token_rows * key_rows * heads, bytes_accessed=bytes_accessed
        ),
    )(packed, weighted, kv_all, bias)


def step(rollout_rows, routing, segment_labels, upstream, passes, group_ids):
    dp_size = lax.axis_size("dp")
    sp_size = lax.axis_size("sp")
    dp_index = lax.axis_index("dp")
    sp_index = lax.axis_index("sp")
    token_rows = rollout_rows.shape[0]
    kv_width = 2 * KEY_VALUE_HEADS * HEAD_SIZE
    longest_segment = sp_size * token_rows // 2
    reach = min(sp_size - 1, (longest_segment + token_rows - 2) // token_rows)
    seq_len = (reach + 1) * token_rows

    packed_q, packed_kv = exchange_rows(rollout_rows, routing, dp_size, sp_size, dp_index, sp_index)
    own_seg = segment_labels[0]
    label_cols = jnp.broadcast_to(own_seg.astype(jnp.bfloat16)[:, None], (token_rows, HEAD_SIZE))
    kv_local = jnp.concatenate([packed_kv, label_cols], axis=1)
    kv_rel = [kv_local] + [
        lax.ppermute(kv_local, "sp", [(k, k + shift) for k in range(sp_size - shift)])
        for shift in range(1, reach + 1)
    ]
    kv_all = jnp.concatenate(kv_rel, axis=0)
    key_seg = kv_all[:, kv_width].astype(jnp.int32)

    advantage = group_advantage(passes, group_ids)
    bin_adv = lax.dynamic_slice_in_dim(advantage, dp_index * SEGS, SEGS)
    tok_adv = jnp.sum(
        jnp.where(
            own_seg[:, None] == jnp.arange(SEGS, dtype=jnp.int32)[None, :], bin_adv[None, :], 0.0
        ),
        axis=1,
    )
    weighted = (upstream[0].astype(jnp.float32) * tok_adv[:, None]).astype(jnp.bfloat16)

    query_pos = sp_index * token_rows + jnp.arange(token_rows, dtype=jnp.int32)
    rel_block = jnp.arange(seq_len, dtype=jnp.int32) // token_rows
    key_pos = (sp_index - rel_block) * token_rows + jnp.arange(seq_len, dtype=jnp.int32) % token_rows
    allowed = (
        (own_seg[:, None] == key_seg[None, :])
        & (key_pos[None, :] <= query_pos[:, None])
        & (key_pos[None, :] >= 0)
    )
    bias = jnp.where(allowed.T, 0.0, -1e30).astype(jnp.float32)
    part_groups = (KEY_VALUE_HEADS - KEY_VALUE_HEADS // 4, KEY_VALUE_HEADS // 4)
    query_parts, key_parts, value_parts = [], [], []
    for part, groups in enumerate(part_groups):
        query_grad, total, *outgoing = attend_pallas(packed_q, weighted, kv_all, bias, sum(part_groups[:part]), groups)
        for shift in range(1, reach + 1):
            arrived = lax.ppermute(
                outgoing[shift - 1], "sp", [(k, k - shift) for k in range(shift, sp_size)]
            )
            total = total + arrived.astype(jnp.float32)
        query_parts.append(query_grad)
        key_parts.append(total[:, : groups * HEAD_SIZE])
        value_parts.append(total[:, groups * HEAD_SIZE :])
    query_gradient = jnp.concatenate(query_parts, axis=1).reshape(
        1, token_rows, QUERY_HEADS * HEAD_SIZE
    )
    kv_grads = jnp.concatenate(key_parts + value_parts, axis=1).astype(jnp.bfloat16)
    return (query_gradient, kv_grads.reshape(1, token_rows, kv_width))


def solution(mesh):
    return jax.shard_map(
        step,
        mesh=mesh,
        in_specs=(
            P(("grp", "dp", "sp"), None),
            P("grp"),
            P(("grp", "dp"), "sp"),
            P(("grp", "dp"), "sp", None),
            P("grp"),
            P("grp"),
        ),
        out_specs=(P(("grp", "dp"), "sp", None), P(("grp", "dp"), "sp", None)),
        check_vma=False,
    )
```

```python
import functools
import math

import jax
import jax.numpy as jnp
from jax import lax
from jax.experimental import pallas as pl
from jax.sharding import PartitionSpec as P


QUERY_HEADS = 32
KEY_VALUE_HEADS = 4
HEAD_SIZE = 128
SEGS = 4
GROUP = 8
TESTS = 10


def group_advantage(passes, group_ids):
    reward = passes.astype(jnp.float32) / TESTS
    labels = jnp.arange(group_ids.shape[0] // GROUP, dtype=jnp.int32)
    member = (group_ids[:, None] == labels[None, :]).astype(jnp.float32)
    group_mean = jnp.sum(member * reward[:, None], axis=0) / jnp.sum(member, axis=0)
    return reward - jnp.sum(member * group_mean[None, :], axis=1)


def exchange_rows(rollout_rows, routing, dp_size, sp_size, dp_index, sp_index):
    token_rows = rollout_rows.shape[0]
    capacity = 2 * token_rows // dp_size
    layout_plan = routing.reshape(dp_size, sp_size, token_rows)
    column_plan = lax.dynamic_index_in_dim(layout_plan, sp_index, axis=1, keepdims=False)
    own_plan = lax.dynamic_index_in_dim(column_plan, dp_index, axis=0, keepdims=False)
    targets = jnp.arange(dp_size, dtype=jnp.int32)
    hit_table = (own_plan[:, None] == targets[None, :]).astype(jnp.int32)
    rank_rows = jnp.sum((jnp.cumsum(hit_table, axis=0) - 1) * hit_table, axis=1)
    slots = jnp.arange(dp_size * capacity, dtype=jnp.int32)
    load_table = jnp.sum((column_plan == dp_index).astype(jnp.int32), axis=1)
    end_marks = jnp.cumsum(load_table)
    start_marks = end_marks - load_table
    positions = jnp.arange(token_rows, dtype=jnp.int32)
    source = jnp.sum((positions[:, None] >= end_marks[None, :]).astype(jnp.int32), axis=1)
    chosen_start = jnp.sum(
        jnp.where(source[:, None] == targets[None, :], start_marks[None, :], 0), axis=1
    )

    def send(columns, by_permute):
        target_slot = (own_plan - dp_index) % dp_size if by_permute else own_plan
        send_pick = (slots[:, None] == (target_slot * capacity + rank_rows)[None, :]).astype(
            columns.dtype
        )
        outgoing = jnp.dot(send_pick, columns, preferred_element_type=jnp.float32).astype(
            columns.dtype
        ).reshape(dp_size, capacity, -1)
        if by_permute:
            arrived = jnp.stack(
                [outgoing[0]]
                + [
                    lax.ppermute(
                        outgoing[shift], "dp", [(k, (k + shift) % dp_size) for k in range(dp_size)]
                    )
                    for shift in range(1, dp_size)
                ]
            )
            source_slot = (dp_index - source) % dp_size
        else:
            arrived = lax.all_to_all(outgoing, "dp", split_axis=0, concat_axis=0, tiled=True)
            source_slot = source
        pick_ids = source_slot * capacity + positions - chosen_start
        recv_pick = (pick_ids[:, None] == slots[None, :]).astype(columns.dtype)
        return jnp.dot(
            recv_pick, arrived.reshape(dp_size * capacity, -1), preferred_element_type=jnp.float32
        ).astype(columns.dtype)

    packed_kv = send(rollout_rows[:, QUERY_HEADS * HEAD_SIZE :], True)
    packed_q = send(rollout_rows[:, : QUERY_HEADS * HEAD_SIZE], True)
    return packed_q, packed_kv


def attend_kernel(q_ref, g_ref, kv_ref, m_ref, dq_ref, local_ref, *send_refs, first_group):
    inv_root = 1.0 / math.sqrt(HEAD_SIZE)
    token_rows = q_ref.shape[0]
    groups = local_ref.shape[1] // (2 * HEAD_SIZE)
    query_group = QUERY_HEADS // KEY_VALUE_HEADS
    bias = m_ref[...]
    for local_group in range(groups):
        group = first_group + local_group
        key_mat = kv_ref[:, group * HEAD_SIZE : (group + 1) * HEAD_SIZE]
        value_mat = kv_ref[
            :, (KEY_VALUE_HEADS + group) * HEAD_SIZE : (KEY_VALUE_HEADS + group + 1) * HEAD_SIZE
        ]
        key_sum = jnp.zeros(key_mat.shape, jnp.float32)
        value_sum = jnp.zeros(value_mat.shape, jnp.float32)
        for head in range(query_group):
            cols = slice(
                (local_group * query_group + head) * HEAD_SIZE,
                (local_group * query_group + head + 1) * HEAD_SIZE,
            )
            query_head = q_ref[:, cols]
            grad_head = g_ref[:, cols]
            scores = (
                lax.dot_general(
                    key_mat, query_head, (((1,), (1,)), ((), ())), preferred_element_type=jnp.float32
                )
                * inv_root
                + bias
            )
            row_top = jnp.max(scores, axis=0, keepdims=True)
            scaled_exp = jnp.exp(scores - row_top)
            weights = scaled_exp * (1.0 / jnp.sum(scaled_exp, axis=0, keepdims=True))
            weight_grads = lax.dot_general(
                value_mat, grad_head, (((1,), (1,)), ((), ())), preferred_element_type=jnp.float32
            )
            row_dot = jnp.sum(weights * weight_grads, axis=0, keepdims=True)
            score_grads = (weights * (weight_grads - row_dot) * inv_root).astype(jnp.bfloat16)
            dq_ref[:, cols] = lax.dot_general(
                score_grads, key_mat, (((0,), (0,)), ((), ())), preferred_element_type=jnp.float32
            ).astype(dq_ref.dtype)
            key_sum = key_sum + jnp.dot(score_grads, query_head, preferred_element_type=jnp.float32)
            value_sum = value_sum + jnp.dot(
                weights.astype(jnp.bfloat16), grad_head, preferred_element_type=jnp.float32
            )
        key_cols = slice(local_group * HEAD_SIZE, (local_group + 1) * HEAD_SIZE)
        value_cols = slice((groups + local_group) * HEAD_SIZE, (groups + local_group + 1) * HEAD_SIZE)
        local_ref[:, key_cols] = key_sum[:token_rows]
        local_ref[:, value_cols] = value_sum[:token_rows]
        for back, send_ref in enumerate(send_refs):
            rows = slice((back + 1) * token_rows, (back + 2) * token_rows)
            send_ref[:, key_cols] = key_sum[rows].astype(send_ref.dtype)
            send_ref[:, value_cols] = value_sum[rows].astype(send_ref.dtype)


def attend_pallas(packed, weighted, kv_all, bias, first_group, groups):
    token_rows = packed.shape[0]
    key_rows = kv_all.shape[0]
    reach = key_rows // token_rows - 1
    part_width = groups * (QUERY_HEADS // KEY_VALUE_HEADS) * HEAD_SIZE
    kv_width = 2 * groups * HEAD_SIZE
    heads = groups * (QUERY_HEADS // KEY_VALUE_HEADS)
    flops = 10 * token_rows * key_rows * HEAD_SIZE * heads
    bytes_accessed = 6 * token_rows * part_width + 2 * key_rows * kv_all.shape[1] + 4 * token_rows * key_rows
    whole = lambda i: (0, 0)
    return pl.pallas_call(
        functools.partial(attend_kernel, first_group=first_group),
        grid=(1,),
        in_specs=[
            pl.BlockSpec((token_rows, part_width), lambda i: (0, first_group // groups)),
            pl.BlockSpec((token_rows, part_width), lambda i: (0, first_group // groups)),
            pl.BlockSpec(kv_all.shape, whole),
            pl.BlockSpec(bias.shape, whole),
        ],
        out_specs=[
            pl.BlockSpec((token_rows, part_width), whole)
        ]
        + [pl.BlockSpec((token_rows, kv_width), whole) for _ in range(reach + 1)],
        out_shape=[
            jax.ShapeDtypeStruct((token_rows, part_width), jnp.bfloat16),
            jax.ShapeDtypeStruct((token_rows, kv_width), jnp.float32),
        ]
        + [jax.ShapeDtypeStruct((token_rows, kv_width), jnp.bfloat16) for _ in range(reach)],
        cost_estimate=pl.CostEstimate(
            flops=flops, transcendentals=token_rows * key_rows * heads, bytes_accessed=bytes_accessed
        ),
    )(packed, weighted, kv_all, bias)


def step(rollout_rows, routing, segment_labels, upstream, passes, group_ids):
    dp_size = lax.axis_size("dp")
    sp_size = lax.axis_size("sp")
    dp_index = lax.axis_index("dp")
    sp_index = lax.axis_index("sp")
    token_rows = rollout_rows.shape[0]
    kv_width = 2 * KEY_VALUE_HEADS * HEAD_SIZE
    longest_segment = sp_size * token_rows // 2
    reach = min(sp_size - 1, (longest_segment + token_rows - 2) // token_rows)
    seq_len = (reach + 1) * token_rows

    packed_q, packed_kv = exchange_rows(rollout_rows, routing, dp_size, sp_size, dp_index, sp_index)
    own_seg = segment_labels[0]
    label_cols = jnp.broadcast_to(own_seg.astype(jnp.bfloat16)[:, None], (token_rows, HEAD_SIZE))
    kv_local = jnp.concatenate([packed_kv, label_cols], axis=1)
    kv_rel = [kv_local] + [
        lax.ppermute(kv_local, "sp", [(k, k + shift) for k in range(sp_size - shift)])
        for shift in range(1, reach + 1)
    ]
    kv_all = jnp.concatenate(kv_rel, axis=0)
    key_seg = kv_all[:, kv_width].astype(jnp.int32)

    advantage = group_advantage(passes, group_ids)
    bin_adv = lax.dynamic_slice_in_dim(advantage, dp_index * SEGS, SEGS)
    tok_adv = jnp.sum(
        jnp.where(
            own_seg[:, None] == jnp.arange(SEGS, dtype=jnp.int32)[None, :], bin_adv[None, :], 0.0
        ),
        axis=1,
    )
    weighted = (upstream[0].astype(jnp.float32) * tok_adv[:, None]).astype(jnp.bfloat16)

    query_pos = sp_index * token_rows + jnp.arange(token_rows, dtype=jnp.int32)
    rel_block = jnp.arange(seq_len, dtype=jnp.int32) // token_rows
    key_pos = (sp_index - rel_block) * token_rows + jnp.arange(seq_len, dtype=jnp.int32) % token_rows
    allowed = (
        (own_seg[:, None] == key_seg[None, :])
        & (key_pos[None, :] <= query_pos[:, None])
        & (key_pos[None, :] >= 0)
    )
    bias = jnp.where(allowed.T, 0.0, -1e30).astype(jnp.float32)
    query_grad, own_part, *behind = attend_pallas(
        packed_q, weighted, kv_all, bias, 0, KEY_VALUE_HEADS
    )
    carry = behind[reach - 1].astype(jnp.float32) if reach > 0 else None
    for back in range(reach, 0, -1):
        arrived = lax.ppermute(
            carry.astype(jnp.bfloat16), "sp", [(k, k - 1) for k in range(1, sp_size)]
        )
        own = behind[back - 2].astype(jnp.float32) if back > 1 else own_part
        carry = own + arrived.astype(jnp.float32)
    total = carry if reach > 0 else own_part
    groups = KEY_VALUE_HEADS
    query_parts = [query_grad]
    key_parts = [total[:, : groups * HEAD_SIZE]]
    value_parts = [total[:, groups * HEAD_SIZE :]]
    query_gradient = jnp.concatenate(query_parts, axis=1).reshape(
        1, token_rows, QUERY_HEADS * HEAD_SIZE
    )
    kv_grads = jnp.concatenate(key_parts + value_parts, axis=1).astype(jnp.bfloat16)
    return (query_gradient, kv_grads.reshape(1, token_rows, kv_width))


def solution(mesh):
    return jax.shard_map(
        step,
        mesh=mesh,
        in_specs=(
            P(("grp", "dp", "sp"), None),
            P("grp"),
            P(("grp", "dp"), "sp"),
            P(("grp", "dp"), "sp", None),
            P("grp"),
            P("grp"),
        ),
        out_specs=(P(("grp", "dp"), "sp", None), P(("grp", "dp"), "sp", None)),
        check_vma=False,
    )
```

```python
import functools
import math

import jax
import jax.numpy as jnp
from jax import lax
from jax.experimental import pallas as pl
from jax.experimental.pallas import tpu as pltpu
from jax.sharding import PartitionSpec as P


QUERY_HEADS = 32
KEY_VALUE_HEADS = 4
HEAD_SIZE = 128
SEGS = 4
GROUP = 8
TESTS = 10


def group_advantage(passes, group_ids):
    reward = passes.astype(jnp.float32) / TESTS
    labels = jnp.arange(group_ids.shape[0] // GROUP, dtype=jnp.int32)
    member = (group_ids[:, None] == labels[None, :]).astype(jnp.float32)
    group_mean = jnp.sum(member * reward[:, None], axis=0) / jnp.sum(member, axis=0)
    return reward - jnp.sum(member * group_mean[None, :], axis=1)


def exchange_rows(rollout_rows, routing, dp_size, sp_size, dp_index, sp_index):
    token_rows = rollout_rows.shape[0]
    capacity = 2 * token_rows // dp_size
    layout_plan = routing.reshape(dp_size, sp_size, token_rows)
    column_plan = lax.dynamic_index_in_dim(layout_plan, sp_index, axis=1, keepdims=False)
    own_plan = lax.dynamic_index_in_dim(column_plan, dp_index, axis=0, keepdims=False)
    targets = jnp.arange(dp_size, dtype=jnp.int32)
    hit_table = (own_plan[:, None] == targets[None, :]).astype(jnp.int32)
    rank_rows = jnp.sum((jnp.cumsum(hit_table, axis=0) - 1) * hit_table, axis=1)
    slots = jnp.arange(dp_size * capacity, dtype=jnp.int32)
    load_table = jnp.sum((column_plan == dp_index).astype(jnp.int32), axis=1)
    end_marks = jnp.cumsum(load_table)
    start_marks = end_marks - load_table
    positions = jnp.arange(token_rows, dtype=jnp.int32)
    source = jnp.sum((positions[:, None] >= end_marks[None, :]).astype(jnp.int32), axis=1)
    chosen_start = jnp.sum(
        jnp.where(source[:, None] == targets[None, :], start_marks[None, :], 0), axis=1
    )

    def send(columns, by_permute, select=True):
        target_slot = (own_plan - dp_index) % dp_size if by_permute else own_plan
        send_pick = (slots[:, None] == (target_slot * capacity + rank_rows)[None, :]).astype(
            columns.dtype
        )
        outgoing = jnp.dot(send_pick, columns, preferred_element_type=jnp.float32).astype(
            columns.dtype
        ).reshape(dp_size, capacity, -1)
        if by_permute:
            arrived = [outgoing[0]] + [
                lax.ppermute(
                    outgoing[shift], "dp", [(k, (k + shift) % dp_size) for k in range(dp_size)]
                )
                for shift in range(1, dp_size)
            ]
            source_slot = (dp_index - source) % dp_size
        else:
            arrived = lax.all_to_all(outgoing, "dp", split_axis=0, concat_axis=0, tiled=True)
            source_slot = source
        pick_ids = source_slot * capacity + positions - chosen_start
        recv_pick = (pick_ids[:, None] == slots[None, :]).astype(columns.dtype)
        if not select:
            return list(arrived), recv_pick
        return jnp.dot(
            recv_pick, jnp.concatenate(list(arrived), axis=0), preferred_element_type=jnp.float32
        ).astype(columns.dtype)

    packed_kv = send(rollout_rows[:, QUERY_HEADS * HEAD_SIZE :], True)
    packed_q = send(rollout_rows[:, : QUERY_HEADS * HEAD_SIZE], True, select=False)
    return packed_q, packed_kv


def attend_kernel(*refs, first_group, chunks, reach):
    chunk_refs = refs[:chunks]
    pick_ref, g_ref, kv_ref, m_ref, dq_ref, local_ref = refs[chunks : chunks + 6]
    send_refs = refs[chunks + 6 : chunks + 6 + reach]
    q_ref = refs[chunks + 6 + reach]
    capacity = chunk_refs[0].shape[0]
    picked = jnp.dot(
        pick_ref[:, :capacity], chunk_refs[0][...], preferred_element_type=jnp.float32
    )
    for k in range(1, chunks):
        picked = picked + jnp.dot(
            pick_ref[:, k * capacity : (k + 1) * capacity],
            chunk_refs[k][...],
            preferred_element_type=jnp.float32,
        )
    q_ref[...] = picked.astype(q_ref.dtype)
    inv_root = 1.0 / math.sqrt(HEAD_SIZE)
    token_rows = q_ref.shape[0]
    groups = local_ref.shape[1] // (2 * HEAD_SIZE)
    query_group = QUERY_HEADS // KEY_VALUE_HEADS
    bias = m_ref[...]
    for local_group in range(groups):
        group = first_group + local_group
        key_mat = kv_ref[:, group * HEAD_SIZE : (group + 1) * HEAD_SIZE]
        value_mat = kv_ref[
            :, (KEY_VALUE_HEADS + group) * HEAD_SIZE : (KEY_VALUE_HEADS + group + 1) * HEAD_SIZE
        ]
        key_sum = jnp.zeros(key_mat.shape, jnp.float32)
        value_sum = jnp.zeros(value_mat.shape, jnp.float32)
        for head in range(query_group):
            cols = slice(
                (local_group * query_group + head) * HEAD_SIZE,
                (local_group * query_group + head + 1) * HEAD_SIZE,
            )
            query_head = q_ref[:, cols]
            grad_head = g_ref[:, cols]
            scores = (
                lax.dot_general(
                    key_mat, query_head, (((1,), (1,)), ((), ())), preferred_element_type=jnp.float32
                )
                * inv_root
                + bias
            )
            row_top = jnp.max(scores, axis=0, keepdims=True)
            scaled_exp = jnp.exp(scores - row_top)
            weights = scaled_exp * (1.0 / jnp.sum(scaled_exp, axis=0, keepdims=True))
            weight_grads = lax.dot_general(
                value_mat, grad_head, (((1,), (1,)), ((), ())), preferred_element_type=jnp.float32
            )
            row_dot = jnp.sum(weights * weight_grads, axis=0, keepdims=True)
            score_grads = (weights * (weight_grads - row_dot) * inv_root).astype(jnp.bfloat16)
            dq_ref[:, cols] = lax.dot_general(
                score_grads, key_mat, (((0,), (0,)), ((), ())), preferred_element_type=jnp.float32
            ).astype(dq_ref.dtype)
            key_sum = key_sum + jnp.dot(score_grads, query_head, preferred_element_type=jnp.float32)
            value_sum = value_sum + jnp.dot(
                weights.astype(jnp.bfloat16), grad_head, preferred_element_type=jnp.float32
            )
        key_cols = slice(local_group * HEAD_SIZE, (local_group + 1) * HEAD_SIZE)
        value_cols = slice((groups + local_group) * HEAD_SIZE, (groups + local_group + 1) * HEAD_SIZE)
        local_ref[:, key_cols] = key_sum[:token_rows]
        local_ref[:, value_cols] = value_sum[:token_rows]
        for back, send_ref in enumerate(send_refs):
            rows = slice((back + 1) * token_rows, (back + 2) * token_rows)
            send_ref[:, key_cols] = key_sum[rows].astype(send_ref.dtype)
            send_ref[:, value_cols] = value_sum[rows].astype(send_ref.dtype)


def attend_pallas(q_chunks, q_pick, weighted, kv_all, bias, part, groups):
    token_rows = weighted.shape[0]
    capacity = q_chunks[0].shape[0]
    key_rows = kv_all.shape[0]
    reach = key_rows // token_rows - 1
    part_width = groups * (QUERY_HEADS // KEY_VALUE_HEADS) * HEAD_SIZE
    kv_width = 2 * groups * HEAD_SIZE
    heads = groups * (QUERY_HEADS // KEY_VALUE_HEADS)
    flops = 10 * token_rows * key_rows * HEAD_SIZE * heads
    bytes_accessed = 6 * token_rows * part_width + 2 * key_rows * kv_all.shape[1] + 4 * token_rows * key_rows
    whole = lambda i: (0, 0)
    return pl.pallas_call(
        functools.partial(attend_kernel, first_group=part * groups, chunks=len(q_chunks), reach=reach),
        grid=(1,),
        in_specs=[pl.BlockSpec((capacity, part_width), lambda i: (0, part)) for _ in q_chunks]
        + [
            pl.BlockSpec(q_pick.shape, whole),
            pl.BlockSpec((token_rows, part_width), lambda i: (0, part)),
            pl.BlockSpec(kv_all.shape, whole),
            pl.BlockSpec(bias.shape, whole),
        ],
        out_specs=[
            pl.BlockSpec((token_rows, part_width), whole)
        ]
        + [pl.BlockSpec((token_rows, kv_width), whole) for _ in range(reach + 1)],
        out_shape=[
            jax.ShapeDtypeStruct((token_rows, part_width), jnp.bfloat16),
            jax.ShapeDtypeStruct((token_rows, kv_width), jnp.float32),
        ]
        + [jax.ShapeDtypeStruct((token_rows, kv_width), jnp.bfloat16) for _ in range(reach)],
        cost_estimate=pl.CostEstimate(
            flops=flops, transcendentals=token_rows * key_rows * heads, bytes_accessed=bytes_accessed
        ),
        scratch_shapes=[pltpu.VMEM((token_rows, part_width), jnp.bfloat16)],
    )(*q_chunks, q_pick, weighted, kv_all, bias)


def step(rollout_rows, routing, segment_labels, upstream, passes, group_ids):
    dp_size = lax.axis_size("dp")
    sp_size = lax.axis_size("sp")
    dp_index = lax.axis_index("dp")
    sp_index = lax.axis_index("sp")
    token_rows = rollout_rows.shape[0]
    kv_width = 2 * KEY_VALUE_HEADS * HEAD_SIZE
    longest_segment = sp_size * token_rows // 2
    reach = min(sp_size - 1, (longest_segment + token_rows - 2) // token_rows)
    seq_len = (reach + 1) * token_rows

    packed_q, packed_kv = exchange_rows(rollout_rows, routing, dp_size, sp_size, dp_index, sp_index)
    own_seg = segment_labels[0]
    label_cols = jnp.broadcast_to(own_seg.astype(jnp.bfloat16)[:, None], (token_rows, HEAD_SIZE))
    kv_local = jnp.concatenate([packed_kv, label_cols], axis=1)
    kv_rel = [kv_local] + [
        lax.ppermute(kv_local, "sp", [(k, k + shift) for k in range(sp_size - shift)])
        for shift in range(1, reach + 1)
    ]
    kv_all = jnp.concatenate(kv_rel, axis=0)
    key_seg = kv_all[:, kv_width].astype(jnp.int32)

    advantage = group_advantage(passes, group_ids)
    bin_adv = lax.dynamic_slice_in_dim(advantage, dp_index * SEGS, SEGS)
    tok_adv = jnp.sum(
        jnp.where(
            own_seg[:, None] == jnp.arange(SEGS, dtype=jnp.int32)[None, :], bin_adv[None, :], 0.0
        ),
        axis=1,
    )
    weighted = (upstream[0].astype(jnp.float32) * tok_adv[:, None]).astype(jnp.bfloat16)

    query_pos = sp_index * token_rows + jnp.arange(token_rows, dtype=jnp.int32)
    rel_block = jnp.arange(seq_len, dtype=jnp.int32) // token_rows
    key_pos = (sp_index - rel_block) * token_rows + jnp.arange(seq_len, dtype=jnp.int32) % token_rows
    allowed = (
        (own_seg[:, None] == key_seg[None, :])
        & (key_pos[None, :] <= query_pos[:, None])
        & (key_pos[None, :] >= 0)
    )
    bias = jnp.where(allowed.T, 0.0, -1e30).astype(jnp.float32)
    groups = KEY_VALUE_HEADS // 2
    query_parts, key_parts, value_parts = [], [], []
    for part in range(2):
        query_grad, total, *outgoing = attend_pallas(
            *packed_q, weighted, kv_all, bias, part, groups
        )
        for shift in range(1, reach + 1):
            arrived = lax.ppermute(
                outgoing[shift - 1], "sp", [(k, k - shift) for k in range(shift, sp_size)]
            )
            total = total + arrived.astype(jnp.float32)
        query_parts.append(query_grad)
        key_parts.append(total[:, : groups * HEAD_SIZE])
        value_parts.append(total[:, groups * HEAD_SIZE :])
    query_gradient = jnp.concatenate(query_parts, axis=1).reshape(
        1, token_rows, QUERY_HEADS * HEAD_SIZE
    )
    kv_grads = jnp.concatenate(key_parts + value_parts, axis=1).astype(jnp.bfloat16)
    return (query_gradient, kv_grads.reshape(1, token_rows, kv_width))


def solution(mesh):
    return jax.shard_map(
        step,
        mesh=mesh,
        in_specs=(
            P(("grp", "dp", "sp"), None),
            P("grp"),
            P(("grp", "dp"), "sp"),
            P(("grp", "dp"), "sp", None),
            P("grp"),
            P("grp"),
        ),
        out_specs=(P(("grp", "dp"), "sp", None), P(("grp", "dp"), "sp", None)),
        check_vma=False,
    )
```

```python
import functools
import math

import jax
import jax.numpy as jnp
from jax import lax
from jax.experimental import pallas as pl
from jax.experimental.pallas import tpu as pltpu
from jax.sharding import PartitionSpec as P


QUERY_HEADS = 32
KEY_VALUE_HEADS = 4
HEAD_SIZE = 128
SEGS = 4
GROUP = 8
TESTS = 10
PIPELINE_PARTS = 4


def group_advantage(passes, group_ids):
    reward = passes.astype(jnp.float32) / TESTS
    labels = jnp.arange(group_ids.shape[0] // GROUP, dtype=jnp.int32)
    member = (group_ids[:, None] == labels[None, :]).astype(jnp.float32)
    group_mean = jnp.sum(member * reward[:, None], axis=0) / jnp.sum(member, axis=0)
    return reward - jnp.sum(member * group_mean[None, :], axis=1)


def exchange_rows(rollout_rows, routing, dp_size, sp_size, dp_index, sp_index):
    token_rows = rollout_rows.shape[0]
    capacity = 2 * token_rows // dp_size
    layout_plan = routing.reshape(dp_size, sp_size, token_rows)
    column_plan = lax.dynamic_index_in_dim(layout_plan, sp_index, axis=1, keepdims=False)
    own_plan = lax.dynamic_index_in_dim(column_plan, dp_index, axis=0, keepdims=False)
    targets = jnp.arange(dp_size, dtype=jnp.int32)
    hit_table = (own_plan[:, None] == targets[None, :]).astype(jnp.int32)
    rank_rows = jnp.sum((jnp.cumsum(hit_table, axis=0) - 1) * hit_table, axis=1)
    slots = jnp.arange(dp_size * capacity, dtype=jnp.int32)
    load_table = jnp.sum((column_plan == dp_index).astype(jnp.int32), axis=1)
    end_marks = jnp.cumsum(load_table)
    start_marks = end_marks - load_table
    positions = jnp.arange(token_rows, dtype=jnp.int32)
    source = jnp.sum((positions[:, None] >= end_marks[None, :]).astype(jnp.int32), axis=1)
    chosen_start = jnp.sum(
        jnp.where(source[:, None] == targets[None, :], start_marks[None, :], 0), axis=1
    )

    def send(columns, by_permute, select=True):
        target_slot = (own_plan - dp_index) % dp_size if by_permute else own_plan
        send_pick = (slots[:, None] == (target_slot * capacity + rank_rows)[None, :]).astype(
            columns.dtype
        )
        outgoing = jnp.dot(send_pick, columns, preferred_element_type=jnp.float32).astype(
            columns.dtype
        ).reshape(dp_size, capacity, -1)
        if by_permute:
            arrived = [outgoing[0]] + [
                lax.ppermute(
                    outgoing[shift], "dp", [(k, (k + shift) % dp_size) for k in range(dp_size)]
                )
                for shift in range(1, dp_size)
            ]
            source_slot = (dp_index - source) % dp_size
        else:
            arrived = lax.all_to_all(outgoing, "dp", split_axis=0, concat_axis=0, tiled=True)
            source_slot = source
        pick_ids = source_slot * capacity + positions - chosen_start
        recv_pick = (pick_ids[:, None] == slots[None, :]).astype(columns.dtype)
        if not select:
            return list(arrived), recv_pick
        return jnp.dot(
            recv_pick, jnp.concatenate(list(arrived), axis=0), preferred_element_type=jnp.float32
        ).astype(columns.dtype)

    packed_kv = send(rollout_rows[:, QUERY_HEADS * HEAD_SIZE :], True)
    packed_q = send(rollout_rows[:, : QUERY_HEADS * HEAD_SIZE], True, select=False)
    return packed_q, packed_kv


def attend_kernel(*refs, first_group, chunks, reach):
    chunk_refs = refs[:chunks]
    pick_ref, g_ref, kv_ref, m_ref, dq_ref, local_ref = refs[chunks : chunks + 6]
    send_refs = refs[chunks + 6 : chunks + 6 + reach]
    q_ref = refs[chunks + 6 + reach]
    capacity = chunk_refs[0].shape[0]
    picked = jnp.dot(
        pick_ref[:, :capacity], chunk_refs[0][...], preferred_element_type=jnp.float32
    )
    for k in range(1, chunks):
        picked = picked + jnp.dot(
            pick_ref[:, k * capacity : (k + 1) * capacity],
            chunk_refs[k][...],
            preferred_element_type=jnp.float32,
        )
    q_ref[...] = picked.astype(q_ref.dtype)
    inv_root = 1.0 / math.sqrt(HEAD_SIZE)
    token_rows = q_ref.shape[0]
    groups = local_ref.shape[1] // (2 * HEAD_SIZE)
    query_group = QUERY_HEADS // KEY_VALUE_HEADS
    bias = m_ref[...]
    for local_group in range(groups):
        group = first_group + local_group
        key_mat = kv_ref[:, group * HEAD_SIZE : (group + 1) * HEAD_SIZE]
        value_mat = kv_ref[
            :, (KEY_VALUE_HEADS + group) * HEAD_SIZE : (KEY_VALUE_HEADS + group + 1) * HEAD_SIZE
        ]
        key_sum = jnp.zeros(key_mat.shape, jnp.float32)
        value_sum = jnp.zeros(value_mat.shape, jnp.float32)
        for head in range(query_group):
            cols = slice(
                (local_group * query_group + head) * HEAD_SIZE,
                (local_group * query_group + head + 1) * HEAD_SIZE,
            )
            query_head = q_ref[:, cols]
            grad_head = g_ref[:, cols]
            scores = (
                lax.dot_general(
                    key_mat, query_head, (((1,), (1,)), ((), ())), preferred_element_type=jnp.float32
                )
                * inv_root
                + bias
            )
            row_top = jnp.max(scores, axis=0, keepdims=True)
            scaled_exp = jnp.exp(scores - row_top)
            weights = scaled_exp * (1.0 / jnp.sum(scaled_exp, axis=0, keepdims=True))
            weight_grads = lax.dot_general(
                value_mat, grad_head, (((1,), (1,)), ((), ())), preferred_element_type=jnp.float32
            )
            row_dot = jnp.sum(weights * weight_grads, axis=0, keepdims=True)
            score_grads = (weights * (weight_grads - row_dot) * inv_root).astype(jnp.bfloat16)
            dq_ref[:, cols] = lax.dot_general(
                score_grads, key_mat, (((0,), (0,)), ((), ())), preferred_element_type=jnp.float32
            ).astype(dq_ref.dtype)
            key_sum = key_sum + jnp.dot(score_grads, query_head, preferred_element_type=jnp.float32)
            value_sum = value_sum + jnp.dot(
                weights.astype(jnp.bfloat16), grad_head, preferred_element_type=jnp.float32
            )
        key_cols = slice(local_group * HEAD_SIZE, (local_group + 1) * HEAD_SIZE)
        value_cols = slice((groups + local_group) * HEAD_SIZE, (groups + local_group + 1) * HEAD_SIZE)
        local_ref[:, key_cols] = key_sum[:token_rows]
        local_ref[:, value_cols] = value_sum[:token_rows]
        for back, send_ref in enumerate(send_refs):
            rows = slice((back + 1) * token_rows, (back + 2) * token_rows)
            send_ref[:, key_cols] = key_sum[rows].astype(send_ref.dtype)
            send_ref[:, value_cols] = value_sum[rows].astype(send_ref.dtype)


def attend_pallas(q_chunks, q_pick, weighted, kv_all, bias, part, groups):
    token_rows = weighted.shape[0]
    capacity = q_chunks[0].shape[0]
    key_rows = kv_all.shape[0]
    reach = key_rows // token_rows - 1
    part_width = groups * (QUERY_HEADS // KEY_VALUE_HEADS) * HEAD_SIZE
    kv_width = 2 * groups * HEAD_SIZE
    heads = groups * (QUERY_HEADS // KEY_VALUE_HEADS)
    flops = 10 * token_rows * key_rows * HEAD_SIZE * heads
    bytes_accessed = 6 * token_rows * part_width + 2 * key_rows * kv_all.shape[1] + 4 * token_rows * key_rows
    whole = lambda i: (0, 0)
    return pl.pallas_call(
        functools.partial(attend_kernel, first_group=part * groups, chunks=len(q_chunks), reach=reach),
        grid=(1,),
        in_specs=[pl.BlockSpec((capacity, part_width), lambda i: (0, part)) for _ in q_chunks]
        + [
            pl.BlockSpec(q_pick.shape, whole),
            pl.BlockSpec((token_rows, part_width), lambda i: (0, part)),
            pl.BlockSpec(kv_all.shape, whole),
            pl.BlockSpec(bias.shape, whole),
        ],
        out_specs=[
            pl.BlockSpec((token_rows, part_width), whole)
        ]
        + [pl.BlockSpec((token_rows, kv_width), whole) for _ in range(reach + 1)],
        out_shape=[
            jax.ShapeDtypeStruct((token_rows, part_width), jnp.bfloat16),
            jax.ShapeDtypeStruct((token_rows, kv_width), jnp.float32),
        ]
        + [jax.ShapeDtypeStruct((token_rows, kv_width), jnp.bfloat16) for _ in range(reach)],
        cost_estimate=pl.CostEstimate(
            flops=flops, transcendentals=token_rows * key_rows * heads, bytes_accessed=bytes_accessed
        ),
        scratch_shapes=[pltpu.VMEM((token_rows, part_width), jnp.bfloat16)],
    )(*q_chunks, q_pick, weighted, kv_all, bias)


def step(rollout_rows, routing, segment_labels, upstream, passes, group_ids):
    dp_size = lax.axis_size("dp")
    sp_size = lax.axis_size("sp")
    dp_index = lax.axis_index("dp")
    sp_index = lax.axis_index("sp")
    token_rows = rollout_rows.shape[0]
    kv_width = 2 * KEY_VALUE_HEADS * HEAD_SIZE
    longest_segment = sp_size * token_rows // 2
    reach = min(sp_size - 1, (longest_segment + token_rows - 2) // token_rows)
    seq_len = (reach + 1) * token_rows

    packed_q, packed_kv = exchange_rows(rollout_rows, routing, dp_size, sp_size, dp_index, sp_index)
    own_seg = segment_labels[0]
    label_cols = jnp.broadcast_to(own_seg.astype(jnp.bfloat16)[:, None], (token_rows, HEAD_SIZE))
    kv_local = jnp.concatenate([packed_kv, label_cols], axis=1)
    kv_rel = [kv_local] + [
        lax.ppermute(kv_local, "sp", [(k, k + shift) for k in range(sp_size - shift)])
        for shift in range(1, reach + 1)
    ]
    kv_all = jnp.concatenate(kv_rel, axis=0)
    key_seg = kv_all[:, kv_width].astype(jnp.int32)

    advantage = group_advantage(passes, group_ids)
    bin_adv = lax.dynamic_slice_in_dim(advantage, dp_index * SEGS, SEGS)
    tok_adv = jnp.sum(
        jnp.where(
            own_seg[:, None] == jnp.arange(SEGS, dtype=jnp.int32)[None, :], bin_adv[None, :], 0.0
        ),
        axis=1,
    )
    weighted = (upstream[0].astype(jnp.float32) * tok_adv[:, None]).astype(jnp.bfloat16)

    query_pos = sp_index * token_rows + jnp.arange(token_rows, dtype=jnp.int32)
    rel_block = jnp.arange(seq_len, dtype=jnp.int32) // token_rows
    key_pos = (sp_index - rel_block) * token_rows + jnp.arange(seq_len, dtype=jnp.int32) % token_rows
    allowed = (
        (own_seg[:, None] == key_seg[None, :])
        & (key_pos[None, :] <= query_pos[:, None])
        & (key_pos[None, :] >= 0)
    )
    bias = jnp.where(allowed.T, 0.0, -1e30).astype(jnp.float32)
    groups = KEY_VALUE_HEADS // PIPELINE_PARTS
    query_parts, key_parts, value_parts = [], [], []
    for part in range(PIPELINE_PARTS):
        query_grad, total, *outgoing = attend_pallas(
            *packed_q, weighted, kv_all, bias, part, groups
        )
        for shift in range(1, reach + 1):
            arrived = lax.ppermute(
                outgoing[shift - 1], "sp", [(k, k - shift) for k in range(shift, sp_size)]
            )
            total = total + arrived.astype(jnp.float32)
        query_parts.append(query_grad)
        key_parts.append(total[:, : groups * HEAD_SIZE])
        value_parts.append(total[:, groups * HEAD_SIZE :])
    query_gradient = jnp.concatenate(query_parts, axis=1).reshape(
        1, token_rows, QUERY_HEADS * HEAD_SIZE
    )
    kv_grads = jnp.concatenate(key_parts + value_parts, axis=1).astype(jnp.bfloat16)
    return (query_gradient, kv_grads.reshape(1, token_rows, kv_width))


def solution(mesh):
    return jax.shard_map(
        step,
        mesh=mesh,
        in_specs=(
            P(("grp", "dp", "sp"), None),
            P("grp"),
            P(("grp", "dp"), "sp"),
            P(("grp", "dp"), "sp", None),
            P("grp"),
            P("grp"),
        ),
        out_specs=(P(("grp", "dp"), "sp", None), P(("grp", "dp"), "sp", None)),
        check_vma=False,
    )
```

```python
import functools
import math

import jax
import jax.numpy as jnp
from jax import lax
from jax.experimental import pallas as pl
from jax.experimental.pallas import tpu as pltpu
from jax.sharding import PartitionSpec as P


QUERY_HEADS = 32
KEY_VALUE_HEADS = 4
HEAD_SIZE = 128
SEGS = 4
GROUP = 8
TESTS = 10


def group_advantage(passes, group_ids):
    reward = passes.astype(jnp.float32) / TESTS
    labels = jnp.arange(group_ids.shape[0] // GROUP, dtype=jnp.int32)
    member = (group_ids[:, None] == labels[None, :]).astype(jnp.float32)
    group_mean = jnp.sum(member * reward[:, None], axis=0) / jnp.sum(member, axis=0)
    return reward - jnp.sum(member * group_mean[None, :], axis=1)


def exchange_rows(rollout_rows, routing, dp_size, sp_size, dp_index, sp_index):
    token_rows = rollout_rows.shape[0]
    capacity = 2 * token_rows // dp_size
    layout_plan = routing.reshape(dp_size, sp_size, token_rows)
    column_plan = lax.dynamic_index_in_dim(layout_plan, sp_index, axis=1, keepdims=False)
    own_plan = lax.dynamic_index_in_dim(column_plan, dp_index, axis=0, keepdims=False)
    targets = jnp.arange(dp_size, dtype=jnp.int32)
    hit_table = (own_plan[:, None] == targets[None, :]).astype(jnp.int32)
    rank_rows = jnp.sum((jnp.cumsum(hit_table, axis=0) - 1) * hit_table, axis=1)
    slots = jnp.arange(dp_size * capacity, dtype=jnp.int32)
    load_table = jnp.sum((column_plan == dp_index).astype(jnp.int32), axis=1)
    end_marks = jnp.cumsum(load_table)
    start_marks = end_marks - load_table
    positions = jnp.arange(token_rows, dtype=jnp.int32)
    source = jnp.sum((positions[:, None] >= end_marks[None, :]).astype(jnp.int32), axis=1)
    chosen_start = jnp.sum(
        jnp.where(source[:, None] == targets[None, :], start_marks[None, :], 0), axis=1
    )

    def send(columns, by_permute, select=True):
        target_slot = (own_plan - dp_index) % dp_size if by_permute else own_plan
        send_pick = (slots[:, None] == (target_slot * capacity + rank_rows)[None, :]).astype(
            columns.dtype
        )
        outgoing = jnp.dot(send_pick, columns, preferred_element_type=jnp.float32).astype(
            columns.dtype
        ).reshape(dp_size, capacity, -1)
        if by_permute:
            arrived = [outgoing[0]] + [
                lax.ppermute(
                    outgoing[shift], "dp", [(k, (k + shift) % dp_size) for k in range(dp_size)]
                )
                for shift in range(1, dp_size)
            ]
            source_slot = (dp_index - source) % dp_size
        else:
            arrived = lax.all_to_all(outgoing, "dp", split_axis=0, concat_axis=0, tiled=True)
            source_slot = source
        pick_ids = source_slot * capacity + positions - chosen_start
        recv_pick = (pick_ids[:, None] == slots[None, :]).astype(columns.dtype)
        if not select:
            return list(arrived), recv_pick
        return jnp.dot(
            recv_pick, jnp.concatenate(list(arrived), axis=0), preferred_element_type=jnp.float32
        ).astype(columns.dtype)

    packed_kv = send(rollout_rows[:, QUERY_HEADS * HEAD_SIZE :], True)
    packed_q = send(rollout_rows[:, : QUERY_HEADS * HEAD_SIZE], True, select=False)
    return packed_q, packed_kv


def attend_kernel(*refs, first_group, chunks, reach):
    chunk_refs = refs[:chunks]
    pick_ref, g_ref, kv_ref, m_ref, dq_ref, local_ref = refs[chunks : chunks + 6]
    send_refs = refs[chunks + 6 : chunks + 6 + reach]
    q_ref = refs[chunks + 6 + reach]
    capacity = chunk_refs[0].shape[0]
    picked = jnp.dot(
        pick_ref[:, :capacity], chunk_refs[0][...], preferred_element_type=jnp.float32
    )
    for k in range(1, chunks):
        picked = picked + jnp.dot(
            pick_ref[:, k * capacity : (k + 1) * capacity],
            chunk_refs[k][...],
            preferred_element_type=jnp.float32,
        )
    q_ref[...] = picked.astype(q_ref.dtype)
    inv_root = 1.0 / math.sqrt(HEAD_SIZE)
    token_rows = q_ref.shape[0]
    groups = local_ref.shape[1] // (2 * HEAD_SIZE)
    query_group = QUERY_HEADS // KEY_VALUE_HEADS
    bias = m_ref[...]
    fold = len(send_refs) > 0 and bias.shape[0] == (len(send_refs) + 1) * token_rows
    if fold:
        far = len(send_refs) * token_rows
        lower = (
            lax.broadcasted_iota(jnp.int32, (token_rows, token_rows), 0)
            <= lax.broadcasted_iota(jnp.int32, (token_rows, token_rows), 1)
        )

        def folded(full):
            return jnp.concatenate(
                [jnp.where(lower, full[:token_rows], full[far:]), full[token_rows:far]], axis=0
            )

        def unfolded(part):
            zero = jnp.zeros_like(part[:token_rows])
            return jnp.concatenate(
                [
                    jnp.where(lower, part[:token_rows], zero),
                    part[token_rows:],
                    jnp.where(lower, zero, part[:token_rows]),
                ],
                axis=0,
            )

        bias = folded(bias)
    else:
        folded = unfolded = lambda x: x
    for local_group in range(groups):
        group = first_group + local_group
        key_mat = kv_ref[:, group * HEAD_SIZE : (group + 1) * HEAD_SIZE]
        value_mat = kv_ref[
            :, (KEY_VALUE_HEADS + group) * HEAD_SIZE : (KEY_VALUE_HEADS + group + 1) * HEAD_SIZE
        ]
        key_sum = jnp.zeros(key_mat.shape, jnp.float32)
        value_sum = jnp.zeros(value_mat.shape, jnp.float32)
        for head in range(query_group):
            cols = slice(
                (local_group * query_group + head) * HEAD_SIZE,
                (local_group * query_group + head + 1) * HEAD_SIZE,
            )
            query_head = q_ref[:, cols]
            grad_head = g_ref[:, cols]
            scores = (
                folded(
                    lax.dot_general(
                        key_mat, query_head, (((1,), (1,)), ((), ())), preferred_element_type=jnp.float32
                    )
                )
                * inv_root
                + bias
            )
            row_top = jnp.max(scores, axis=0, keepdims=True)
            scaled_exp = jnp.exp(scores - row_top)
            weights = scaled_exp * (1.0 / jnp.sum(scaled_exp, axis=0, keepdims=True))
            weight_grads = folded(
                lax.dot_general(
                    value_mat, grad_head, (((1,), (1,)), ((), ())), preferred_element_type=jnp.float32
                )
            )
            row_dot = jnp.sum(weights * weight_grads, axis=0, keepdims=True)
            score_grads = unfolded(
                (weights * (weight_grads - row_dot) * inv_root).astype(jnp.bfloat16)
            )
            weights_low = unfolded(weights.astype(jnp.bfloat16))
            dq_ref[:, cols] = lax.dot_general(
                score_grads, key_mat, (((0,), (0,)), ((), ())), preferred_element_type=jnp.float32
            ).astype(dq_ref.dtype)
            key_sum = key_sum + jnp.dot(score_grads, query_head, preferred_element_type=jnp.float32)
            value_sum = value_sum + jnp.dot(weights_low, grad_head, preferred_element_type=jnp.float32)
        key_cols = slice(local_group * HEAD_SIZE, (local_group + 1) * HEAD_SIZE)
        value_cols = slice((groups + local_group) * HEAD_SIZE, (groups + local_group + 1) * HEAD_SIZE)
        local_ref[:, key_cols] = key_sum[:token_rows]
        local_ref[:, value_cols] = value_sum[:token_rows]
        for back, send_ref in enumerate(send_refs):
            rows = slice((back + 1) * token_rows, (back + 2) * token_rows)
            send_ref[:, key_cols] = key_sum[rows].astype(send_ref.dtype)
            send_ref[:, value_cols] = value_sum[rows].astype(send_ref.dtype)


def attend_pallas(q_chunks, q_pick, weighted, kv_all, bias, part, groups):
    token_rows = weighted.shape[0]
    capacity = q_chunks[0].shape[0]
    key_rows = kv_all.shape[0]
    reach = key_rows // token_rows - 1
    part_width = groups * (QUERY_HEADS // KEY_VALUE_HEADS) * HEAD_SIZE
    kv_width = 2 * groups * HEAD_SIZE
    heads = groups * (QUERY_HEADS // KEY_VALUE_HEADS)
    flops = 10 * token_rows * key_rows * HEAD_SIZE * heads
    bytes_accessed = 6 * token_rows * part_width + 2 * key_rows * kv_all.shape[1] + 4 * token_rows * key_rows
    whole = lambda i: (0, 0)
    return pl.pallas_call(
        functools.partial(attend_kernel, first_group=part * groups, chunks=len(q_chunks), reach=reach),
        grid=(1,),
        in_specs=[pl.BlockSpec((capacity, part_width), lambda i: (0, part)) for _ in q_chunks]
        + [
            pl.BlockSpec(q_pick.shape, whole),
            pl.BlockSpec((token_rows, part_width), lambda i: (0, part)),
            pl.BlockSpec(kv_all.shape, whole),
            pl.BlockSpec(bias.shape, whole),
        ],
        out_specs=[
            pl.BlockSpec((token_rows, part_width), whole)
        ]
        + [pl.BlockSpec((token_rows, kv_width), whole) for _ in range(reach + 1)],
        out_shape=[
            jax.ShapeDtypeStruct((token_rows, part_width), jnp.bfloat16),
            jax.ShapeDtypeStruct((token_rows, kv_width), jnp.float32),
        ]
        + [jax.ShapeDtypeStruct((token_rows, kv_width), jnp.bfloat16) for _ in range(reach)],
        cost_estimate=pl.CostEstimate(
            flops=flops, transcendentals=token_rows * key_rows * heads, bytes_accessed=bytes_accessed
        ),
        scratch_shapes=[pltpu.VMEM((token_rows, part_width), jnp.bfloat16)],
    )(*q_chunks, q_pick, weighted, kv_all, bias)


def step(rollout_rows, routing, segment_labels, upstream, passes, group_ids):
    dp_size = lax.axis_size("dp")
    sp_size = lax.axis_size("sp")
    dp_index = lax.axis_index("dp")
    sp_index = lax.axis_index("sp")
    token_rows = rollout_rows.shape[0]
    kv_width = 2 * KEY_VALUE_HEADS * HEAD_SIZE
    longest_segment = sp_size * token_rows // 2
    reach = min(sp_size - 1, (longest_segment + token_rows - 2) // token_rows)
    seq_len = (reach + 1) * token_rows

    packed_q, packed_kv = exchange_rows(rollout_rows, routing, dp_size, sp_size, dp_index, sp_index)
    own_seg = segment_labels[0]
    label_cols = jnp.broadcast_to(own_seg.astype(jnp.bfloat16)[:, None], (token_rows, HEAD_SIZE))
    kv_local = jnp.concatenate([packed_kv, label_cols], axis=1)
    kv_rel = [kv_local] + [
        lax.ppermute(kv_local, "sp", [(k, k + shift) for k in range(sp_size - shift)])
        for shift in range(1, reach + 1)
    ]
    kv_all = jnp.concatenate(kv_rel, axis=0)
    key_seg = kv_all[:, kv_width].astype(jnp.int32)

    advantage = group_advantage(passes, group_ids)
    bin_adv = lax.dynamic_slice_in_dim(advantage, dp_index * SEGS, SEGS)
    tok_adv = jnp.sum(
        jnp.where(
            own_seg[:, None] == jnp.arange(SEGS, dtype=jnp.int32)[None, :], bin_adv[None, :], 0.0
        ),
        axis=1,
    )
    weighted = (upstream[0].astype(jnp.float32) * tok_adv[:, None]).astype(jnp.bfloat16)

    query_pos = sp_index * token_rows + jnp.arange(token_rows, dtype=jnp.int32)
    rel_block = jnp.arange(seq_len, dtype=jnp.int32) // token_rows
    key_pos = (sp_index - rel_block) * token_rows + jnp.arange(seq_len, dtype=jnp.int32) % token_rows
    allowed = (
        (own_seg[:, None] == key_seg[None, :])
        & (key_pos[None, :] <= query_pos[:, None])
        & (key_pos[None, :] >= 0)
    )
    bias = jnp.where(allowed.T, 0.0, -1e30).astype(jnp.float32)
    groups = KEY_VALUE_HEADS // 2
    query_parts, key_parts, value_parts = [], [], []
    for part in range(2):
        query_grad, total, *outgoing = attend_pallas(
            *packed_q, weighted, kv_all, bias, part, groups
        )
        for shift in range(1, reach + 1):
            arrived = lax.ppermute(
                outgoing[shift - 1], "sp", [(k, k - shift) for k in range(shift, sp_size)]
            )
            total = total + arrived.astype(jnp.float32)
        query_parts.append(query_grad)
        key_parts.append(total[:, : groups * HEAD_SIZE])
        value_parts.append(total[:, groups * HEAD_SIZE :])
    query_gradient = jnp.concatenate(query_parts, axis=1).reshape(
        1, token_rows, QUERY_HEADS * HEAD_SIZE
    )
    kv_grads = jnp.concatenate(key_parts + value_parts, axis=1).astype(jnp.bfloat16)
    return (query_gradient, kv_grads.reshape(1, token_rows, kv_width))


def solution(mesh):
    return jax.shard_map(
        step,
        mesh=mesh,
        in_specs=(
            P(("grp", "dp", "sp"), None),
            P("grp"),
            P(("grp", "dp"), "sp"),
            P(("grp", "dp"), "sp", None),
            P("grp"),
            P("grp"),
        ),
        out_specs=(P(("grp", "dp"), "sp", None), P(("grp", "dp"), "sp", None)),
        check_vma=False,
    )
```

```python
import functools
import math

import jax
import jax.numpy as jnp
from jax import lax
from jax.experimental import pallas as pl
from jax.experimental.pallas import tpu as pltpu
from jax.sharding import PartitionSpec as P


QUERY_HEADS = 32
KEY_VALUE_HEADS = 4
HEAD_SIZE = 128
SEGS = 4
GROUP = 8
TESTS = 10


def group_advantage(passes, group_ids):
    reward = passes.astype(jnp.float32) / TESTS
    labels = jnp.arange(group_ids.shape[0] // GROUP, dtype=jnp.int32)
    member = (group_ids[:, None] == labels[None, :]).astype(jnp.float32)
    group_mean = jnp.sum(member * reward[:, None], axis=0) / jnp.sum(member, axis=0)
    return reward - jnp.sum(member * group_mean[None, :], axis=1)


def exchange_rows(rollout_rows, routing, dp_size, sp_size, dp_index, sp_index):
    token_rows = rollout_rows.shape[0]
    capacity = 2 * token_rows // dp_size
    layout_plan = routing.reshape(dp_size, sp_size, token_rows)
    column_plan = lax.dynamic_index_in_dim(layout_plan, sp_index, axis=1, keepdims=False)
    own_plan = lax.dynamic_index_in_dim(column_plan, dp_index, axis=0, keepdims=False)
    targets = jnp.arange(dp_size, dtype=jnp.int32)
    hit_table = (own_plan[:, None] == targets[None, :]).astype(jnp.int32)
    rank_rows = jnp.sum((jnp.cumsum(hit_table, axis=0) - 1) * hit_table, axis=1)
    slots = jnp.arange(dp_size * capacity, dtype=jnp.int32)
    load_table = jnp.sum((column_plan == dp_index).astype(jnp.int32), axis=1)
    end_marks = jnp.cumsum(load_table)
    start_marks = end_marks - load_table
    positions = jnp.arange(token_rows, dtype=jnp.int32)
    source = jnp.sum((positions[:, None] >= end_marks[None, :]).astype(jnp.int32), axis=1)
    chosen_start = jnp.sum(
        jnp.where(source[:, None] == targets[None, :], start_marks[None, :], 0), axis=1
    )

    def send(columns, by_permute, select=True):
        target_slot = (own_plan - dp_index) % dp_size if by_permute else own_plan
        send_pick = (slots[:, None] == (target_slot * capacity + rank_rows)[None, :]).astype(
            columns.dtype
        )
        outgoing = jnp.dot(send_pick, columns, preferred_element_type=jnp.float32).astype(
            columns.dtype
        ).reshape(dp_size, capacity, -1)
        if by_permute:
            arrived = [outgoing[0]] + [
                lax.ppermute(
                    outgoing[shift], "dp", [(k, (k + shift) % dp_size) for k in range(dp_size)]
                )
                for shift in range(1, dp_size)
            ]
            source_slot = (dp_index - source) % dp_size
        else:
            arrived = lax.all_to_all(outgoing, "dp", split_axis=0, concat_axis=0, tiled=True)
            source_slot = source
        pick_ids = source_slot * capacity + positions - chosen_start
        recv_pick = (pick_ids[:, None] == slots[None, :]).astype(columns.dtype)
        if not select:
            return list(arrived), recv_pick
        return jnp.dot(
            recv_pick, jnp.concatenate(list(arrived), axis=0), preferred_element_type=jnp.float32
        ).astype(columns.dtype)

    packed_kv = send(rollout_rows[:, QUERY_HEADS * HEAD_SIZE :], True)
    packed_q = send(rollout_rows[:, : QUERY_HEADS * HEAD_SIZE], True, select=False)
    return packed_q, packed_kv


def attend_kernel(*refs, first_group, chunks, reach, fold):
    chunk_refs = refs[:chunks]
    pick_ref, g_ref, kv_ref, key_info, query_info, dq_ref, local_ref = refs[chunks : chunks + 7]
    send_refs = refs[chunks + 7 : chunks + 7 + reach]
    q_ref = refs[chunks + 7 + reach]
    capacity = chunk_refs[0].shape[0]
    picked = jnp.dot(
        pick_ref[:, :capacity], chunk_refs[0][...], preferred_element_type=jnp.float32
    )
    for k in range(1, chunks):
        picked = picked + jnp.dot(
            pick_ref[:, k * capacity : (k + 1) * capacity],
            chunk_refs[k][...],
            preferred_element_type=jnp.float32,
        )
    q_ref[...] = picked.astype(q_ref.dtype)
    inv_root = 1.0 / math.sqrt(HEAD_SIZE)
    token_rows = q_ref.shape[0]
    groups = local_ref.shape[1] // (2 * HEAD_SIZE)
    query_group = QUERY_HEADS // KEY_VALUE_HEADS
    key_seg = key_info[:, 0:1]
    key_pos = key_info[:, 1:2]
    allowed = (
        (key_seg == query_info[0:1, :]) & (key_pos <= query_info[1:2, :]) & (key_pos >= 0.0)
    )
    bias = jnp.where(allowed, 0.0, -1e30).astype(jnp.float32)
    if fold:
        far = len(send_refs) * token_rows
        lower = (
            lax.broadcasted_iota(jnp.int32, (token_rows, token_rows), 0)
            <= lax.broadcasted_iota(jnp.int32, (token_rows, token_rows), 1)
        )

        def folded(full):
            return jnp.concatenate(
                [jnp.where(lower, full[:token_rows], full[far:]), full[token_rows:far]], axis=0
            )

        def unfolded(part):
            zero = jnp.zeros_like(part[:token_rows])
            return jnp.concatenate(
                [
                    jnp.where(lower, part[:token_rows], zero),
                    part[token_rows:],
                    jnp.where(lower, zero, part[:token_rows]),
                ],
                axis=0,
            )

        bias = folded(bias)
    else:
        folded = unfolded = lambda x: x
    for local_group in range(groups):
        group = first_group + local_group
        key_mat = kv_ref[:, group * HEAD_SIZE : (group + 1) * HEAD_SIZE]
        value_mat = kv_ref[
            :, (KEY_VALUE_HEADS + group) * HEAD_SIZE : (KEY_VALUE_HEADS + group + 1) * HEAD_SIZE
        ]
        key_sum = jnp.zeros(key_mat.shape, jnp.float32)
        value_sum = jnp.zeros(value_mat.shape, jnp.float32)
        for head in range(query_group):
            cols = slice(
                (local_group * query_group + head) * HEAD_SIZE,
                (local_group * query_group + head + 1) * HEAD_SIZE,
            )
            query_head = q_ref[:, cols]
            grad_head = g_ref[:, cols]
            scores = (
                folded(
                    lax.dot_general(
                        key_mat, query_head, (((1,), (1,)), ((), ())), preferred_element_type=jnp.float32
                    )
                )
                * inv_root
                + bias
            )
            row_top = jnp.max(scores, axis=0, keepdims=True)
            scaled_exp = jnp.exp(scores - row_top)
            weights = scaled_exp * (1.0 / jnp.sum(scaled_exp, axis=0, keepdims=True))
            weight_grads = folded(
                lax.dot_general(
                    value_mat, grad_head, (((1,), (1,)), ((), ())), preferred_element_type=jnp.float32
                )
            )
            row_dot = jnp.sum(weights * weight_grads, axis=0, keepdims=True)
            score_grads = unfolded(
                (weights * (weight_grads - row_dot) * inv_root).astype(jnp.bfloat16)
            )
            weights_low = unfolded(weights.astype(jnp.bfloat16))
            dq_ref[:, cols] = lax.dot_general(
                score_grads, key_mat, (((0,), (0,)), ((), ())), preferred_element_type=jnp.float32
            ).astype(dq_ref.dtype)
            key_sum = key_sum + jnp.dot(score_grads, query_head, preferred_element_type=jnp.float32)
            value_sum = value_sum + jnp.dot(weights_low, grad_head, preferred_element_type=jnp.float32)
        key_cols = slice(local_group * HEAD_SIZE, (local_group + 1) * HEAD_SIZE)
        value_cols = slice((groups + local_group) * HEAD_SIZE, (groups + local_group + 1) * HEAD_SIZE)
        local_ref[:, key_cols] = key_sum[:token_rows]
        local_ref[:, value_cols] = value_sum[:token_rows]
        for back, send_ref in enumerate(send_refs):
            rows = slice((back + 1) * token_rows, (back + 2) * token_rows)
            send_ref[:, key_cols] = key_sum[rows].astype(send_ref.dtype)
            send_ref[:, value_cols] = value_sum[rows].astype(send_ref.dtype)


def attend_pallas(q_chunks, q_pick, weighted, kv_all, key_info, query_info, part, groups, fold):
    token_rows = weighted.shape[0]
    capacity = q_chunks[0].shape[0]
    key_rows = kv_all.shape[0]
    reach = key_rows // token_rows - 1
    part_width = groups * (QUERY_HEADS // KEY_VALUE_HEADS) * HEAD_SIZE
    kv_width = 2 * groups * HEAD_SIZE
    heads = groups * (QUERY_HEADS // KEY_VALUE_HEADS)
    flops = 10 * token_rows * key_rows * HEAD_SIZE * heads
    bytes_accessed = 6 * token_rows * part_width + 2 * key_rows * kv_all.shape[1] + 8 * (token_rows + key_rows)
    whole = lambda i: (0, 0)
    return pl.pallas_call(
        functools.partial(
            attend_kernel, first_group=part * groups, chunks=len(q_chunks), reach=reach, fold=fold
        ),
        grid=(1,),
        in_specs=[pl.BlockSpec((capacity, part_width), lambda i: (0, part)) for _ in q_chunks]
        + [
            pl.BlockSpec(q_pick.shape, whole),
            pl.BlockSpec((token_rows, part_width), lambda i: (0, part)),
            pl.BlockSpec(kv_all.shape, whole),
            pl.BlockSpec(key_info.shape, whole),
            pl.BlockSpec(query_info.shape, whole),
        ],
        out_specs=[
            pl.BlockSpec((token_rows, part_width), whole)
        ]
        + [pl.BlockSpec((token_rows, kv_width), whole) for _ in range(reach + 1)],
        out_shape=[
            jax.ShapeDtypeStruct((token_rows, part_width), jnp.bfloat16),
            jax.ShapeDtypeStruct((token_rows, kv_width), jnp.float32),
        ]
        + [jax.ShapeDtypeStruct((token_rows, kv_width), jnp.bfloat16) for _ in range(reach)],
        cost_estimate=pl.CostEstimate(
            flops=flops, transcendentals=token_rows * key_rows * heads, bytes_accessed=bytes_accessed
        ),
        scratch_shapes=[pltpu.VMEM((token_rows, part_width), jnp.bfloat16)],
    )(*q_chunks, q_pick, weighted, kv_all, key_info, query_info)


def step(rollout_rows, routing, segment_labels, upstream, passes, group_ids):
    dp_size = lax.axis_size("dp")
    sp_size = lax.axis_size("sp")
    dp_index = lax.axis_index("dp")
    sp_index = lax.axis_index("sp")
    token_rows = rollout_rows.shape[0]
    kv_width = 2 * KEY_VALUE_HEADS * HEAD_SIZE
    longest_segment = sp_size * token_rows // 2
    reach = min(sp_size - 1, (longest_segment + token_rows - 2) // token_rows)
    seq_len = (reach + 1) * token_rows
    fold = reach > 0 and longest_segment == reach * token_rows

    packed_q, packed_kv = exchange_rows(rollout_rows, routing, dp_size, sp_size, dp_index, sp_index)
    own_seg = segment_labels[0]
    label_cols = jnp.broadcast_to(own_seg.astype(jnp.bfloat16)[:, None], (token_rows, HEAD_SIZE))
    kv_local = jnp.concatenate([packed_kv, label_cols], axis=1)
    kv_rel = [kv_local] + [
        lax.ppermute(kv_local, "sp", [(k, k + shift) for k in range(sp_size - shift)])
        for shift in range(1, reach + 1)
    ]
    kv_all = jnp.concatenate(kv_rel, axis=0)
    key_seg = kv_all[:, kv_width].astype(jnp.int32)

    advantage = group_advantage(passes, group_ids)
    bin_adv = lax.dynamic_slice_in_dim(advantage, dp_index * SEGS, SEGS)
    tok_adv = jnp.sum(
        jnp.where(
            own_seg[:, None] == jnp.arange(SEGS, dtype=jnp.int32)[None, :], bin_adv[None, :], 0.0
        ),
        axis=1,
    )
    weighted = (upstream[0].astype(jnp.float32) * tok_adv[:, None]).astype(jnp.bfloat16)

    query_pos = sp_index * token_rows + jnp.arange(token_rows, dtype=jnp.int32)
    rel_block = jnp.arange(seq_len, dtype=jnp.int32) // token_rows
    key_pos = (sp_index - rel_block) * token_rows + jnp.arange(seq_len, dtype=jnp.int32) % token_rows
    key_info = jnp.stack([key_seg, key_pos], axis=1).astype(jnp.float32)
    query_info = jnp.stack([own_seg, query_pos], axis=0).astype(jnp.float32)
    groups = KEY_VALUE_HEADS // 2
    query_parts, key_parts, value_parts = [], [], []
    for part in range(2):
        query_grad, total, *outgoing = attend_pallas(
            *packed_q, weighted, kv_all, key_info, query_info, part, groups, fold
        )
        for shift in range(1, reach + 1):
            arrived = lax.ppermute(
                outgoing[shift - 1], "sp", [(k, k - shift) for k in range(shift, sp_size)]
            )
            total = total + arrived.astype(jnp.float32)
        query_parts.append(query_grad)
        key_parts.append(total[:, : groups * HEAD_SIZE])
        value_parts.append(total[:, groups * HEAD_SIZE :])
    query_gradient = jnp.concatenate(query_parts, axis=1).reshape(
        1, token_rows, QUERY_HEADS * HEAD_SIZE
    )
    kv_grads = jnp.concatenate(key_parts + value_parts, axis=1).astype(jnp.bfloat16)
    return (query_gradient, kv_grads.reshape(1, token_rows, kv_width))


def solution(mesh):
    return jax.shard_map(
        step,
        mesh=mesh,
        in_specs=(
            P(("grp", "dp", "sp"), None),
            P("grp"),
            P(("grp", "dp"), "sp"),
            P(("grp", "dp"), "sp", None),
            P("grp"),
            P("grp"),
        ),
        out_specs=(P(("grp", "dp"), "sp", None), P(("grp", "dp"), "sp", None)),
        check_vma=False,
    )
```

```python
import functools
import math

import jax
import jax.numpy as jnp
from jax import lax
from jax.experimental import pallas as pl
from jax.experimental.pallas import tpu as pltpu
from jax.sharding import PartitionSpec as P


QUERY_HEADS = 32
KEY_VALUE_HEADS = 4
HEAD_SIZE = 128
SEGS = 4
GROUP = 8
TESTS = 10


def group_advantage(passes, group_ids):
    reward = passes.astype(jnp.float32) / TESTS
    labels = jnp.arange(group_ids.shape[0] // GROUP, dtype=jnp.int32)
    member = (group_ids[:, None] == labels[None, :]).astype(jnp.float32)
    group_mean = jnp.sum(member * reward[:, None], axis=0) / jnp.sum(member, axis=0)
    return reward - jnp.sum(member * group_mean[None, :], axis=1)


def exchange_rows(rollout_rows, routing, dp_size, sp_size, dp_index, sp_index):
    token_rows = rollout_rows.shape[0]
    capacity = 2 * token_rows // dp_size
    layout_plan = routing.reshape(dp_size, sp_size, token_rows)
    column_plan = lax.dynamic_index_in_dim(layout_plan, sp_index, axis=1, keepdims=False)
    own_plan = lax.dynamic_index_in_dim(column_plan, dp_index, axis=0, keepdims=False)
    targets = jnp.arange(dp_size, dtype=jnp.int32)
    hit_table = (own_plan[:, None] == targets[None, :]).astype(jnp.int32)
    rank_rows = jnp.sum((jnp.cumsum(hit_table, axis=0) - 1) * hit_table, axis=1)
    slots = jnp.arange(dp_size * capacity, dtype=jnp.int32)
    load_table = jnp.sum((column_plan == dp_index).astype(jnp.int32), axis=1)
    end_marks = jnp.cumsum(load_table)
    start_marks = end_marks - load_table
    positions = jnp.arange(token_rows, dtype=jnp.int32)
    source = jnp.sum((positions[:, None] >= end_marks[None, :]).astype(jnp.int32), axis=1)
    chosen_start = jnp.sum(
        jnp.where(source[:, None] == targets[None, :], start_marks[None, :], 0), axis=1
    )

    def send(columns, by_permute, select=True):
        target_slot = (own_plan - dp_index) % dp_size if by_permute else own_plan
        send_pick = (slots[:, None] == (target_slot * capacity + rank_rows)[None, :]).astype(
            columns.dtype
        )
        outgoing = jnp.dot(send_pick, columns, preferred_element_type=jnp.float32).astype(
            columns.dtype
        ).reshape(dp_size, capacity, -1)
        if by_permute:
            arrived = [outgoing[0]] + [
                lax.ppermute(
                    outgoing[shift], "dp", [(k, (k + shift) % dp_size) for k in range(dp_size)]
                )
                for shift in range(1, dp_size)
            ]
            source_slot = (dp_index - source) % dp_size
        else:
            arrived = lax.all_to_all(outgoing, "dp", split_axis=0, concat_axis=0, tiled=True)
            source_slot = source
        pick_ids = source_slot * capacity + positions - chosen_start
        recv_pick = (pick_ids[:, None] == slots[None, :]).astype(columns.dtype)
        if not select:
            return list(arrived), recv_pick
        return jnp.dot(
            recv_pick, jnp.concatenate(list(arrived), axis=0), preferred_element_type=jnp.float32
        ).astype(columns.dtype)

    packed_kv = send(rollout_rows[:, QUERY_HEADS * HEAD_SIZE :], True)
    packed_q = send(rollout_rows[:, : QUERY_HEADS * HEAD_SIZE], True, select=False)
    return packed_q, packed_kv


def attend_kernel(*refs, first_group, chunks, reach, fold):
    chunk_refs = refs[:chunks]
    pick_ref, g_ref, kv_ref, m_ref, dq_ref, local_ref = refs[chunks : chunks + 6]
    send_refs = refs[chunks + 6 : chunks + 6 + reach]
    q_ref = refs[chunks + 6 + reach]
    capacity = chunk_refs[0].shape[0]
    picked = jnp.dot(
        pick_ref[:, :capacity], chunk_refs[0][...], preferred_element_type=jnp.float32
    )
    for k in range(1, chunks):
        picked = picked + jnp.dot(
            pick_ref[:, k * capacity : (k + 1) * capacity],
            chunk_refs[k][...],
            preferred_element_type=jnp.float32,
        )
    q_ref[...] = picked.astype(q_ref.dtype)
    inv_root = 1.0 / math.sqrt(HEAD_SIZE)
    token_rows = q_ref.shape[0]
    groups = local_ref.shape[1] // (2 * HEAD_SIZE)
    query_group = QUERY_HEADS // KEY_VALUE_HEADS
    bias = m_ref[...]
    if fold:
        far = len(send_refs) * token_rows
        lower = (
            lax.broadcasted_iota(jnp.int32, (token_rows, token_rows), 0)
            <= lax.broadcasted_iota(jnp.int32, (token_rows, token_rows), 1)
        )

        def folded(full):
            return jnp.concatenate(
                [jnp.where(lower, full[:token_rows], full[far:]), full[token_rows:far]], axis=0
            )

        def unfolded(part):
            zero = jnp.zeros_like(part[:token_rows])
            return jnp.concatenate(
                [
                    jnp.where(lower, part[:token_rows], zero),
                    part[token_rows:],
                    jnp.where(lower, zero, part[:token_rows]),
                ],
                axis=0,
            )

        bias = folded(bias)
    else:
        folded = unfolded = lambda x: x
    for local_group in range(groups):
        group = first_group + local_group
        key_mat = kv_ref[:, group * HEAD_SIZE : (group + 1) * HEAD_SIZE]
        value_mat = kv_ref[
            :, (KEY_VALUE_HEADS + group) * HEAD_SIZE : (KEY_VALUE_HEADS + group + 1) * HEAD_SIZE
        ]
        key_sum = jnp.zeros(key_mat.shape, jnp.float32)
        value_sum = jnp.zeros(value_mat.shape, jnp.float32)
        for head in range(query_group):
            cols = slice(
                (local_group * query_group + head) * HEAD_SIZE,
                (local_group * query_group + head + 1) * HEAD_SIZE,
            )
            query_head = q_ref[:, cols]
            grad_head = g_ref[:, cols]
            scores = (
                folded(
                    lax.dot_general(
                        key_mat, query_head, (((1,), (1,)), ((), ())), preferred_element_type=jnp.float32
                    )
                )
                * inv_root
                + bias
            )
            row_top = jnp.max(scores, axis=0, keepdims=True)
            scaled_exp = jnp.exp(scores - row_top)
            weights = scaled_exp * (1.0 / jnp.sum(scaled_exp, axis=0, keepdims=True))
            weight_grads = folded(
                lax.dot_general(
                    value_mat, grad_head, (((1,), (1,)), ((), ())), preferred_element_type=jnp.float32
                )
            )
            row_dot = jnp.sum(weights * weight_grads, axis=0, keepdims=True)
            score_grads = unfolded(
                (weights * (weight_grads - row_dot) * inv_root).astype(jnp.bfloat16)
            )
            weights_low = unfolded(weights.astype(jnp.bfloat16))
            dq_ref[:, cols] = lax.dot_general(
                score_grads, key_mat, (((0,), (0,)), ((), ())), preferred_element_type=jnp.float32
            ).astype(dq_ref.dtype)
            key_sum = key_sum + jnp.dot(score_grads, query_head, preferred_element_type=jnp.float32)
            value_sum = value_sum + jnp.dot(weights_low, grad_head, preferred_element_type=jnp.float32)
        key_cols = slice(local_group * HEAD_SIZE, (local_group + 1) * HEAD_SIZE)
        value_cols = slice((groups + local_group) * HEAD_SIZE, (groups + local_group + 1) * HEAD_SIZE)
        local_ref[:, key_cols] = key_sum[:token_rows]
        local_ref[:, value_cols] = value_sum[:token_rows]
        for back, send_ref in enumerate(send_refs):
            rows = slice((back + 1) * token_rows, (back + 2) * token_rows)
            send_ref[:, key_cols] = key_sum[rows].astype(send_ref.dtype)
            send_ref[:, value_cols] = value_sum[rows].astype(send_ref.dtype)


def attend_pallas(q_chunks, q_pick, weighted, kv_all, bias, part, groups, fold):
    token_rows = weighted.shape[0]
    capacity = q_chunks[0].shape[0]
    key_rows = kv_all.shape[0]
    reach = key_rows // token_rows - 1
    part_width = groups * (QUERY_HEADS // KEY_VALUE_HEADS) * HEAD_SIZE
    kv_width = 2 * groups * HEAD_SIZE
    heads = groups * (QUERY_HEADS // KEY_VALUE_HEADS)
    flops = 10 * token_rows * key_rows * HEAD_SIZE * heads
    bytes_accessed = 6 * token_rows * part_width + 2 * key_rows * kv_all.shape[1] + 4 * token_rows * key_rows
    whole = lambda i: (0, 0)
    return pl.pallas_call(
        functools.partial(
            attend_kernel, first_group=part * groups, chunks=len(q_chunks), reach=reach, fold=fold
        ),
        grid=(1,),
        in_specs=[pl.BlockSpec((capacity, part_width), lambda i: (0, part)) for _ in q_chunks]
        + [
            pl.BlockSpec(q_pick.shape, whole),
            pl.BlockSpec((token_rows, part_width), lambda i: (0, part)),
            pl.BlockSpec(kv_all.shape, whole),
            pl.BlockSpec(bias.shape, whole),
        ],
        out_specs=[
            pl.BlockSpec((token_rows, part_width), whole)
        ]
        + [pl.BlockSpec((token_rows, kv_width), whole) for _ in range(reach + 1)],
        out_shape=[
            jax.ShapeDtypeStruct((token_rows, part_width), jnp.bfloat16),
            jax.ShapeDtypeStruct((token_rows, kv_width), jnp.float32),
        ]
        + [jax.ShapeDtypeStruct((token_rows, kv_width), jnp.bfloat16) for _ in range(reach)],
        cost_estimate=pl.CostEstimate(
            flops=flops, transcendentals=token_rows * key_rows * heads, bytes_accessed=bytes_accessed
        ),
        scratch_shapes=[pltpu.VMEM((token_rows, part_width), jnp.bfloat16)],
    )(*q_chunks, q_pick, weighted, kv_all, bias)


def step(rollout_rows, routing, segment_labels, upstream, passes, group_ids):
    dp_size = lax.axis_size("dp")
    sp_size = lax.axis_size("sp")
    dp_index = lax.axis_index("dp")
    sp_index = lax.axis_index("sp")
    token_rows = rollout_rows.shape[0]
    kv_width = 2 * KEY_VALUE_HEADS * HEAD_SIZE
    longest_segment = sp_size * token_rows // 2
    reach = min(sp_size - 1, (longest_segment + token_rows - 2) // token_rows)
    seq_len = (reach + 1) * token_rows
    fold = reach > 0 and longest_segment == reach * token_rows

    packed_q, packed_kv = exchange_rows(rollout_rows, routing, dp_size, sp_size, dp_index, sp_index)
    own_seg = segment_labels[0]
    label_cols = jnp.broadcast_to(own_seg.astype(jnp.bfloat16)[:, None], (token_rows, HEAD_SIZE))
    kv_local = jnp.concatenate([packed_kv, label_cols], axis=1)
    kv_rel = [kv_local] + [
        lax.ppermute(kv_local, "sp", [(k, k + shift) for k in range(sp_size - shift)])
        for shift in range(1, reach + 1)
    ]
    kv_all = jnp.concatenate(kv_rel, axis=0)
    key_seg = kv_all[:, kv_width].astype(jnp.int32)

    advantage = group_advantage(passes, group_ids)
    bin_adv = lax.dynamic_slice_in_dim(advantage, dp_index * SEGS, SEGS)
    tok_adv = jnp.sum(
        jnp.where(
            own_seg[:, None] == jnp.arange(SEGS, dtype=jnp.int32)[None, :], bin_adv[None, :], 0.0
        ),
        axis=1,
    )
    weighted = (upstream[0].astype(jnp.float32) * tok_adv[:, None]).astype(jnp.bfloat16)

    query_pos = sp_index * token_rows + jnp.arange(token_rows, dtype=jnp.int32)
    rel_block = jnp.arange(seq_len, dtype=jnp.int32) // token_rows
    key_pos = (sp_index - rel_block) * token_rows + jnp.arange(seq_len, dtype=jnp.int32) % token_rows
    allowed = (
        (own_seg[:, None] == key_seg[None, :])
        & (key_pos[None, :] <= query_pos[:, None])
        & (key_pos[None, :] >= 0)
    )
    bias = jnp.where(allowed.T, 0.0, -1e30).astype(jnp.float32)
    groups = KEY_VALUE_HEADS // 2
    query_parts, key_parts, value_parts = [], [], []
    for part in range(2):
        query_grad, total, *outgoing = attend_pallas(
            *packed_q, weighted, kv_all, bias, part, groups, fold
        )
        for shift in range(reach, 0, -1):
            arrived = lax.ppermute(
                outgoing[shift - 1], "sp", [(k, k - shift) for k in range(shift, sp_size)]
            )
            total = total + arrived.astype(jnp.float32)
        query_parts.append(query_grad)
        key_parts.append(total[:, : groups * HEAD_SIZE])
        value_parts.append(total[:, groups * HEAD_SIZE :])
    query_gradient = jnp.concatenate(query_parts, axis=1).reshape(
        1, token_rows, QUERY_HEADS * HEAD_SIZE
    )
    kv_grads = jnp.concatenate(key_parts + value_parts, axis=1).astype(jnp.bfloat16)
    return (query_gradient, kv_grads.reshape(1, token_rows, kv_width))


def solution(mesh):
    return jax.shard_map(
        step,
        mesh=mesh,
        in_specs=(
            P(("grp", "dp", "sp"), None),
            P("grp"),
            P(("grp", "dp"), "sp"),
            P(("grp", "dp"), "sp", None),
            P("grp"),
            P("grp"),
        ),
        out_specs=(P(("grp", "dp"), "sp", None), P(("grp", "dp"), "sp", None)),
        check_vma=False,
    )
```
